32 devices in a mesh: grp: 2 (over y), row: 4 (over z), col: 2 (over x), vec: 2 (over core).
Axes of the slice: x: 2, y: 2, z: 4, core: 2. Of those that a mesh axis runs over, the one named last changes fastest.
Arguments:
- start: float32 [64, 2048], P('vec', ('grp', 'row')), parts along dimension 1, may hold values from -6 to 6
- tiles: bfloat16 [16, 32, 128, 128], P(('grp', 'row'), 'col'), parts along dimension 0, may hold values from -6 to 6
- pattern: int32 [16, 32], P(('grp', 'row')), parts along dimension 0, may hold values from 0 to 7
- counts: int32 [16], P(('grp', 'row')), parts along dimension 0, may hold values from 1 to 32
Outputs:
- basis: float32 [64, 2048], P('vec', ('grp', 'row')), parts along dimension 1
The draws below stay inside these ranges and needn't reach their ends.
There are 2 independent parts, one for each index of `grp`. The reference program is written for one: setup_inputs(seed, part) draws one part's arguments, and reference() takes and returns one part's arrays. A program takes and returns all parts, laid end to end along the dimension named above; each array names one. Nothing has to cross between parts.
Inputs may be any that keep to these rules, and one draw needn't show every extreme that they name: pattern may name a block column more than once in a block row; such tiles add.
All inputs are finite; a program needn't handle non-finite values.
Results may differ from the reference program's by a relative error of at most 0.03.
Values may be sent and summed in bfloat16 or wider, within the bound.
No kernel may reach another device: no remote copies, remote signals or barrier semaphores. Data moves between devices by JAX's collectives and lax.ppermute only.
A program may use at most 64 MiB of HBM per device.

```python
import jax
import jax.numpy as jnp
from jax import lax

BLK = 128
COLS = 64
DEGREE = 8
ITERS = 2
KB = 32
NBLK = 8
NROWS = 1024


def place_ends(array, stream_key, least, largest):
    longest = array.shape.index(max(array.shape))
    spots = []
    for shift in (0, 1):
        where = [jax.random.randint(jax.random.fold_in(stream_key, axis), (), 0, length) for axis, length in enumerate(array.shape)]
        where[longest] = (where[longest] + shift) % array.shape[longest]
        spots.append(tuple(where))
    return array.at[spots[0]].set(least).at[spots[1]].set(largest)


def levels(stream_key, shape, cuts, low, largest):
    level = 1.0
    for axis_at, shards_of in cuts:
        heights = jax.random.uniform(jax.random.fold_in(jax.random.fold_in(stream_key, 6), axis_at), (shards_of,), jnp.float32, low / len(cuts), largest / len(cuts))
        level = level * jnp.repeat(jnp.exp(heights), shape[axis_at] // shards_of).reshape((-1,) + (1,) * (len(shape) - 1 - axis_at))
    return level


def noise(rng, extent, width, limit, cuts=(), kind=jnp.bfloat16):
    array = jax.random.normal(rng, extent, jnp.float32) * width
    if len(cuts) > 0:
        array = levels(rng, extent, cuts, -0.22, 0.18) * array
    return jnp.clip(array, min=-limit, max=limit).astype(kind)


def setup_inputs(seed: int = 0, part: int = 0) -> dict:
    key_of = jax.random.split(jax.random.key(seed), 5)
    own_keys = jax.random.split(jax.random.fold_in(key_of[4], part), 5)
    return {
        "start": noise(own_keys[0], (COLS, NROWS), 1.0, 6.0, ((0, 2), (1, 4)), jnp.float32),
        "tiles": noise(own_keys[1], (NBLK, KB, BLK, BLK), 1.0, 6.0, ((0, 4), (1, 2))),
        "pattern": place_ends(jax.random.randint(own_keys[2], (NBLK, KB), 0, NBLK), jax.random.fold_in(own_keys[2], 1), 0, NBLK - 1).astype(jnp.int32),
        "counts": place_ends(jax.random.randint(own_keys[3], (NBLK,), 1, KB + 1), jax.random.fold_in(own_keys[3], 1), 1, KB).astype(jnp.int32),
    }


HALF_WIDTH = 2.0
EPSILON = 1e-06

def reference(start, tiles, pattern, counts):
    slot_ids = jnp.arange(KB, dtype=jnp.int32)
    live = (slot_ids[None, :] < counts[:, None]).astype(jnp.bfloat16)
    masked = tiles * live[:, :, None, None]
    wide = masked.astype(jnp.float32)
    square_sums = lax.optimization_barrier(jnp.sum(wide * wide, axis=(1, 3)))
    entries = (counts * BLK).astype(jnp.float32)[:, None]
    scaling = lax.rsqrt(square_sums / entries + EPSILON) / jnp.sqrt(entries) / HALF_WIDTH
    scaling = scaling.reshape(NROWS)

    def apply(current):
        rounded = lax.optimization_barrier(current.astype(jnp.bfloat16)).astype(jnp.float32)
        blocks = rounded.reshape(COLS, NBLK, BLK)

        def one_row(inputs):
            tile_row, cols_row = inputs
            picked = jnp.take(blocks, cols_row, axis=1)
            return jnp.einsum('ckn,kmn->cm', picked, tile_row.astype(jnp.float32))
        product = lax.map(one_row, (masked, pattern))
        product = jnp.transpose(product, (1, 0, 2)).reshape(COLS, NROWS)
        return product * scaling[None, :]
    current = start
    for outer in range(ITERS):
        previous = current
        present = apply(current)
        for step in range(DEGREE - 1):
            previous, present = (present, 2.0 * apply(present) - previous)
        gram = jnp.dot(present, present.T, precision=lax.Precision.HIGHEST) / NROWS
        lower = jnp.linalg.cholesky(gram)
        current = jax.scipy.linalg.solve_triangular(lower, present, lower=True)
    return current
```

```python
import jax
import jax.numpy as jnp
from jax import lax
from jax.sharding import PartitionSpec as P

DEGREE = 8
ITERS = 2


HALF_WIDTH = 2.0
EPSILON = 1e-06
DENSE_BUDGET = 16 * 1024 * 1024


def row_scaling(square_sums, live_counts, block):
    entries = (live_counts * block).astype(jnp.float32)[:, None]
    scaled = lax.rsqrt(square_sums / entries + EPSILON) / jnp.sqrt(entries)
    return (scaled / HALF_WIDTH).reshape(1, -1)


def chebyshev(first, apply):
    previous = first
    present = apply(first)
    for step in range(DEGREE - 1):
        previous, present = (present, 2.0 * apply(present) - previous)
    return present


def orthonormal(mine, total_rows):
    both = lax.all_gather(mine.astype(jnp.bfloat16), "vec", axis=0, tiled=True).astype(mine.dtype)
    part_gram = jnp.dot(both, both.T, precision=lax.Precision.HIGHEST)
    gram = lax.psum(part_gram, "row") / total_rows
    lower = jnp.linalg.cholesky(gram)
    solved = jax.scipy.linalg.solve_triangular(lower, both, lower=True)
    width = mine.shape[0]
    return lax.dynamic_slice_in_dim(solved, lax.axis_index("vec") * width, width, 0)


def distributed(start, tiles, pattern, counts):
    nb_dev = tiles.shape[0]
    block = tiles.shape[2]
    total_rows = nb_dev * block * lax.axis_size("row")
    vec_cols = start.shape[0]
    col_index = lax.axis_index("col")
    kb_dev = tiles.shape[1]
    slot_ids = col_index * kb_dev + jnp.arange(kb_dev, dtype=jnp.int32)
    live = (slot_ids[None, :] < counts[:, None]).astype(jnp.bfloat16)
    masked = tiles * live[:, :, None, None]
    local_pattern = lax.dynamic_slice_in_dim(pattern, col_index * kb_dev, kb_dev, 1)
    partial_squares = jnp.einsum(
        "bkmn,bkmn->bm", masked, masked, preferred_element_type=jnp.float32
    )
    square_sums = lax.psum(partial_squares, "col")
    scaling = row_scaling(square_sums, counts, block)

    def apply_slots(current):
        whole = lax.all_gather(current.astype(jnp.bfloat16), "row", axis=1, tiled=True)
        blocks = whole.reshape(vec_cols, -1, block)
        picked = jnp.take(blocks, local_pattern, axis=1)
        product = jnp.einsum("cbkn,bkmn->cbm", picked, masked, preferred_element_type=jnp.float32)
        total = lax.psum(product.astype(jnp.bfloat16), "col").astype(jnp.float32)
        return total.reshape(vec_cols, -1) * scaling

    current = start
    for outer in range(ITERS):
        filtered = chebyshev(current, apply_slots)
        current = orthonormal(filtered, total_rows)
    return current


def split_bf16(values):
    high = values.astype(jnp.bfloat16)
    low = (values - high.astype(jnp.float32)).astype(jnp.bfloat16)
    return high, low


def replicated(start, tiles, pattern, counts):
    nb_dev, kb_dev, block = tiles.shape[0], tiles.shape[1], tiles.shape[2]
    n_row, n_col = lax.axis_size("row"), lax.axis_size("col")
    nblk = nb_dev * n_row
    total_rows = nblk * block
    share = block // n_col
    vec_cols = start.shape[0]
    cols = 2 * vec_cols
    row_index = lax.axis_index("row")
    col_index = lax.axis_index("col")
    vec_index = lax.axis_index("vec")

    own_tiles = lax.dynamic_index_in_dim(tiles, vec_index, 0, keepdims=False)
    own_pattern = lax.dynamic_slice_in_dim(
        lax.dynamic_index_in_dim(pattern, vec_index, 0, keepdims=False), col_index * kb_dev, kb_dev, 0
    )
    own_count = lax.dynamic_index_in_dim(counts, vec_index, 0, keepdims=False)
    slot_ids = col_index * kb_dev + jnp.arange(kb_dev, dtype=jnp.int32)
    live = slot_ids < own_count
    position = (own_pattern % nb_dev) * n_row + own_pattern // nb_dev
    onehot = (position[:, None] == jnp.arange(nblk, dtype=jnp.int32)) & live[:, None]
    dense = jnp.einsum(
        "kj,kmn->mjn", onehot.astype(jnp.bfloat16), own_tiles, preferred_element_type=jnp.float32
    ).reshape(block, total_rows)
    masked = own_tiles * live.astype(jnp.bfloat16)[:, None, None]
    squares = jnp.einsum("kmn,kmn->m", masked, masked, preferred_element_type=jnp.float32)
    squares = jnp.broadcast_to(squares[:, None], (block, 128))
    partial = jnp.concatenate([dense, squares], axis=1)
    summed = lax.psum_scatter(partial, "col", scatter_dimension=0, tiled=True)

    entries = (own_count * block).astype(jnp.float32)
    scale = lax.rsqrt(summed[:, total_rows] / entries + EPSILON) / jnp.sqrt(entries) / HALF_WIDTH
    scale_hi, scale_lo = split_bf16(scale)

    piece = start.reshape(vec_cols, nb_dev, block)
    piece = lax.dynamic_slice_in_dim(piece, col_index * share, share, 2).reshape(vec_cols, nb_dev * share)
    start_hi, start_lo = split_bf16(piece)
    extra = jnp.concatenate([start_hi, start_lo], axis=0)
    extra = jnp.concatenate(
        [extra, scale_hi[:, None], scale_lo[:, None], jnp.zeros((share, 254 - nb_dev * share), jnp.bfloat16)],
        axis=1,
    )
    packed = jnp.concatenate([summed[:, :total_rows].astype(jnp.bfloat16), extra], axis=1)
    across = lax.all_gather(packed, ("row", "col"), axis=0, tiled=False)
    whole = lax.all_gather(across, "vec", axis=0, tiled=False)
    whole = whole.reshape(total_rows, total_rows + 256)
    weights = whole[:, :total_rows]
    scaling = (
        whole[:, total_rows + nb_dev * share].astype(jnp.float32)
        + whole[:, total_rows + nb_dev * share + 1].astype(jnp.float32)
    )[None, :]
    coded = whole[:, total_rows : total_rows + nb_dev * share].astype(jnp.float32)
    coded = coded.reshape(2, n_row, n_col, 2, vec_cols, nb_dev, share)
    coded = coded[:, :, :, 0] + coded[:, :, :, 1]
    current = coded.transpose(0, 3, 4, 1, 2, 5).reshape(cols, total_rows)

    def apply_dense(values):
        product = jnp.einsum(
            "cj,ij->ci", values.astype(jnp.bfloat16), weights, preferred_element_type=jnp.float32
        )
        return product * scaling

    for outer in range(ITERS):
        filtered = chebyshev(current, apply_dense)
        gram = jnp.dot(filtered, filtered.T, precision=lax.Precision.HIGHEST) / total_rows
        lower = jnp.linalg.cholesky(gram)
        if outer < ITERS - 1:
            current = jax.scipy.linalg.solve_triangular(lower, filtered, lower=True)
        else:
            mine = filtered.reshape(cols, nb_dev, n_row, block)
            mine = lax.dynamic_index_in_dim(mine, row_index, 2, keepdims=False).reshape(cols, nb_dev * block)
            solved = jax.scipy.linalg.solve_triangular(lower, mine, lower=True)
            current = lax.dynamic_slice_in_dim(solved, vec_index * vec_cols, vec_cols, 0)
    return current


def per_device(start, tiles, pattern, counts):
    total_rows = tiles.shape[0] * tiles.shape[2] * lax.axis_size("row")
    n_col, n_vec = lax.axis_size("col"), lax.axis_size("vec")
    block = tiles.shape[2]
    fits = (
        total_rows * total_rows * 2 <= DENSE_BUDGET
        and n_vec == 2
        and tiles.shape[0] == n_vec
        and block % n_col == 0
        and block // n_col == 2 * start.shape[0]
        and tiles.shape[0] * (block // n_col) <= 254
    )
    if fits:
        return replicated(start, tiles, pattern, counts)
    return distributed(start, tiles, pattern, counts)


def solution(mesh):
    in_specs = (
        P("vec", ("grp", "row")),
        P(("grp", "row"), "col", None, None),
        P(("grp", "row"), None),
        P(("grp", "row")),
    )
    out_specs = P("vec", ("grp", "row"))
    return jax.shard_map(
        per_device, mesh=mesh, in_specs=in_specs, out_specs=out_specs, check_vma=False
    )
```

```python
import jax
import jax.numpy as jnp
from jax import lax
from jax.sharding import PartitionSpec as P

DEGREE = 8
ITERS = 2


HALF_WIDTH = 2.0
EPSILON = 1e-06
DENSE_BUDGET = 16 * 1024 * 1024


def row_scaling(square_sums, live_counts, block):
    entries = (live_counts * block).astype(jnp.float32)[:, None]
    scaled = lax.rsqrt(square_sums / entries + EPSILON) / jnp.sqrt(entries)
    return (scaled / HALF_WIDTH).reshape(1, -1)


def chebyshev(first, apply):
    previous = first
    present = apply(first)
    for step in range(DEGREE - 1):
        previous, present = (present, 2.0 * apply(present) - previous)
    return present


def orthonormal(mine, total_rows):
    both = lax.all_gather(mine.astype(jnp.bfloat16), "vec", axis=0, tiled=True).astype(mine.dtype)
    part_gram = jnp.dot(both, both.T, precision=lax.Precision.HIGHEST)
    gram = lax.psum(part_gram, "row") / total_rows
    lower = jnp.linalg.cholesky(gram)
    solved = jax.scipy.linalg.solve_triangular(lower, both, lower=True)
    width = mine.shape[0]
    return lax.dynamic_slice_in_dim(solved, lax.axis_index("vec") * width, width, 0)


def distributed(start, tiles, pattern, counts):
    nb_dev = tiles.shape[0]
    block = tiles.shape[2]
    total_rows = nb_dev * block * lax.axis_size("row")
    vec_cols = start.shape[0]
    col_index = lax.axis_index("col")
    kb_dev = tiles.shape[1]
    slot_ids = col_index * kb_dev + jnp.arange(kb_dev, dtype=jnp.int32)
    live = (slot_ids[None, :] < counts[:, None]).astype(jnp.bfloat16)
    masked = tiles * live[:, :, None, None]
    local_pattern = lax.dynamic_slice_in_dim(pattern, col_index * kb_dev, kb_dev, 1)
    partial_squares = jnp.einsum(
        "bkmn,bkmn->bm", masked, masked, preferred_element_type=jnp.float32
    )
    square_sums = lax.psum(partial_squares, "col")
    scaling = row_scaling(square_sums, counts, block)

    def apply_slots(current):
        whole = lax.all_gather(current.astype(jnp.bfloat16), "row", axis=1, tiled=True)
        blocks = whole.reshape(vec_cols, -1, block)
        picked = jnp.take(blocks, local_pattern, axis=1)
        product = jnp.einsum("cbkn,bkmn->cbm", picked, masked, preferred_element_type=jnp.float32)
        total = lax.psum(product.astype(jnp.bfloat16), "col").astype(jnp.float32)
        return total.reshape(vec_cols, -1) * scaling

    current = start
    for outer in range(ITERS):
        filtered = chebyshev(current, apply_slots)
        current = orthonormal(filtered, total_rows)
    return current


def split_bf16(values):
    high = values.astype(jnp.bfloat16)
    low = (values - high.astype(jnp.float32)).astype(jnp.bfloat16)
    return high, low


def replicated(start, tiles, pattern, counts):
    nb_dev, kb_dev, block = tiles.shape[0], tiles.shape[1], tiles.shape[2]
    n_row, n_col = lax.axis_size("row"), lax.axis_size("col")
    nblk = nb_dev * n_row
    total_rows = nblk * block
    share = block // n_col
    vec_cols = start.shape[0]
    cols = 2 * vec_cols
    row_index = lax.axis_index("row")
    col_index = lax.axis_index("col")
    vec_index = lax.axis_index("vec")

    own_tiles = lax.dynamic_index_in_dim(tiles, vec_index, 0, keepdims=False)
    own_pattern = lax.dynamic_slice_in_dim(
        lax.dynamic_index_in_dim(pattern, vec_index, 0, keepdims=False), col_index * kb_dev, kb_dev, 0
    )
    own_count = lax.dynamic_index_in_dim(counts, vec_index, 0, keepdims=False)
    slot_ids = col_index * kb_dev + jnp.arange(kb_dev, dtype=jnp.int32)
    live = slot_ids < own_count
    position = (own_pattern % nb_dev) * n_row + own_pattern // nb_dev
    onehot = (position[:, None] == jnp.arange(nblk, dtype=jnp.int32)) & live[:, None]
    dense = jnp.einsum(
        "kj,kmn->mjn", onehot.astype(jnp.bfloat16), own_tiles, preferred_element_type=jnp.float32
    ).reshape(block, total_rows)
    masked = own_tiles * live.astype(jnp.bfloat16)[:, None, None]
    squares = jnp.einsum("kmn,kmn->m", masked, masked, preferred_element_type=jnp.float32)
    squares = jnp.broadcast_to(squares[:, None], (block, 128))
    partial = jnp.concatenate([dense, squares], axis=1)
    chunks = partial.reshape(n_col, share, total_rows + 128)
    summed = lax.dynamic_index_in_dim(chunks, col_index, 0, keepdims=False)
    for shift in range(1, n_col):
        sent = lax.dynamic_index_in_dim(chunks, (col_index + shift) % n_col, 0, keepdims=False)
        summed = summed + lax.ppermute(sent, "col", [(i, (i + shift) % n_col) for i in range(n_col)])

    entries = (own_count * block).astype(jnp.float32)
    scale = lax.rsqrt(summed[:, total_rows] / entries + EPSILON) / jnp.sqrt(entries) / HALF_WIDTH
    scale_hi, scale_lo = split_bf16(scale)

    piece = start.reshape(vec_cols, nb_dev, block)
    piece = lax.dynamic_slice_in_dim(piece, col_index * share, share, 2).reshape(vec_cols, nb_dev * share)
    start_hi, start_lo = split_bf16(piece)
    extra = jnp.concatenate([start_hi, start_lo], axis=0)
    extra = jnp.concatenate(
        [extra, scale_hi[:, None], scale_lo[:, None], jnp.zeros((share, 126), jnp.bfloat16)], axis=1
    )
    rows_bf16 = summed[:, :total_rows].astype(jnp.bfloat16)

    n_rc = n_row * n_col
    rc_index = row_index * n_col + col_index
    received = [(rows_bf16, extra)]
    for shift in range(1, n_rc):
        perm = [(i, (i + shift) % n_rc) for i in range(n_rc)]
        received.append(lax.ppermute((rows_bf16, extra), ("row", "col"), perm))
    order = (rc_index - jnp.arange(n_rc, dtype=jnp.int32)) % n_rc
    half_rows = jnp.take(jnp.stack([r[0] for r in received]), order, axis=0)
    half_extra = jnp.take(jnp.stack([r[1] for r in received]), order, axis=0)
    other_rows, other_extra = lax.ppermute((half_rows, half_extra), "vec", [(0, 1), (1, 0)])
    pair = (jnp.arange(2, dtype=jnp.int32) - vec_index) % 2
    weights = jnp.take(jnp.stack([half_rows, other_rows]), pair, axis=0).reshape(total_rows, total_rows)
    extras = jnp.take(jnp.stack([half_extra, other_extra]), pair, axis=0).reshape(total_rows, 256)
    scaling = (
        extras[:, nb_dev * share].astype(jnp.float32) + extras[:, nb_dev * share + 1].astype(jnp.float32)
    )[None, :]
    coded = extras[:, : nb_dev * share].astype(jnp.float32)
    coded = coded.reshape(2, n_row, n_col, 2, vec_cols, nb_dev, share)
    coded = coded[:, :, :, 0] + coded[:, :, :, 1]
    current = coded.transpose(0, 3, 4, 1, 2, 5).reshape(cols, total_rows)

    def apply_dense(values):
        product = jnp.einsum(
            "cj,ij->ci", values.astype(jnp.bfloat16), weights, preferred_element_type=jnp.float32
        )
        return product * scaling

    for outer in range(ITERS):
        filtered = chebyshev(current, apply_dense)
        gram = jnp.dot(filtered, filtered.T, precision=lax.Precision.HIGHEST) / total_rows
        lower = jnp.linalg.cholesky(gram)
        if outer < ITERS - 1:
            current = jax.scipy.linalg.solve_triangular(lower, filtered, lower=True)
        else:
            mine = filtered.reshape(cols, nb_dev, n_row, block)
            mine = lax.dynamic_index_in_dim(mine, row_index, 2, keepdims=False).reshape(cols, nb_dev * block)
            solved = jax.scipy.linalg.solve_triangular(lower, mine, lower=True)
            current = lax.dynamic_slice_in_dim(solved, vec_index * vec_cols, vec_cols, 0)
    return current


def per_device(start, tiles, pattern, counts):
    total_rows = tiles.shape[0] * tiles.shape[2] * lax.axis_size("row")
    n_col, n_vec = lax.axis_size("col"), lax.axis_size("vec")
    block = tiles.shape[2]
    fits = (
        total_rows * total_rows * 2 <= DENSE_BUDGET
        and n_vec == 2
        and tiles.shape[0] == n_vec
        and block % n_col == 0
        and block // n_col == 2 * start.shape[0]
        and tiles.shape[0] * (block // n_col) <= 128
    )
    if fits:
        return replicated(start, tiles, pattern, counts)
    return distributed(start, tiles, pattern, counts)


def solution(mesh):
    in_specs = (
        P("vec", ("grp", "row")),
        P(("grp", "row"), "col", None, None),
        P(("grp", "row"), None),
        P(("grp", "row")),
    )
    out_specs = P("vec", ("grp", "row"))
    return jax.shard_map(
        per_device, mesh=mesh, in_specs=in_specs, out_specs=out_specs, check_vma=False
    )
```

```python
import jax
import jax.numpy as jnp
from jax import lax
from jax.sharding import PartitionSpec as P

DEGREE = 8
ITERS = 2


HALF_WIDTH = 2.0
EPSILON = 1e-06
DENSE_BUDGET = 16 * 1024 * 1024


def row_scaling(square_sums, live_counts, block):
    entries = (live_counts * block).astype(jnp.float32)[:, None]
    scaled = lax.rsqrt(square_sums / entries + EPSILON) / jnp.sqrt(entries)
    return (scaled / HALF_WIDTH).reshape(1, -1)


def chebyshev(first, apply):
    previous = first
    present = apply(first)
    for step in range(DEGREE - 1):
        previous, present = (present, 2.0 * apply(present) - previous)
    return present


def orthonormal(mine, total_rows):
    both = lax.all_gather(mine.astype(jnp.bfloat16), "vec", axis=0, tiled=True).astype(mine.dtype)
    part_gram = jnp.dot(both, both.T, precision=lax.Precision.HIGHEST)
    gram = lax.psum(part_gram, "row") / total_rows
    lower = jnp.linalg.cholesky(gram)
    solved = jax.scipy.linalg.solve_triangular(lower, both, lower=True)
    width = mine.shape[0]
    return lax.dynamic_slice_in_dim(solved, lax.axis_index("vec") * width, width, 0)


def distributed(start, tiles, pattern, counts):
    nb_dev = tiles.shape[0]
    block = tiles.shape[2]
    total_rows = nb_dev * block * lax.axis_size("row")
    vec_cols = start.shape[0]
    col_index = lax.axis_index("col")
    kb_dev = tiles.shape[1]
    slot_ids = col_index * kb_dev + jnp.arange(kb_dev, dtype=jnp.int32)
    live = (slot_ids[None, :] < counts[:, None]).astype(jnp.bfloat16)
    masked = tiles * live[:, :, None, None]
    local_pattern = lax.dynamic_slice_in_dim(pattern, col_index * kb_dev, kb_dev, 1)
    partial_squares = jnp.einsum(
        "bkmn,bkmn->bm", masked, masked, preferred_element_type=jnp.float32
    )
    square_sums = lax.psum(partial_squares, "col")
    scaling = row_scaling(square_sums, counts, block)

    def apply_slots(current):
        whole = lax.all_gather(current.astype(jnp.bfloat16), "row", axis=1, tiled=True)
        blocks = whole.reshape(vec_cols, -1, block)
        picked = jnp.take(blocks, local_pattern, axis=1)
        product = jnp.einsum("cbkn,bkmn->cbm", picked, masked, preferred_element_type=jnp.float32)
        total = lax.psum(product.astype(jnp.bfloat16), "col").astype(jnp.float32)
        return total.reshape(vec_cols, -1) * scaling

    current = start
    for outer in range(ITERS):
        filtered = chebyshev(current, apply_slots)
        current = orthonormal(filtered, total_rows)
    return current


def split_bf16(values):
    high = values.astype(jnp.bfloat16)
    low = (values - high.astype(jnp.float32)).astype(jnp.bfloat16)
    return high, low


def replicated(start, tiles, pattern, counts):
    nb_dev, kb_dev, block = tiles.shape[0], tiles.shape[1], tiles.shape[2]
    n_row, n_col = lax.axis_size("row"), lax.axis_size("col")
    nblk = nb_dev * n_row
    total_rows = nblk * block
    share = block // n_col
    vec_cols = start.shape[0]
    cols = 2 * vec_cols
    row_index = lax.axis_index("row")
    col_index = lax.axis_index("col")
    vec_index = lax.axis_index("vec")

    own_tiles = lax.dynamic_index_in_dim(tiles, vec_index, 0, keepdims=False)
    own_pattern = lax.dynamic_slice_in_dim(
        lax.dynamic_index_in_dim(pattern, vec_index, 0, keepdims=False), col_index * kb_dev, kb_dev, 0
    )
    own_count = lax.dynamic_index_in_dim(counts, vec_index, 0, keepdims=False)
    slot_ids = col_index * kb_dev + jnp.arange(kb_dev, dtype=jnp.int32)
    live = slot_ids < own_count
    position = (own_pattern % nb_dev) * n_row + own_pattern // nb_dev
    onehot = (position[:, None] == jnp.arange(nblk, dtype=jnp.int32)) & live[:, None]
    dense = jnp.einsum(
        "kj,kmn->mjn", onehot.astype(jnp.bfloat16), own_tiles, preferred_element_type=jnp.float32
    ).reshape(block, total_rows)
    masked = own_tiles * live.astype(jnp.bfloat16)[:, None, None]
    squares = jnp.einsum("kmn,kmn->m", masked, masked, preferred_element_type=jnp.float32)
    squares = jnp.broadcast_to(squares[:, None], (block, 128))
    partial = jnp.concatenate([dense, squares], axis=1)
    chunks = partial.reshape(n_col, share, total_rows + 128)
    summed = jnp.sum(lax.all_to_all(chunks, "col", 0, 0, tiled=True), axis=0)

    entries = (own_count * block).astype(jnp.float32)
    scale = lax.rsqrt(summed[:, total_rows] / entries + EPSILON) / jnp.sqrt(entries) / HALF_WIDTH
    scale_hi, scale_lo = split_bf16(scale)

    piece = start.reshape(vec_cols, nb_dev, block)
    piece = lax.dynamic_slice_in_dim(piece, col_index * share, share, 2).reshape(vec_cols, nb_dev * share)
    start_hi, start_lo = split_bf16(piece)
    extra = jnp.concatenate([start_hi, start_lo], axis=0)
    extra = jnp.concatenate(
        [extra, scale_hi[:, None], scale_lo[:, None], jnp.zeros((share, 126), jnp.bfloat16)], axis=1
    )
    rows_bf16 = summed[:, :total_rows].astype(jnp.bfloat16)

    packed = jnp.concatenate([rows_bf16, extra], axis=1)
    copies = jnp.broadcast_to(packed[None], (n_row * n_col,) + packed.shape)
    half = lax.all_to_all(copies, ("row", "col"), 0, 0, tiled=True)
    copies = jnp.broadcast_to(half[None], (2,) + half.shape)
    whole = lax.all_to_all(copies, "vec", 0, 0, tiled=True).reshape(total_rows, total_rows + 256)
    weights = whole[:, :total_rows]
    extras = whole[:, total_rows:]
    scaling = (
        extras[:, nb_dev * share].astype(jnp.float32) + extras[:, nb_dev * share + 1].astype(jnp.float32)
    )[None, :]
    coded = extras[:, : nb_dev * share].astype(jnp.float32)
    coded = coded.reshape(2, n_row, n_col, 2, vec_cols, nb_dev, share)
    coded = coded[:, :, :, 0] + coded[:, :, :, 1]
    current = coded.transpose(0, 3, 4, 1, 2, 5).reshape(cols, total_rows)

    def apply_dense(values):
        product = jnp.einsum(
            "cj,ij->ci", values.astype(jnp.bfloat16), weights, preferred_element_type=jnp.float32
        )
        return product * scaling

    for outer in range(ITERS):
        filtered = chebyshev(current, apply_dense)
        gram = jnp.dot(filtered, filtered.T, precision=lax.Precision.HIGHEST) / total_rows
        lower = jnp.linalg.cholesky(gram)
        if outer < ITERS - 1:
            current = jax.scipy.linalg.solve_triangular(lower, filtered, lower=True)
        else:
            mine = filtered.reshape(cols, nb_dev, n_row, block)
            mine = lax.dynamic_index_in_dim(mine, row_index, 2, keepdims=False).reshape(cols, nb_dev * block)
            solved = jax.scipy.linalg.solve_triangular(lower, mine, lower=True)
            current = lax.dynamic_slice_in_dim(solved, vec_index * vec_cols, vec_cols, 0)
    return current


def per_device(start, tiles, pattern, counts):
    total_rows = tiles.shape[0] * tiles.shape[2] * lax.axis_size("row")
    n_col, n_vec = lax.axis_size("col"), lax.axis_size("vec")
    block = tiles.shape[2]
    fits = (
        total_rows * total_rows * 2 <= DENSE_BUDGET
        and n_vec == 2
        and tiles.shape[0] == n_vec
        and block % n_col == 0
        and block // n_col == 2 * start.shape[0]
        and tiles.shape[0] * (block // n_col) <= 128
    )
    if fits:
        return replicated(start, tiles, pattern, counts)
    return distributed(start, tiles, pattern, counts)


def solution(mesh):
    in_specs = (
        P("vec", ("grp", "row")),
        P(("grp", "row"), "col", None, None),
        P(("grp", "row"), None),
        P(("grp", "row")),
    )
    out_specs = P("vec", ("grp", "row"))
    return jax.shard_map(
        per_device, mesh=mesh, in_specs=in_specs, out_specs=out_specs, check_vma=False
    )
```

```python
import jax
import jax.numpy as jnp
from jax import lax
from jax.experimental import pallas as pl
from jax.experimental.pallas import tpu as pltpu
from jax.sharding import PartitionSpec as P

DEGREE = 8
ITERS = 2


HALF_WIDTH = 2.0
EPSILON = 1e-06
DENSE_BUDGET = 16 * 1024 * 1024


def row_scaling(square_sums, live_counts, block):
    entries = (live_counts * block).astype(jnp.float32)[:, None]
    scaled = lax.rsqrt(square_sums / entries + EPSILON) / jnp.sqrt(entries)
    return (scaled / HALF_WIDTH).reshape(1, -1)


def chebyshev(first, apply):
    previous = first
    present = apply(first)
    for step in range(DEGREE - 1):
        previous, present = (present, 2.0 * apply(present) - previous)
    return present


def orthonormal(mine, total_rows):
    both = lax.all_gather(mine.astype(jnp.bfloat16), "vec", axis=0, tiled=True).astype(mine.dtype)
    part_gram = jnp.dot(both, both.T, precision=lax.Precision.HIGHEST)
    gram = lax.psum(part_gram, "row") / total_rows
    lower = jnp.linalg.cholesky(gram)
    solved = jax.scipy.linalg.solve_triangular(lower, both, lower=True)
    width = mine.shape[0]
    return lax.dynamic_slice_in_dim(solved, lax.axis_index("vec") * width, width, 0)


def orthonormal_kernel(y_ref, x_ref):
    y = y_ref[...]
    n, total = y.shape
    hi = lax.Precision.HIGHEST
    a = lax.dot_general(y, y, (((1,), (1,)), ((), ())), precision=hi, preferred_element_type=jnp.float32)
    a = a / total
    rows = lax.broadcasted_iota(jnp.int32, (n, n), 0)
    cols = lax.broadcasted_iota(jnp.int32, (n, n), 1)
    inverse = (rows == cols).astype(jnp.float32)
    for k in range(n):
        pivot = jnp.sqrt(a[k : k + 1, k : k + 1])
        down = jnp.where(rows[:, k : k + 1] >= k, a[:, k : k + 1] / pivot, 0.0)
        across = jnp.where(cols[k : k + 1, :] >= k, a[k : k + 1, :] / pivot, 0.0)
        a = a - down * across
        solved = inverse[k : k + 1, :] / pivot
        below = jnp.where(rows[:, k : k + 1] > k, down, 0.0)
        inverse = jnp.where(rows == k, solved, inverse - below * solved)
    x_ref[...] = lax.dot_general(
        inverse, y, (((1,), (0,)), ((), ())), precision=hi, preferred_element_type=jnp.float32
    )


def orthonormal_local(y):
    return pl.pallas_call(
        orthonormal_kernel,
        out_shape=jax.ShapeDtypeStruct(y.shape, jnp.float32),
        in_specs=[pl.BlockSpec(memory_space=pltpu.VMEM)],
        out_specs=pl.BlockSpec(memory_space=pltpu.VMEM),
    )(y)


def distributed(start, tiles, pattern, counts):
    nb_dev = tiles.shape[0]
    block = tiles.shape[2]
    total_rows = nb_dev * block * lax.axis_size("row")
    vec_cols = start.shape[0]
    col_index = lax.axis_index("col")
    kb_dev = tiles.shape[1]
    slot_ids = col_index * kb_dev + jnp.arange(kb_dev, dtype=jnp.int32)
    live = (slot_ids[None, :] < counts[:, None]).astype(jnp.bfloat16)
    masked = tiles * live[:, :, None, None]
    local_pattern = lax.dynamic_slice_in_dim(pattern, col_index * kb_dev, kb_dev, 1)
    partial_squares = jnp.einsum(
        "bkmn,bkmn->bm", masked, masked, preferred_element_type=jnp.float32
    )
    square_sums = lax.psum(partial_squares, "col")
    scaling = row_scaling(square_sums, counts, block)

    def apply_slots(current):
        whole = lax.all_gather(current.astype(jnp.bfloat16), "row", axis=1, tiled=True)
        blocks = whole.reshape(vec_cols, -1, block)
        picked = jnp.take(blocks, local_pattern, axis=1)
        product = jnp.einsum("cbkn,bkmn->cbm", picked, masked, preferred_element_type=jnp.float32)
        total = lax.psum(product.astype(jnp.bfloat16), "col").astype(jnp.float32)
        return total.reshape(vec_cols, -1) * scaling

    current = start
    for outer in range(ITERS):
        filtered = chebyshev(current, apply_slots)
        current = orthonormal(filtered, total_rows)
    return current


def split_bf16(values):
    high = values.astype(jnp.bfloat16)
    low = (values - high.astype(jnp.float32)).astype(jnp.bfloat16)
    return high, low


def replicated(start, tiles, pattern, counts):
    nb_dev, kb_dev, block = tiles.shape[0], tiles.shape[1], tiles.shape[2]
    n_row, n_col = lax.axis_size("row"), lax.axis_size("col")
    nblk = nb_dev * n_row
    total_rows = nblk * block
    share = block // n_col
    vec_cols = start.shape[0]
    cols = 2 * vec_cols
    row_index = lax.axis_index("row")
    col_index = lax.axis_index("col")
    vec_index = lax.axis_index("vec")

    own_tiles = lax.dynamic_index_in_dim(tiles, vec_index, 0, keepdims=False)
    own_pattern = lax.dynamic_slice_in_dim(
        lax.dynamic_index_in_dim(pattern, vec_index, 0, keepdims=False), col_index * kb_dev, kb_dev, 0
    )
    own_count = lax.dynamic_index_in_dim(counts, vec_index, 0, keepdims=False)
    slot_ids = col_index * kb_dev + jnp.arange(kb_dev, dtype=jnp.int32)
    live = slot_ids < own_count
    position = (own_pattern % nb_dev) * n_row + own_pattern // nb_dev
    onehot = (position[:, None] == jnp.arange(nblk, dtype=jnp.int32)) & live[:, None]
    dense = jnp.einsum(
        "kj,kmn->mjn", onehot.astype(jnp.bfloat16), own_tiles, preferred_element_type=jnp.float32
    ).reshape(block, total_rows)
    masked = own_tiles * live.astype(jnp.bfloat16)[:, None, None]
    squares = jnp.einsum("kmn,kmn->m", masked, masked, preferred_element_type=jnp.float32)
    squares = jnp.broadcast_to(squares[:, None], (block, 128))
    partial = jnp.concatenate([dense, squares], axis=1)
    chunks = partial.reshape(n_col, share, total_rows + 128)
    summed = jnp.sum(lax.all_to_all(chunks, "col", 0, 0, tiled=True), axis=0)

    entries = (own_count * block).astype(jnp.float32)
    scale = lax.rsqrt(summed[:, total_rows] / entries + EPSILON) / jnp.sqrt(entries) / HALF_WIDTH
    scale_hi, scale_lo = split_bf16(scale)

    piece = start.reshape(vec_cols, nb_dev, block)
    piece = lax.dynamic_slice_in_dim(piece, col_index * share, share, 2).reshape(vec_cols, nb_dev * share)
    start_hi, start_lo = split_bf16(piece)
    extra = jnp.concatenate([start_hi, start_lo], axis=0)
    extra = jnp.concatenate(
        [extra, scale_hi[:, None], scale_lo[:, None], jnp.zeros((share, 126), jnp.bfloat16)], axis=1
    )
    rows_bf16 = summed[:, :total_rows].astype(jnp.bfloat16)

    packed = jnp.concatenate([rows_bf16, extra], axis=1)
    copies = jnp.broadcast_to(packed[None], (n_row * n_col,) + packed.shape)
    half = lax.all_to_all(copies, ("row", "col"), 0, 0, tiled=True)
    copies = jnp.broadcast_to(half[None], (2,) + half.shape)
    whole = lax.all_to_all(copies, "vec", 0, 0, tiled=True).reshape(total_rows, total_rows + 256)
    weights = whole[:, :total_rows]
    extras = whole[:, total_rows:]
    scaling = (
        extras[:, nb_dev * share].astype(jnp.float32) + extras[:, nb_dev * share + 1].astype(jnp.float32)
    )[None, :]
    coded = extras[:, : nb_dev * share].astype(jnp.float32)
    coded = coded.reshape(2, n_row, n_col, 2, vec_cols, nb_dev, share)
    coded = coded[:, :, :, 0] + coded[:, :, :, 1]
    current = coded.transpose(0, 3, 4, 1, 2, 5).reshape(cols, total_rows)

    def apply_dense(values):
        product = jnp.einsum(
            "cj,ij->ci", values.astype(jnp.bfloat16), weights, preferred_element_type=jnp.float32
        )
        return product * scaling

    for outer in range(ITERS):
        current = orthonormal_local(chebyshev(current, apply_dense))
    mine = current.reshape(cols, nb_dev, n_row, block)
    mine = lax.dynamic_index_in_dim(mine, row_index, 2, keepdims=False).reshape(cols, nb_dev * block)
    current = lax.dynamic_slice_in_dim(mine, vec_index * vec_cols, vec_cols, 0)
    return current


def per_device(start, tiles, pattern, counts):
    total_rows = tiles.shape[0] * tiles.shape[2] * lax.axis_size("row")
    n_col, n_vec = lax.axis_size("col"), lax.axis_size("vec")
    block = tiles.shape[2]
    fits = (
        total_rows * total_rows * 2 <= DENSE_BUDGET
        and n_vec == 2
        and tiles.shape[0] == n_vec
        and block % n_col == 0
        and block // n_col == 2 * start.shape[0]
        and tiles.shape[0] * (block // n_col) <= 128
    )
    if fits:
        return replicated(start, tiles, pattern, counts)
    return distributed(start, tiles, pattern, counts)


def solution(mesh):
    in_specs = (
        P("vec", ("grp", "row")),
        P(("grp", "row"), "col", None, None),
        P(("grp", "row"), None),
        P(("grp", "row")),
    )
    out_specs = P("vec", ("grp", "row"))
    return jax.shard_map(
        per_device, mesh=mesh, in_specs=in_specs, out_specs=out_specs, check_vma=False
    )
```

```python
import jax
import jax.numpy as jnp
from jax import lax
from jax.experimental import pallas as pl
from jax.experimental.pallas import tpu as pltpu
from jax.sharding import PartitionSpec as P

DEGREE = 8
ITERS = 2


HALF_WIDTH = 2.0
EPSILON = 1e-06
DENSE_BUDGET = 16 * 1024 * 1024


def row_scaling(square_sums, live_counts, block):
    entries = (live_counts * block).astype(jnp.float32)[:, None]
    scaled = lax.rsqrt(square_sums / entries + EPSILON) / jnp.sqrt(entries)
    return (scaled / HALF_WIDTH).reshape(1, -1)


def chebyshev(first, apply):
    previous = first
    present = apply(first)
    for step in range(DEGREE - 1):
        previous, present = (present, 2.0 * apply(present) - previous)
    return present


def orthonormal(mine, total_rows):
    both = lax.all_gather(mine.astype(jnp.bfloat16), "vec", axis=0, tiled=True).astype(mine.dtype)
    part_gram = jnp.dot(both, both.T, precision=lax.Precision.HIGHEST)
    gram = lax.psum(part_gram, "row") / total_rows
    lower = jnp.linalg.cholesky(gram)
    solved = jax.scipy.linalg.solve_triangular(lower, both, lower=True)
    width = mine.shape[0]
    return lax.dynamic_slice_in_dim(solved, lax.axis_index("vec") * width, width, 0)


def orthonormal_value(y):
    n, total = y.shape
    hi = lax.Precision.HIGHEST
    a = lax.dot_general(y, y, (((1,), (1,)), ((), ())), precision=hi, preferred_element_type=jnp.float32)
    a = a / total
    rows = lax.broadcasted_iota(jnp.int32, (n, n), 0)
    cols = lax.broadcasted_iota(jnp.int32, (n, n), 1)
    inverse = (rows == cols).astype(jnp.float32)
    for k in range(n):
        pivot = jnp.sqrt(a[k : k + 1, k : k + 1])
        down = jnp.where(rows[:, k : k + 1] >= k, a[:, k : k + 1] / pivot, 0.0)
        across = jnp.where(cols[k : k + 1, :] >= k, a[k : k + 1, :] / pivot, 0.0)
        a = a - down * across
        solved = inverse[k : k + 1, :] / pivot
        below = jnp.where(rows[:, k : k + 1] > k, down, 0.0)
        inverse = jnp.where(rows == k, solved, inverse - below * solved)
    return lax.dot_general(
        inverse, y, (((1,), (0,)), ((), ())), precision=hi, preferred_element_type=jnp.float32
    )


def filter_kernel(w_ref, s_ref, y_ref, x_ref):
    total = y_ref.shape[1]
    scaling = s_ref[...]

    def apply(values):
        product = lax.dot_general(
            values.astype(jnp.bfloat16),
            w_ref[:, :total],
            (((1,), (1,)), ((), ())),
            preferred_element_type=jnp.float32,
        )
        return product * scaling

    current = y_ref[...]
    for outer in range(ITERS):
        current = orthonormal_value(chebyshev(current, apply))
    x_ref[...] = current


def filter_local(packed_weights, scaling, start):
    return pl.pallas_call(
        filter_kernel,
        out_shape=jax.ShapeDtypeStruct(start.shape, jnp.float32),
        in_specs=[pl.BlockSpec(memory_space=pltpu.VMEM)] * 3,
        out_specs=pl.BlockSpec(memory_space=pltpu.VMEM),
    )(packed_weights, scaling, start)

def distributed(start, tiles, pattern, counts):
    nb_dev = tiles.shape[0]
    block = tiles.shape[2]
    total_rows = nb_dev * block * lax.axis_size("row")
    vec_cols = start.shape[0]
    col_index = lax.axis_index("col")
    kb_dev = tiles.shape[1]
    slot_ids = col_index * kb_dev + jnp.arange(kb_dev, dtype=jnp.int32)
    live = (slot_ids[None, :] < counts[:, None]).astype(jnp.bfloat16)
    masked = tiles * live[:, :, None, None]
    local_pattern = lax.dynamic_slice_in_dim(pattern, col_index * kb_dev, kb_dev, 1)
    partial_squares = jnp.einsum(
        "bkmn,bkmn->bm", masked, masked, preferred_element_type=jnp.float32
    )
    square_sums = lax.psum(partial_squares, "col")
    scaling = row_scaling(square_sums, counts, block)

    def apply_slots(current):
        whole = lax.all_gather(current.astype(jnp.bfloat16), "row", axis=1, tiled=True)
        blocks = whole.reshape(vec_cols, -1, block)
        picked = jnp.take(blocks, local_pattern, axis=1)
        product = jnp.einsum("cbkn,bkmn->cbm", picked, masked, preferred_element_type=jnp.float32)
        total = lax.psum(product.astype(jnp.bfloat16), "col").astype(jnp.float32)
        return total.reshape(vec_cols, -1) * scaling

    current = start
    for outer in range(ITERS):
        filtered = chebyshev(current, apply_slots)
        current = orthonormal(filtered, total_rows)
    return current


def split_bf16(values):
    high = values.astype(jnp.bfloat16)
    low = (values - high.astype(jnp.float32)).astype(jnp.bfloat16)
    return high, low


def replicated(start, tiles, pattern, counts):
    nb_dev, kb_dev, block = tiles.shape[0], tiles.shape[1], tiles.shape[2]
    n_row, n_col = lax.axis_size("row"), lax.axis_size("col")
    nblk = nb_dev * n_row
    total_rows = nblk * block
    share = block // n_col
    vec_cols = start.shape[0]
    cols = 2 * vec_cols
    row_index = lax.axis_index("row")
    col_index = lax.axis_index("col")
    vec_index = lax.axis_index("vec")

    own_tiles = lax.dynamic_index_in_dim(tiles, vec_index, 0, keepdims=False)
    own_pattern = lax.dynamic_slice_in_dim(
        lax.dynamic_index_in_dim(pattern, vec_index, 0, keepdims=False), col_index * kb_dev, kb_dev, 0
    )
    own_count = lax.dynamic_index_in_dim(counts, vec_index, 0, keepdims=False)
    slot_ids = col_index * kb_dev + jnp.arange(kb_dev, dtype=jnp.int32)
    live = slot_ids < own_count
    position = (own_pattern % nb_dev) * n_row + own_pattern // nb_dev
    onehot = (position[:, None] == jnp.arange(nblk, dtype=jnp.int32)) & live[:, None]
    dense = jnp.einsum(
        "kj,kmn->mjn", onehot.astype(jnp.bfloat16), own_tiles, preferred_element_type=jnp.float32
    ).reshape(block, total_rows)
    masked = own_tiles * live.astype(jnp.bfloat16)[:, None, None]
    squares = jnp.einsum("kmn,kmn->m", masked, masked, preferred_element_type=jnp.float32)
    squares = jnp.broadcast_to(squares[:, None], (block, 128))
    partial = jnp.concatenate([dense, squares], axis=1)
    chunks = partial.reshape(n_col, share, total_rows + 128)
    summed = jnp.sum(lax.all_to_all(chunks, "col", 0, 0, tiled=True), axis=0)

    entries = (own_count * block).astype(jnp.float32)
    scale = lax.rsqrt(summed[:, total_rows] / entries + EPSILON) / jnp.sqrt(entries) / HALF_WIDTH
    scale_hi, scale_lo = split_bf16(scale)

    piece = start.reshape(vec_cols, nb_dev, block)
    piece = lax.dynamic_slice_in_dim(piece, col_index * share, share, 2).reshape(vec_cols, nb_dev * share)
    start_hi, start_lo = split_bf16(piece)
    extra = jnp.concatenate([start_hi, start_lo], axis=0)
    extra = jnp.concatenate(
        [extra, scale_hi[:, None], scale_lo[:, None], jnp.zeros((share, 126), jnp.bfloat16)], axis=1
    )
    rows_bf16 = summed[:, :total_rows].astype(jnp.bfloat16)

    packed = jnp.concatenate([rows_bf16, extra], axis=1)
    copies = jnp.broadcast_to(packed[None], (n_row * n_col,) + packed.shape)
    half = lax.all_to_all(copies, ("row", "col"), 0, 0, tiled=True)
    copies = jnp.broadcast_to(half[None], (2,) + half.shape)
    whole = lax.all_to_all(copies, "vec", 0, 0, tiled=True).reshape(total_rows, total_rows + 256)
    extras = whole[:, total_rows:]
    scaling = (
        extras[:, nb_dev * share].astype(jnp.float32) + extras[:, nb_dev * share + 1].astype(jnp.float32)
    )[None, :]
    coded = extras[:, : nb_dev * share].astype(jnp.float32)
    coded = coded.reshape(2, n_row, n_col, 2, vec_cols, nb_dev, share)
    coded = coded[:, :, :, 0] + coded[:, :, :, 1]
    current = coded.transpose(0, 3, 4, 1, 2, 5).reshape(cols, total_rows)

    current = filter_local(whole, scaling, current)
    mine = current.reshape(cols, nb_dev, n_row, block)
    mine = lax.dynamic_index_in_dim(mine, row_index, 2, keepdims=False).reshape(cols, nb_dev * block)
    current = lax.dynamic_slice_in_dim(mine, vec_index * vec_cols, vec_cols, 0)
    return current


def per_device(start, tiles, pattern, counts):
    total_rows = tiles.shape[0] * tiles.shape[2] * lax.axis_size("row")
    n_col, n_vec = lax.axis_size("col"), lax.axis_size("vec")
    block = tiles.shape[2]
    fits = (
        total_rows * total_rows * 2 <= DENSE_BUDGET
        and n_vec == 2
        and tiles.shape[0] == n_vec
        and block % n_col == 0
        and block // n_col == 2 * start.shape[0]
        and tiles.shape[0] * (block // n_col) <= 128
    )
    if fits:
        return replicated(start, tiles, pattern, counts)
    return distributed(start, tiles, pattern, counts)


def solution(mesh):
    in_specs = (
        P("vec", ("grp", "row")),
        P(("grp", "row"), "col", None, None),
        P(("grp", "row"), None),
        P(("grp", "row")),
    )
    out_specs = P("vec", ("grp", "row"))
    return jax.shard_map(
        per_device, mesh=mesh, in_specs=in_specs, out_specs=out_specs, check_vma=False
    )
```

```python
import jax
import jax.numpy as jnp
from jax import lax
from jax.experimental import pallas as pl
from jax.experimental.pallas import tpu as pltpu
from jax.sharding import PartitionSpec as P

DEGREE = 8
ITERS = 2


HALF_WIDTH = 2.0
EPSILON = 1e-06
DENSE_BUDGET = 16 * 1024 * 1024


def row_scaling(square_sums, live_counts, block):
    entries = (live_counts * block).astype(jnp.float32)[:, None]
    scaled = lax.rsqrt(square_sums / entries + EPSILON) / jnp.sqrt(entries)
    return (scaled / HALF_WIDTH).reshape(1, -1)


def chebyshev(first, apply):
    previous = first
    present = apply(first)
    for step in range(DEGREE - 1):
        previous, present = (present, 2.0 * apply(present) - previous)
    return present


def orthonormal(mine, total_rows):
    both = lax.all_gather(mine.astype(jnp.bfloat16), "vec", axis=0, tiled=True).astype(mine.dtype)
    part_gram = jnp.dot(both, both.T, precision=lax.Precision.HIGHEST)
    gram = lax.psum(part_gram, "row") / total_rows
    lower = jnp.linalg.cholesky(gram)
    solved = jax.scipy.linalg.solve_triangular(lower, both, lower=True)
    width = mine.shape[0]
    return lax.dynamic_slice_in_dim(solved, lax.axis_index("vec") * width, width, 0)


def orthonormal_value(y):
    n, total = y.shape
    hi = lax.Precision.HIGHEST
    a = lax.dot_general(y, y, (((1,), (1,)), ((), ())), precision=hi, preferred_element_type=jnp.float32)
    a = a / total
    rows = lax.broadcasted_iota(jnp.int32, (n, n), 0)
    cols = lax.broadcasted_iota(jnp.int32, (n, n), 1)
    inverse = (rows == cols).astype(jnp.float32)
    diagonal = jnp.zeros((n, 1), jnp.float32)
    for k in range(n):
        pivot = a[k : k + 1, k : k + 1]
        down = jnp.where(rows[:, k : k + 1] > k, a[:, k : k + 1] * (1.0 / pivot), 0.0)
        across = jnp.where(cols[k : k + 1, :] > k, a[k : k + 1, :], 0.0)
        a = a - down * across
        inverse = inverse - down * inverse[k : k + 1, :]
        diagonal = jnp.where(rows[:, :1] == k, pivot, diagonal)
    inverse = inverse / jnp.sqrt(diagonal)
    return lax.dot_general(
        inverse, y, (((1,), (0,)), ((), ())), precision=hi, preferred_element_type=jnp.float32
    )


def filter_kernel(w_ref, s_ref, y_ref, x_ref):
    total = y_ref.shape[1]
    scaling = s_ref[...]

    def apply(values):
        product = lax.dot_general(
            values.astype(jnp.bfloat16),
            w_ref[:, :total],
            (((1,), (1,)), ((), ())),
            preferred_element_type=jnp.float32,
        )
        return product * scaling

    current = y_ref[...]
    for outer in range(ITERS):
        current = orthonormal_value(chebyshev(current, apply))
    x_ref[...] = current


def filter_local(packed_weights, scaling, start):
    return pl.pallas_call(
        filter_kernel,
        out_shape=jax.ShapeDtypeStruct(start.shape, jnp.float32),
        in_specs=[pl.BlockSpec(memory_space=pltpu.VMEM)] * 3,
        out_specs=pl.BlockSpec(memory_space=pltpu.VMEM),
    )(packed_weights, scaling, start)

def distributed(start, tiles, pattern, counts):
    nb_dev = tiles.shape[0]
    block = tiles.shape[2]
    total_rows = nb_dev * block * lax.axis_size("row")
    vec_cols = start.shape[0]
    col_index = lax.axis_index("col")
    kb_dev = tiles.shape[1]
    slot_ids = col_index * kb_dev + jnp.arange(kb_dev, dtype=jnp.int32)
    live = (slot_ids[None, :] < counts[:, None]).astype(jnp.bfloat16)
    masked = tiles * live[:, :, None, None]
    local_pattern = lax.dynamic_slice_in_dim(pattern, col_index * kb_dev, kb_dev, 1)
    partial_squares = jnp.einsum(
        "bkmn,bkmn->bm", masked, masked, preferred_element_type=jnp.float32
    )
    square_sums = lax.psum(partial_squares, "col")
    scaling = row_scaling(square_sums, counts, block)

    def apply_slots(current):
        whole = lax.all_gather(current.astype(jnp.bfloat16), "row", axis=1, tiled=True)
        blocks = whole.reshape(vec_cols, -1, block)
        picked = jnp.take(blocks, local_pattern, axis=1)
        product = jnp.einsum("cbkn,bkmn->cbm", picked, masked, preferred_element_type=jnp.float32)
        total = lax.psum(product.astype(jnp.bfloat16), "col").astype(jnp.float32)
        return total.reshape(vec_cols, -1) * scaling

    current = start
    for outer in range(ITERS):
        filtered = chebyshev(current, apply_slots)
        current = orthonormal(filtered, total_rows)
    return current


def split_bf16(values):
    rounded = lax.reduce_precision(values, exponent_bits=8, mantissa_bits=7)
    return rounded.astype(jnp.bfloat16), (values - rounded).astype(jnp.bfloat16)


def replicated(start, tiles, pattern, counts):
    nb_dev, kb_dev, block = tiles.shape[0], tiles.shape[1], tiles.shape[2]
    n_row, n_col = lax.axis_size("row"), lax.axis_size("col")
    nblk = nb_dev * n_row
    total_rows = nblk * block
    share = block // n_col
    vec_cols = start.shape[0]
    cols = 2 * vec_cols
    row_index = lax.axis_index("row")
    col_index = lax.axis_index("col")
    vec_index = lax.axis_index("vec")

    own_tiles = lax.dynamic_index_in_dim(tiles, vec_index, 0, keepdims=False)
    own_pattern = lax.dynamic_slice_in_dim(
        lax.dynamic_index_in_dim(pattern, vec_index, 0, keepdims=False), col_index * kb_dev, kb_dev, 0
    )
    own_count = lax.dynamic_index_in_dim(counts, vec_index, 0, keepdims=False)
    slot_ids = col_index * kb_dev + jnp.arange(kb_dev, dtype=jnp.int32)
    live = slot_ids < own_count
    position = (own_pattern % nb_dev) * n_row + own_pattern // nb_dev
    onehot = (position[:, None] == jnp.arange(nblk, dtype=jnp.int32)) & live[:, None]
    dense = jnp.einsum(
        "kj,kmn->mjn", onehot.astype(jnp.bfloat16), own_tiles, preferred_element_type=jnp.float32
    ).reshape(block, total_rows)
    masked = own_tiles * live.astype(jnp.bfloat16)[:, None, None]
    squares = jnp.einsum("kmn,kmn->m", masked, masked, preferred_element_type=jnp.float32)
    squares = jnp.broadcast_to(squares[:, None], (block, 128))
    partial = jnp.concatenate([dense, squares], axis=1)
    chunks = partial.reshape(n_col, share, total_rows + 128)
    summed = jnp.sum(lax.all_to_all(chunks, "col", 0, 0, tiled=True), axis=0)

    entries = (own_count * block).astype(jnp.float32)
    scale = lax.rsqrt(summed[:, total_rows] / entries + EPSILON) / jnp.sqrt(entries) / HALF_WIDTH
    scale_hi, scale_lo = split_bf16(scale)

    piece = start.reshape(vec_cols, nb_dev, block)
    piece = lax.dynamic_slice_in_dim(piece, col_index * share, share, 2).reshape(vec_cols, nb_dev * share)
    start_hi, start_lo = split_bf16(piece)
    extra = jnp.concatenate([start_hi, start_lo], axis=0)
    extra = jnp.concatenate(
        [extra, scale_hi[:, None], scale_lo[:, None], jnp.zeros((share, 126), jnp.bfloat16)], axis=1
    )
    rows_bf16 = summed[:, :total_rows].astype(jnp.bfloat16)

    packed = jnp.concatenate([rows_bf16, extra], axis=1)
    copies = jnp.broadcast_to(packed[None], (n_row * n_col,) + packed.shape)
    half = lax.all_to_all(copies, ("row", "col"), 0, 0, tiled=True)
    copies = jnp.broadcast_to(half[None], (2,) + half.shape)
    whole = lax.all_to_all(copies, "vec", 0, 0, tiled=True).reshape(total_rows, total_rows + 256)
    extras = whole[:, total_rows:]
    scaling = (
        extras[:, nb_dev * share].astype(jnp.float32) + extras[:, nb_dev * share + 1].astype(jnp.float32)
    )[None, :]
    coded = extras[:, : nb_dev * share].astype(jnp.float32)
    coded = coded.reshape(2, n_row, n_col, 2, vec_cols, nb_dev, share)
    coded = coded[:, :, :, 0] + coded[:, :, :, 1]
    current = coded.transpose(0, 3, 4, 1, 2, 5).reshape(cols, total_rows)

    current = filter_local(whole, scaling, current)
    mine = current.reshape(cols, nb_dev, n_row, block)
    mine = lax.dynamic_index_in_dim(mine, row_index, 2, keepdims=False).reshape(cols, nb_dev * block)
    current = lax.dynamic_slice_in_dim(mine, vec_index * vec_cols, vec_cols, 0)
    return current


def per_device(start, tiles, pattern, counts):
    total_rows = tiles.shape[0] * tiles.shape[2] * lax.axis_size("row")
    n_col, n_vec = lax.axis_size("col"), lax.axis_size("vec")
    block = tiles.shape[2]
    fits = (
        total_rows * total_rows * 2 <= DENSE_BUDGET
        and n_vec == 2
        and tiles.shape[0] == n_vec
        and block % n_col == 0
        and block // n_col == 2 * start.shape[0]
        and tiles.shape[0] * (block // n_col) <= 128
    )
    if fits:
        return replicated(start, tiles, pattern, counts)
    return distributed(start, tiles, pattern, counts)


def solution(mesh):
    in_specs = (
        P("vec", ("grp", "row")),
        P(("grp", "row"), "col", None, None),
        P(("grp", "row"), None),
        P(("grp", "row")),
    )
    out_specs = P("vec", ("grp", "row"))
    return jax.shard_map(
        per_device, mesh=mesh, in_specs=in_specs, out_specs=out_specs, check_vma=False
    )
```

```python
import jax
import jax.numpy as jnp
from jax import lax
from jax.experimental import pallas as pl
from jax.experimental.pallas import tpu as pltpu
from jax.sharding import PartitionSpec as P

DEGREE = 8
ITERS = 2


HALF_WIDTH = 2.0
EPSILON = 1e-06
DENSE_BUDGET = 16 * 1024 * 1024


def row_scaling(square_sums, live_counts, block):
    entries = (live_counts * block).astype(jnp.float32)[:, None]
    scaled = lax.rsqrt(square_sums / entries + EPSILON) / jnp.sqrt(entries)
    return (scaled / HALF_WIDTH).reshape(1, -1)


def chebyshev(first, apply):
    previous = first
    present = apply(first)
    for step in range(DEGREE - 1):
        previous, present = (present, 2.0 * apply(present) - previous)
    return present


def orthonormal(mine, total_rows):
    both = lax.all_gather(mine.astype(jnp.bfloat16), "vec", axis=0, tiled=True).astype(mine.dtype)
    part_gram = jnp.dot(both, both.T, precision=lax.Precision.HIGHEST)
    gram = lax.psum(part_gram, "row") / total_rows
    lower = jnp.linalg.cholesky(gram)
    solved = jax.scipy.linalg.solve_triangular(lower, both, lower=True)
    width = mine.shape[0]
    return lax.dynamic_slice_in_dim(solved, lax.axis_index("vec") * width, width, 0)


def orthonormal_value(y):
    n, total = y.shape
    hi = lax.Precision.HIGHEST
    a = lax.dot_general(y, y, (((1,), (1,)), ((), ())), precision=hi, preferred_element_type=jnp.float32)
    a = a / total
    rows = lax.broadcasted_iota(jnp.int32, (n, n), 0)
    cols = lax.broadcasted_iota(jnp.int32, (n, n), 1)
    inverse = (rows == cols).astype(jnp.float32)
    diagonal = jnp.zeros((n, 1), jnp.float32)
    for k in range(n):
        top = (k // 8) * 8
        pivot = a[k : k + 1, k : k + 1]
        down = jnp.where(rows[top:, k : k + 1] > k, a[top:, k : k + 1] * (1.0 / pivot), 0.0)
        across = jnp.where(cols[k : k + 1, :] > k, a[k : k + 1, :], 0.0)
        lower_a = a[top:] - down * across
        lower_inverse = inverse[top:] - down * inverse[k : k + 1, :]
        if top:
            a = jnp.concatenate([a[:top], lower_a], axis=0)
            inverse = jnp.concatenate([inverse[:top], lower_inverse], axis=0)
        else:
            a, inverse = lower_a, lower_inverse
        diagonal = jnp.where(rows[:, :1] == k, pivot, diagonal)
    inverse = inverse / jnp.sqrt(diagonal)
    return lax.dot_general(
        inverse, y, (((1,), (0,)), ((), ())), precision=hi, preferred_element_type=jnp.float32
    )


def filter_kernel(w_ref, s_ref, y_ref, x_ref):
    total = y_ref.shape[1]
    scaling = s_ref[...]

    def apply(values):
        product = lax.dot_general(
            values.astype(jnp.bfloat16),
            w_ref[:, :total],
            (((1,), (1,)), ((), ())),
            preferred_element_type=jnp.float32,
        )
        return product * scaling

    current = y_ref[...]
    for outer in range(ITERS):
        current = orthonormal_value(chebyshev(current, apply))
    x_ref[...] = current


def filter_local(packed_weights, scaling, start):
    return pl.pallas_call(
        filter_kernel,
        out_shape=jax.ShapeDtypeStruct(start.shape, jnp.float32),
        in_specs=[pl.BlockSpec(memory_space=pltpu.VMEM)] * 3,
        out_specs=pl.BlockSpec(memory_space=pltpu.VMEM),
    )(packed_weights, scaling, start)

def distributed(start, tiles, pattern, counts):
    nb_dev = tiles.shape[0]
    block = tiles.shape[2]
    total_rows = nb_dev * block * lax.axis_size("row")
    vec_cols = start.shape[0]
    col_index = lax.axis_index("col")
    kb_dev = tiles.shape[1]
    slot_ids = col_index * kb_dev + jnp.arange(kb_dev, dtype=jnp.int32)
    live = (slot_ids[None, :] < counts[:, None]).astype(jnp.bfloat16)
    masked = tiles * live[:, :, None, None]
    local_pattern = lax.dynamic_slice_in_dim(pattern, col_index * kb_dev, kb_dev, 1)
    partial_squares = jnp.einsum(
        "bkmn,bkmn->bm", masked, masked, preferred_element_type=jnp.float32
    )
    square_sums = lax.psum(partial_squares, "col")
    scaling = row_scaling(square_sums, counts, block)

    def apply_slots(current):
        whole = lax.all_gather(current.astype(jnp.bfloat16), "row", axis=1, tiled=True)
        blocks = whole.reshape(vec_cols, -1, block)
        picked = jnp.take(blocks, local_pattern, axis=1)
        product = jnp.einsum("cbkn,bkmn->cbm", picked, masked, preferred_element_type=jnp.float32)
        total = lax.psum(product.astype(jnp.bfloat16), "col").astype(jnp.float32)
        return total.reshape(vec_cols, -1) * scaling

    current = start
    for outer in range(ITERS):
        filtered = chebyshev(current, apply_slots)
        current = orthonormal(filtered, total_rows)
    return current


def split_bf16(values):
    rounded = lax.reduce_precision(values, exponent_bits=8, mantissa_bits=7)
    return rounded.astype(jnp.bfloat16), (values - rounded).astype(jnp.bfloat16)


def replicated(start, tiles, pattern, counts):
    nb_dev, kb_dev, block = tiles.shape[0], tiles.shape[1], tiles.shape[2]
    n_row, n_col = lax.axis_size("row"), lax.axis_size("col")
    nblk = nb_dev * n_row
    total_rows = nblk * block
    share = block // n_col
    vec_cols = start.shape[0]
    cols = 2 * vec_cols
    row_index = lax.axis_index("row")
    col_index = lax.axis_index("col")
    vec_index = lax.axis_index("vec")

    own_tiles = lax.dynamic_index_in_dim(tiles, vec_index, 0, keepdims=False)
    own_pattern = lax.dynamic_slice_in_dim(
        lax.dynamic_index_in_dim(pattern, vec_index, 0, keepdims=False), col_index * kb_dev, kb_dev, 0
    )
    own_count = lax.dynamic_index_in_dim(counts, vec_index, 0, keepdims=False)
    slot_ids = col_index * kb_dev + jnp.arange(kb_dev, dtype=jnp.int32)
    live = slot_ids < own_count
    position = (own_pattern % nb_dev) * n_row + own_pattern // nb_dev
    onehot = (position[:, None] == jnp.arange(nblk, dtype=jnp.int32)) & live[:, None]
    dense = jnp.einsum(
        "kj,kmn->mjn", onehot.astype(jnp.bfloat16), own_tiles, preferred_element_type=jnp.float32
    ).reshape(block, total_rows)
    masked = own_tiles * live.astype(jnp.bfloat16)[:, None, None]
    squares = jnp.einsum("kmn,kmn->m", masked, masked, preferred_element_type=jnp.float32)
    squares = jnp.broadcast_to(squares[:, None], (block, 128))
    partial = jnp.concatenate([dense, squares], axis=1)
    chunks = partial.reshape(n_col, share, total_rows + 128)
    summed = jnp.sum(lax.all_to_all(chunks, "col", 0, 0, tiled=True), axis=0)

    entries = (own_count * block).astype(jnp.float32)
    scale = lax.rsqrt(summed[:, total_rows] / entries + EPSILON) / jnp.sqrt(entries) / HALF_WIDTH
    scale_hi, scale_lo = split_bf16(scale)

    piece = start.reshape(vec_cols, nb_dev, block)
    piece = lax.dynamic_slice_in_dim(piece, col_index * share, share, 2).reshape(vec_cols, nb_dev * share)
    start_hi, start_lo = split_bf16(piece)
    extra = jnp.concatenate([start_hi, start_lo], axis=0)
    extra = jnp.concatenate(
        [extra, scale_hi[:, None], scale_lo[:, None], jnp.zeros((share, 126), jnp.bfloat16)], axis=1
    )
    rows_bf16 = summed[:, :total_rows].astype(jnp.bfloat16)

    packed = jnp.concatenate([rows_bf16, extra], axis=1)
    copies = jnp.broadcast_to(packed[None], (n_row * n_col,) + packed.shape)
    half = lax.all_to_all(copies, ("row", "col"), 0, 0, tiled=True)
    copies = jnp.broadcast_to(half[None], (2,) + half.shape)
    whole = lax.all_to_all(copies, "vec", 0, 0, tiled=True).reshape(total_rows, total_rows + 256)
    extras = whole[:, total_rows:]
    scaling = (
        extras[:, nb_dev * share].astype(jnp.float32) + extras[:, nb_dev * share + 1].astype(jnp.float32)
    )[None, :]
    coded = extras[:, : nb_dev * share].astype(jnp.float32)
    coded = coded.reshape(2, n_row, n_col, 2, vec_cols, nb_dev, share)
    coded = coded[:, :, :, 0] + coded[:, :, :, 1]
    current = coded.transpose(0, 3, 4, 1, 2, 5).reshape(cols, total_rows)

    current = filter_local(whole, scaling, current)
    mine = current.reshape(cols, nb_dev, n_row, block)
    mine = lax.dynamic_index_in_dim(mine, row_index, 2, keepdims=False).reshape(cols, nb_dev * block)
    current = lax.dynamic_slice_in_dim(mine, vec_index * vec_cols, vec_cols, 0)
    return current


def per_device(start, tiles, pattern, counts):
    total_rows = tiles.shape[0] * tiles.shape[2] * lax.axis_size("row")
    n_col, n_vec = lax.axis_size("col"), lax.axis_size("vec")
    block = tiles.shape[2]
    fits = (
        total_rows * total_rows * 2 <= DENSE_BUDGET
        and n_vec == 2
        and tiles.shape[0] == n_vec
        and block % n_col == 0
        and block // n_col == 2 * start.shape[0]
        and tiles.shape[0] * (block // n_col) <= 128
    )
    if fits:
        return replicated(start, tiles, pattern, counts)
    return distributed(start, tiles, pattern, counts)


def solution(mesh):
    in_specs = (
        P("vec", ("grp", "row")),
        P(("grp", "row"), "col", None, None),
        P(("grp", "row"), None),
        P(("grp", "row")),
    )
    out_specs = P("vec", ("grp", "row"))
    return jax.shard_map(
        per_device, mesh=mesh, in_specs=in_specs, out_specs=out_specs, check_vma=False
    )
```

```python
import jax
import jax.numpy as jnp
from jax import lax
from jax.experimental import pallas as pl
from jax.experimental.pallas import tpu as pltpu
from jax.sharding import PartitionSpec as P

DEGREE = 8
ITERS = 2


HALF_WIDTH = 2.0
EPSILON = 1e-06
DENSE_BUDGET = 16 * 1024 * 1024


def row_scaling(square_sums, live_counts, block):
    entries = (live_counts * block).astype(jnp.float32)[:, None]
    scaled = lax.rsqrt(square_sums / entries + EPSILON) / jnp.sqrt(entries)
    return (scaled / HALF_WIDTH).reshape(1, -1)


def chebyshev(first, apply):
    previous = first
    present = apply(first)
    for step in range(DEGREE - 1):
        previous, present = (present, 2.0 * apply(present) - previous)
    return present


def orthonormal(mine, total_rows):
    both = lax.all_gather(mine.astype(jnp.bfloat16), "vec", axis=0, tiled=True).astype(mine.dtype)
    part_gram = jnp.dot(both, both.T, precision=lax.Precision.HIGHEST)
    gram = lax.psum(part_gram, "row") / total_rows
    lower = jnp.linalg.cholesky(gram)
    solved = jax.scipy.linalg.solve_triangular(lower, both, lower=True)
    width = mine.shape[0]
    return lax.dynamic_slice_in_dim(solved, lax.axis_index("vec") * width, width, 0)


def orthonormal_value(y):
    n, total = y.shape
    hi = lax.Precision.HIGHEST
    a = lax.dot_general(y, y, (((1,), (1,)), ((), ())), precision=hi, preferred_element_type=jnp.float32)
    a = a / total
    rows = lax.broadcasted_iota(jnp.int32, (n, n), 0)
    cols = lax.broadcasted_iota(jnp.int32, (n, n), 1)
    inverse = (rows == cols).astype(jnp.float32)
    diagonal = jnp.zeros((n, 1), jnp.float32)
    for k in range(n):
        top = (k // 8) * 8
        pivot = a[k : k + 1, k : k + 1]
        down = jnp.where(rows[top:, k : k + 1] > k, a[top:, k : k + 1] * (1.0 / pivot), 0.0)
        across = jnp.where(cols[k : k + 1, :] > k, a[k : k + 1, :], 0.0)
        lower_a = a[top:] - down * across
        lower_inverse = inverse[top:] - down * inverse[k : k + 1, :]
        if top:
            a = jnp.concatenate([a[:top], lower_a], axis=0)
            inverse = jnp.concatenate([inverse[:top], lower_inverse], axis=0)
        else:
            a, inverse = lower_a, lower_inverse
        diagonal = jnp.where(rows[:, :1] == k, pivot, diagonal)
    inverse = inverse / jnp.sqrt(diagonal)
    return lax.dot_general(
        inverse, y, (((1,), (0,)), ((), ())), precision=hi, preferred_element_type=jnp.float32
    )


def filter_kernel(w_ref, y_ref, x_ref):
    total = y_ref.shape[1]

    def apply(values):
        product = lax.dot_general(
            values.astype(jnp.bfloat16),
            w_ref[:, :total],
            (((1,), (1,)), ((), ())),
            preferred_element_type=jnp.float32,
        )
        return product

    current = y_ref[...]
    for outer in range(ITERS):
        current = orthonormal_value(chebyshev(current, apply))
    x_ref[...] = current


def filter_local(packed_weights, start):
    return pl.pallas_call(
        filter_kernel,
        out_shape=jax.ShapeDtypeStruct(start.shape, jnp.float32),
        in_specs=[pl.BlockSpec(memory_space=pltpu.VMEM)] * 2,
        out_specs=pl.BlockSpec(memory_space=pltpu.VMEM),
    )(packed_weights, start)

def distributed(start, tiles, pattern, counts):
    nb_dev = tiles.shape[0]
    block = tiles.shape[2]
    total_rows = nb_dev * block * lax.axis_size("row")
    vec_cols = start.shape[0]
    col_index = lax.axis_index("col")
    kb_dev = tiles.shape[1]
    slot_ids = col_index * kb_dev + jnp.arange(kb_dev, dtype=jnp.int32)
    live = (slot_ids[None, :] < counts[:, None]).astype(jnp.bfloat16)
    masked = tiles * live[:, :, None, None]
    local_pattern = lax.dynamic_slice_in_dim(pattern, col_index * kb_dev, kb_dev, 1)
    partial_squares = jnp.einsum(
        "bkmn,bkmn->bm", masked, masked, preferred_element_type=jnp.float32
    )
    square_sums = lax.psum(partial_squares, "col")
    scaling = row_scaling(square_sums, counts, block)

    def apply_slots(current):
        whole = lax.all_gather(current.astype(jnp.bfloat16), "row", axis=1, tiled=True)
        blocks = whole.reshape(vec_cols, -1, block)
        picked = jnp.take(blocks, local_pattern, axis=1)
        product = jnp.einsum("cbkn,bkmn->cbm", picked, masked, preferred_element_type=jnp.float32)
        total = lax.psum(product.astype(jnp.bfloat16), "col").astype(jnp.float32)
        return total.reshape(vec_cols, -1) * scaling

    current = start
    for outer in range(ITERS):
        filtered = chebyshev(current, apply_slots)
        current = orthonormal(filtered, total_rows)
    return current


def split_bf16(values):
    rounded = lax.reduce_precision(values, exponent_bits=8, mantissa_bits=7)
    return rounded.astype(jnp.bfloat16), (values - rounded).astype(jnp.bfloat16)


def replicated(start, tiles, pattern, counts):
    nb_dev, kb_dev, block = tiles.shape[0], tiles.shape[1], tiles.shape[2]
    n_row, n_col = lax.axis_size("row"), lax.axis_size("col")
    nblk = nb_dev * n_row
    total_rows = nblk * block
    share = block // n_col
    vec_cols = start.shape[0]
    cols = 2 * vec_cols
    row_index = lax.axis_index("row")
    col_index = lax.axis_index("col")
    vec_index = lax.axis_index("vec")

    own_tiles = lax.dynamic_index_in_dim(tiles, vec_index, 0, keepdims=False)
    own_pattern = lax.dynamic_slice_in_dim(
        lax.dynamic_index_in_dim(pattern, vec_index, 0, keepdims=False), col_index * kb_dev, kb_dev, 0
    )
    own_count = lax.dynamic_index_in_dim(counts, vec_index, 0, keepdims=False)
    slot_ids = col_index * kb_dev + jnp.arange(kb_dev, dtype=jnp.int32)
    live = slot_ids < own_count
    position = (own_pattern % nb_dev) * n_row + own_pattern // nb_dev
    onehot = (position[:, None] == jnp.arange(nblk, dtype=jnp.int32)) & live[:, None]
    dense = jnp.einsum(
        "kj,kmn->mjn", onehot.astype(jnp.bfloat16), own_tiles, preferred_element_type=jnp.float32
    ).reshape(block, total_rows)
    masked = own_tiles * live.astype(jnp.bfloat16)[:, None, None]
    squares = jnp.einsum("kmn,kmn->m", masked, masked, preferred_element_type=jnp.float32)
    squares = jnp.broadcast_to(squares[:, None], (block, 128))
    partial = jnp.concatenate([dense, squares], axis=1)
    chunks = partial.reshape(n_col, share, total_rows + 128)
    summed = jnp.sum(lax.all_to_all(chunks, "col", 0, 0, tiled=True), axis=0)

    entries = (own_count * block).astype(jnp.float32)
    scale = lax.rsqrt(summed[:, total_rows] / entries + EPSILON) / jnp.sqrt(entries) / HALF_WIDTH

    piece = start.reshape(vec_cols, nb_dev, block)
    piece = lax.dynamic_slice_in_dim(piece, col_index * share, share, 2).reshape(vec_cols, nb_dev * share)
    start_hi, start_lo = split_bf16(piece)
    extra = jnp.concatenate([start_hi, start_lo], axis=0)
    extra = jnp.concatenate([extra, jnp.zeros((share, 128 - nb_dev * share), jnp.bfloat16)], axis=1)
    rows_bf16 = (summed[:, :total_rows] * scale[:, None]).astype(jnp.bfloat16)

    packed = jnp.concatenate([rows_bf16, extra], axis=1)
    copies = jnp.broadcast_to(packed[None], (n_row * n_col,) + packed.shape)
    half = lax.all_to_all(copies, ("row", "col"), 0, 0, tiled=True)
    copies = jnp.broadcast_to(half[None], (2,) + half.shape)
    whole = lax.all_to_all(copies, "vec", 0, 0, tiled=True).reshape(total_rows, total_rows + 128)
    extras = whole[:, total_rows:]
    coded = extras[:, : nb_dev * share].astype(jnp.float32)
    coded = coded.reshape(2, n_row, n_col, 2, vec_cols, nb_dev, share)
    coded = coded[:, :, :, 0] + coded[:, :, :, 1]
    current = coded.transpose(0, 3, 4, 1, 2, 5).reshape(cols, total_rows)

    current = filter_local(whole, current)
    mine = current.reshape(cols, nb_dev, n_row, block)
    mine = lax.dynamic_index_in_dim(mine, row_index, 2, keepdims=False).reshape(cols, nb_dev * block)
    current = lax.dynamic_slice_in_dim(mine, vec_index * vec_cols, vec_cols, 0)
    return current


def per_device(start, tiles, pattern, counts):
    total_rows = tiles.shape[0] * tiles.shape[2] * lax.axis_size("row")
    n_col, n_vec = lax.axis_size("col"), lax.axis_size("vec")
    block = tiles.shape[2]
    fits = (
        total_rows * total_rows * 2 <= DENSE_BUDGET
        and n_vec == 2
        and tiles.shape[0] == n_vec
        and block % n_col == 0
        and block // n_col == 2 * start.shape[0]
        and tiles.shape[0] * (block // n_col) <= 128
    )
    if fits:
        return replicated(start, tiles, pattern, counts)
    return distributed(start, tiles, pattern, counts)


def solution(mesh):
    in_specs = (
        P("vec", ("grp", "row")),
        P(("grp", "row"), "col", None, None),
        P(("grp", "row"), None),
        P(("grp", "row")),
    )
    out_specs = P("vec", ("grp", "row"))
    return jax.shard_map(
        per_device, mesh=mesh, in_specs=in_specs, out_specs=out_specs, check_vma=False
    )
```

```python
import functools

import jax
import jax.numpy as jnp
from jax import lax
from jax.experimental import pallas as pl
from jax.experimental.pallas import tpu as pltpu
from jax.sharding import PartitionSpec as P

DEGREE = 8
ITERS = 2


HALF_WIDTH = 2.0
EPSILON = 1e-06
DENSE_BUDGET = 16 * 1024 * 1024


def row_scaling(square_sums, live_counts, block):
    entries = (live_counts * block).astype(jnp.float32)[:, None]
    scaled = lax.rsqrt(square_sums / entries + EPSILON) / jnp.sqrt(entries)
    return (scaled / HALF_WIDTH).reshape(1, -1)


def chebyshev(first, apply):
    previous = first
    present = apply(first)
    for step in range(DEGREE - 1):
        previous, present = (present, 2.0 * apply(present) - previous)
    return present


def orthonormal(mine, total_rows):
    both = lax.all_gather(mine.astype(jnp.bfloat16), "vec", axis=0, tiled=True).astype(mine.dtype)
    part_gram = jnp.dot(both, both.T, precision=lax.Precision.HIGHEST)
    gram = lax.psum(part_gram, "row") / total_rows
    lower = jnp.linalg.cholesky(gram)
    solved = jax.scipy.linalg.solve_triangular(lower, both, lower=True)
    width = mine.shape[0]
    return lax.dynamic_slice_in_dim(solved, lax.axis_index("vec") * width, width, 0)


def orthonormal_value(y):
    n, total = y.shape
    hi = lax.Precision.HIGHEST
    a = lax.dot_general(y, y, (((1,), (1,)), ((), ())), precision=hi, preferred_element_type=jnp.float32)
    a = a / total
    rows = lax.broadcasted_iota(jnp.int32, (n, n), 0)
    cols = lax.broadcasted_iota(jnp.int32, (n, n), 1)
    inverse = (rows == cols).astype(jnp.float32)
    diagonal = jnp.zeros((n, 1), jnp.float32)
    for k in range(n):
        top = (k // 8) * 8
        pivot = a[k : k + 1, k : k + 1]
        down = jnp.where(rows[top:, k : k + 1] > k, a[top:, k : k + 1] * (1.0 / pivot), 0.0)
        across = jnp.where(cols[k : k + 1, :] > k, a[k : k + 1, :], 0.0)
        lower_a = a[top:] - down * across
        lower_inverse = inverse[top:] - down * inverse[k : k + 1, :]
        if top:
            a = jnp.concatenate([a[:top], lower_a], axis=0)
            inverse = jnp.concatenate([inverse[:top], lower_inverse], axis=0)
        else:
            a, inverse = lower_a, lower_inverse
        diagonal = jnp.where(rows[:, :1] == k, pivot, diagonal)
    inverse = inverse / jnp.sqrt(diagonal)
    return lax.dot_general(
        inverse, y, (((1,), (0,)), ((), ())), precision=hi, preferred_element_type=jnp.float32
    )


def filter_kernel(index_ref, w_ref, x_ref, whole_ref, *, n_row, n_col, vec_cols):
    total = w_ref.shape[0]
    block = w_ref.shape[1] - total
    nb_dev = total // (block * n_row)
    share = 2 * vec_cols
    halves = []
    for half in range(2):
        parts = []
        for place in range(total // block):
            local, row = divmod(place, n_row)
            base = half * n_row * n_col * share + (row * n_col + local) * share
            high = w_ref[base : base + vec_cols, total:].astype(jnp.float32)
            low = w_ref[base + vec_cols : base + share, total:].astype(jnp.float32)
            parts.append(high + low)
        halves.append(jnp.concatenate(parts, axis=1))
    current = jnp.concatenate(halves, axis=0)

    def apply(values):
        return lax.dot_general(
            values.astype(jnp.bfloat16),
            w_ref[:, :total],
            (((1,), (1,)), ((), ())),
            preferred_element_type=jnp.float32,
        )

    for outer in range(ITERS):
        current = orthonormal_value(chebyshev(current, apply))
    whole_ref[...] = current
    row = index_ref[0]
    first = pl.multiple_of(index_ref[1] * vec_cols, 8)
    for local in range(nb_dev):
        place = pl.multiple_of((local * n_row + row) * block, 128)
        x_ref[:, local * block : (local + 1) * block] = whole_ref[pl.ds(first, vec_cols), pl.ds(place, block)]


def filter_local(packed, index, n_row, n_col, vec_cols):
    total = packed.shape[0]
    block = packed.shape[1] - total
    nb_dev = total // (block * n_row)
    return pl.pallas_call(
        functools.partial(filter_kernel, n_row=n_row, n_col=n_col, vec_cols=vec_cols),
        out_shape=jax.ShapeDtypeStruct((vec_cols, nb_dev * block), jnp.float32),
        in_specs=[pl.BlockSpec(memory_space=pltpu.SMEM), pl.BlockSpec(memory_space=pltpu.VMEM)],
        out_specs=pl.BlockSpec(memory_space=pltpu.VMEM),
        scratch_shapes=[pltpu.VMEM((2 * vec_cols, total), jnp.float32)],
    )(index, packed)

def distributed(start, tiles, pattern, counts):
    nb_dev = tiles.shape[0]
    block = tiles.shape[2]
    total_rows = nb_dev * block * lax.axis_size("row")
    vec_cols = start.shape[0]
    col_index = lax.axis_index("col")
    kb_dev = tiles.shape[1]
    slot_ids = col_index * kb_dev + jnp.arange(kb_dev, dtype=jnp.int32)
    live = (slot_ids[None, :] < counts[:, None]).astype(jnp.bfloat16)
    masked = tiles * live[:, :, None, None]
    local_pattern = lax.dynamic_slice_in_dim(pattern, col_index * kb_dev, kb_dev, 1)
    partial_squares = jnp.einsum(
        "bkmn,bkmn->bm", masked, masked, preferred_element_type=jnp.float32
    )
    square_sums = lax.psum(partial_squares, "col")
    scaling = row_scaling(square_sums, counts, block)

    def apply_slots(current):
        whole = lax.all_gather(current.astype(jnp.bfloat16), "row", axis=1, tiled=True)
        blocks = whole.reshape(vec_cols, -1, block)
        picked = jnp.take(blocks, local_pattern, axis=1)
        product = jnp.einsum("cbkn,bkmn->cbm", picked, masked, preferred_element_type=jnp.float32)
        total = lax.psum(product.astype(jnp.bfloat16), "col").astype(jnp.float32)
        return total.reshape(vec_cols, -1) * scaling

    current = start
    for outer in range(ITERS):
        filtered = chebyshev(current, apply_slots)
        current = orthonormal(filtered, total_rows)
    return current


def split_bf16(values):
    rounded = lax.reduce_precision(values, exponent_bits=8, mantissa_bits=7)
    return rounded.astype(jnp.bfloat16), (values - rounded).astype(jnp.bfloat16)


def replicated(start, tiles, pattern, counts):
    nb_dev, kb_dev, block = tiles.shape[0], tiles.shape[1], tiles.shape[2]
    n_row, n_col = lax.axis_size("row"), lax.axis_size("col")
    nblk = nb_dev * n_row
    total_rows = nblk * block
    share = block // n_col
    vec_cols = start.shape[0]
    cols = 2 * vec_cols
    row_index = lax.axis_index("row")
    col_index = lax.axis_index("col")
    vec_index = lax.axis_index("vec")

    own_tiles = lax.dynamic_index_in_dim(tiles, vec_index, 0, keepdims=False)
    own_pattern = lax.dynamic_slice_in_dim(
        lax.dynamic_index_in_dim(pattern, vec_index, 0, keepdims=False), col_index * kb_dev, kb_dev, 0
    )
    own_count = lax.dynamic_index_in_dim(counts, vec_index, 0, keepdims=False)
    slot_ids = col_index * kb_dev + jnp.arange(kb_dev, dtype=jnp.int32)
    live = slot_ids < own_count
    position = (own_pattern % nb_dev) * n_row + own_pattern // nb_dev
    onehot = (position[:, None] == jnp.arange(nblk, dtype=jnp.int32)) & live[:, None]
    dense = jnp.einsum(
        "kj,kmn->mjn", onehot.astype(jnp.bfloat16), own_tiles, preferred_element_type=jnp.float32
    ).reshape(block, total_rows)
    masked = own_tiles * live.astype(jnp.bfloat16)[:, None, None]
    squares = jnp.einsum("kmn,kmn->m", masked, masked, preferred_element_type=jnp.float32)
    squares = jnp.broadcast_to(squares[:, None], (block, 128))
    partial = jnp.concatenate([dense, squares], axis=1)
    chunks = partial.reshape(n_col, share, total_rows + 128)
    summed = jnp.sum(lax.all_to_all(chunks, "col", 0, 0, tiled=True), axis=0)

    entries = (own_count * block).astype(jnp.float32)
    scale = lax.rsqrt(summed[:, total_rows] / entries + EPSILON) / jnp.sqrt(entries) / HALF_WIDTH

    piece = lax.dynamic_slice_in_dim(start, col_index * block, block, 1)
    start_hi, start_lo = split_bf16(piece)
    extra = jnp.concatenate([start_hi, start_lo], axis=0)
    rows_bf16 = (summed[:, :total_rows] * scale[:, None]).astype(jnp.bfloat16)

    packed = jnp.concatenate([rows_bf16, extra], axis=1)
    copies = jnp.broadcast_to(packed[None], (n_row * n_col,) + packed.shape)
    half = lax.all_to_all(copies, ("row", "col"), 0, 0, tiled=True)
    copies = jnp.broadcast_to(half[None], (2,) + half.shape)
    whole = lax.all_to_all(copies, "vec", 0, 0, tiled=True).reshape(total_rows, total_rows + block)
    index = jnp.stack([row_index, vec_index]).astype(jnp.int32)
    current = filter_local(whole, index, n_row, n_col, vec_cols)
    return current


def per_device(start, tiles, pattern, counts):
    total_rows = tiles.shape[0] * tiles.shape[2] * lax.axis_size("row")
    n_col, n_vec = lax.axis_size("col"), lax.axis_size("vec")
    block = tiles.shape[2]
    fits = (
        total_rows * total_rows * 2 <= DENSE_BUDGET
        and n_vec == 2
        and tiles.shape[0] == n_vec
        and block % n_col == 0
        and block // n_col == 2 * start.shape[0]
        and tiles.shape[0] == n_col
    )
    if fits:
        return replicated(start, tiles, pattern, counts)
    return distributed(start, tiles, pattern, counts)


def solution(mesh):
    in_specs = (
        P("vec", ("grp", "row")),
        P(("grp", "row"), "col", None, None),
        P(("grp", "row"), None),
        P(("grp", "row")),
    )
    out_specs = P("vec", ("grp", "row"))
    return jax.shard_map(
        per_device, mesh=mesh, in_specs=in_specs, out_specs=out_specs, check_vma=False
    )
```

```python
import functools

import jax
import jax.numpy as jnp
from jax import lax
from jax.experimental import pallas as pl
from jax.experimental.pallas import tpu as pltpu
from jax.sharding import PartitionSpec as P

DEGREE = 8
ITERS = 2


HALF_WIDTH = 2.0
EPSILON = 1e-06
DENSE_BUDGET = 16 * 1024 * 1024


def row_scaling(square_sums, live_counts, block):
    entries = (live_counts * block).astype(jnp.float32)[:, None]
    scaled = lax.rsqrt(square_sums / entries + EPSILON) / jnp.sqrt(entries)
    return (scaled / HALF_WIDTH).reshape(1, -1)


def chebyshev(first, apply):
    previous = first
    present = apply(first)
    for step in range(DEGREE - 1):
        previous, present = (present, 2.0 * apply(present) - previous)
    return present


def orthonormal(mine, total_rows):
    both = lax.all_gather(mine.astype(jnp.bfloat16), "vec", axis=0, tiled=True).astype(mine.dtype)
    part_gram = jnp.dot(both, both.T, precision=lax.Precision.HIGHEST)
    gram = lax.psum(part_gram, "row") / total_rows
    lower = jnp.linalg.cholesky(gram)
    solved = jax.scipy.linalg.solve_triangular(lower, both, lower=True)
    width = mine.shape[0]
    return lax.dynamic_slice_in_dim(solved, lax.axis_index("vec") * width, width, 0)


def orthonormal_value(y):
    n, total = y.shape
    hi = lax.Precision.HIGHEST
    a = lax.dot_general(y, y, (((1,), (1,)), ((), ())), precision=hi, preferred_element_type=jnp.float32)
    a = a / total
    rows = lax.broadcasted_iota(jnp.int32, (n, n), 0)
    cols = lax.broadcasted_iota(jnp.int32, (n, n), 1)
    inverse = (rows == cols).astype(jnp.float32)
    diagonal = jnp.zeros((n, 1), jnp.float32)
    for k in range(0, n, 2):
        top = (k // 8) * 8
        first, second = a[k : k + 1, :], a[k + 1 : k + 2, :]
        pivot = first[:, k : k + 1]
        coupling = first[:, k + 1 : k + 2]
        factor = coupling * (1.0 / pivot)
        pivot_next = second[:, k + 1 : k + 2] - factor * coupling
        down = jnp.where(rows[top:, k : k + 1] > k, a[top:, k : k + 1] * (1.0 / pivot), 0.0)
        next_col = a[top:, k + 1 : k + 2] - down * coupling
        down_next = jnp.where(rows[top:, k : k + 1] > k + 1, next_col * (1.0 / pivot_next), 0.0)
        across = jnp.where(cols[k : k + 1, :] > k, first, 0.0)
        across_next = jnp.where(cols[k : k + 1, :] > k + 1, second - factor * first, 0.0)
        lower_a = a[top:] - down * across - down_next * across_next
        inverse_next = inverse[k + 1 : k + 2, :] - factor * inverse[k : k + 1, :]
        lower_inverse = inverse[top:] - down * inverse[k : k + 1, :] - down_next * inverse_next
        if top:
            a = jnp.concatenate([a[:top], lower_a], axis=0)
            inverse = jnp.concatenate([inverse[:top], lower_inverse], axis=0)
        else:
            a, inverse = lower_a, lower_inverse
        diagonal = jnp.where(rows[:, :1] == k, pivot, diagonal)
        diagonal = jnp.where(rows[:, :1] == k + 1, pivot_next, diagonal)
    inverse = inverse / jnp.sqrt(diagonal)
    return lax.dot_general(
        inverse, y, (((1,), (0,)), ((), ())), precision=hi, preferred_element_type=jnp.float32
    )


def filter_kernel(index_ref, w_ref, x_ref, whole_ref, *, n_row, n_col, vec_cols):
    total = w_ref.shape[0]
    block = w_ref.shape[1] - total
    nb_dev = total // (block * n_row)
    share = 2 * vec_cols
    halves = []
    for half in range(2):
        parts = []
        for place in range(total // block):
            local, row = divmod(place, n_row)
            base = half * n_row * n_col * share + (row * n_col + local) * share
            high = w_ref[base : base + vec_cols, total:].astype(jnp.float32)
            low = w_ref[base + vec_cols : base + share, total:].astype(jnp.float32)
            parts.append(high + low)
        halves.append(jnp.concatenate(parts, axis=1))
    current = jnp.concatenate(halves, axis=0)

    def apply(values):
        return lax.dot_general(
            values.astype(jnp.bfloat16),
            w_ref[:, :total],
            (((1,), (1,)), ((), ())),
            preferred_element_type=jnp.float32,
        )

    for outer in range(ITERS):
        current = orthonormal_value(chebyshev(current, apply))
    whole_ref[...] = current
    row = index_ref[0]
    first = pl.multiple_of(index_ref[1] * vec_cols, 8)
    for local in range(nb_dev):
        place = pl.multiple_of((local * n_row + row) * block, 128)
        x_ref[:, local * block : (local + 1) * block] = whole_ref[pl.ds(first, vec_cols), pl.ds(place, block)]


def filter_local(packed, index, n_row, n_col, vec_cols):
    total = packed.shape[0]
    block = packed.shape[1] - total
    nb_dev = total // (block * n_row)
    return pl.pallas_call(
        functools.partial(filter_kernel, n_row=n_row, n_col=n_col, vec_cols=vec_cols),
        out_shape=jax.ShapeDtypeStruct((vec_cols, nb_dev * block), jnp.float32),
        in_specs=[pl.BlockSpec(memory_space=pltpu.SMEM), pl.BlockSpec(memory_space=pltpu.VMEM)],
        out_specs=pl.BlockSpec(memory_space=pltpu.VMEM),
        scratch_shapes=[pltpu.VMEM((2 * vec_cols, total), jnp.float32)],
    )(index, packed)

def distributed(start, tiles, pattern, counts):
    nb_dev = tiles.shape[0]
    block = tiles.shape[2]
    total_rows = nb_dev * block * lax.axis_size("row")
    vec_cols = start.shape[0]
    col_index = lax.axis_index("col")
    kb_dev = tiles.shape[1]
    slot_ids = col_index * kb_dev + jnp.arange(kb_dev, dtype=jnp.int32)
    live = (slot_ids[None, :] < counts[:, None]).astype(jnp.bfloat16)
    masked = tiles * live[:, :, None, None]
    local_pattern = lax.dynamic_slice_in_dim(pattern, col_index * kb_dev, kb_dev, 1)
    partial_squares = jnp.einsum(
        "bkmn,bkmn->bm", masked, masked, preferred_element_type=jnp.float32
    )
    square_sums = lax.psum(partial_squares, "col")
    scaling = row_scaling(square_sums, counts, block)

    def apply_slots(current):
        whole = lax.all_gather(current.astype(jnp.bfloat16), "row", axis=1, tiled=True)
        blocks = whole.reshape(vec_cols, -1, block)
        picked = jnp.take(blocks, local_pattern, axis=1)
        product = jnp.einsum("cbkn,bkmn->cbm", picked, masked, preferred_element_type=jnp.float32)
        total = lax.psum(product.astype(jnp.bfloat16), "col").astype(jnp.float32)
        return total.reshape(vec_cols, -1) * scaling

    current = start
    for outer in range(ITERS):
        filtered = chebyshev(current, apply_slots)
        current = orthonormal(filtered, total_rows)
    return current


def split_bf16(values):
    rounded = lax.reduce_precision(values, exponent_bits=8, mantissa_bits=7)
    return rounded.astype(jnp.bfloat16), (values - rounded).astype(jnp.bfloat16)


def replicated(start, tiles, pattern, counts):
    nb_dev, kb_dev, block = tiles.shape[0], tiles.shape[1], tiles.shape[2]
    n_row, n_col = lax.axis_size("row"), lax.axis_size("col")
    nblk = nb_dev * n_row
    total_rows = nblk * block
    share = block // n_col
    vec_cols = start.shape[0]
    cols = 2 * vec_cols
    row_index = lax.axis_index("row")
    col_index = lax.axis_index("col")
    vec_index = lax.axis_index("vec")

    own_tiles = lax.dynamic_index_in_dim(tiles, vec_index, 0, keepdims=False)
    own_pattern = lax.dynamic_slice_in_dim(
        lax.dynamic_index_in_dim(pattern, vec_index, 0, keepdims=False), col_index * kb_dev, kb_dev, 0
    )
    own_count = lax.dynamic_index_in_dim(counts, vec_index, 0, keepdims=False)
    slot_ids = col_index * kb_dev + jnp.arange(kb_dev, dtype=jnp.int32)
    live = slot_ids < own_count
    position = (own_pattern % nb_dev) * n_row + own_pattern // nb_dev
    onehot = (position[:, None] == jnp.arange(nblk, dtype=jnp.int32)) & live[:, None]
    dense = jnp.einsum(
        "kj,kmn->mjn", onehot.astype(jnp.bfloat16), own_tiles, preferred_element_type=jnp.float32
    ).reshape(block, total_rows)
    masked = own_tiles * live.astype(jnp.bfloat16)[:, None, None]
    squares = jnp.einsum("kmn,kmn->m", masked, masked, preferred_element_type=jnp.float32)
    squares = jnp.broadcast_to(squares[:, None], (block, 128))
    partial = jnp.concatenate([dense, squares], axis=1)
    chunks = partial.reshape(n_col, share, total_rows + 128)
    summed = jnp.sum(lax.all_to_all(chunks, "col", 0, 0, tiled=True), axis=0)

    entries = (own_count * block).astype(jnp.float32)
    scale = lax.rsqrt(summed[:, total_rows] / entries + EPSILON) / jnp.sqrt(entries) / HALF_WIDTH

    piece = lax.dynamic_slice_in_dim(start, col_index * block, block, 1)
    start_hi, start_lo = split_bf16(piece)
    extra = jnp.concatenate([start_hi, start_lo], axis=0)
    rows_bf16 = (summed[:, :total_rows] * scale[:, None]).astype(jnp.bfloat16)

    packed = jnp.concatenate([rows_bf16, extra], axis=1)
    copies = jnp.broadcast_to(packed[None], (n_row * n_col,) + packed.shape)
    half = lax.all_to_all(copies, ("row", "col"), 0, 0, tiled=True)
    copies = jnp.broadcast_to(half[None], (2,) + half.shape)
    whole = lax.all_to_all(copies, "vec", 0, 0, tiled=True).reshape(total_rows, total_rows + block)
    index = jnp.stack([row_index, vec_index]).astype(jnp.int32)
    current = filter_local(whole, index, n_row, n_col, vec_cols)
    return current


def per_device(start, tiles, pattern, counts):
    total_rows = tiles.shape[0] * tiles.shape[2] * lax.axis_size("row")
    n_col, n_vec = lax.axis_size("col"), lax.axis_size("vec")
    block = tiles.shape[2]
    fits = (
        total_rows * total_rows * 2 <= DENSE_BUDGET
        and n_vec == 2
        and tiles.shape[0] == n_vec
        and block % n_col == 0
        and block // n_col == 2 * start.shape[0]
        and tiles.shape[0] == n_col
    )
    if fits:
        return replicated(start, tiles, pattern, counts)
    return distributed(start, tiles, pattern, counts)


def solution(mesh):
    in_specs = (
        P("vec", ("grp", "row")),
        P(("grp", "row"), "col", None, None),
        P(("grp", "row"), None),
        P(("grp", "row")),
    )
    out_specs = P("vec", ("grp", "row"))
    return jax.shard_map(
        per_device, mesh=mesh, in_specs=in_specs, out_specs=out_specs, check_vma=False
    )
```

```python
import functools

import jax
import jax.numpy as jnp
from jax import lax
from jax.experimental import pallas as pl
from jax.experimental.pallas import tpu as pltpu
from jax.sharding import PartitionSpec as P

DEGREE = 8
ITERS = 2


HALF_WIDTH = 2.0
EPSILON = 1e-06
DENSE_BUDGET = 16 * 1024 * 1024


def row_scaling(square_sums, live_counts, block):
    entries = (live_counts * block).astype(jnp.float32)[:, None]
    scaled = lax.rsqrt(square_sums / entries + EPSILON) / jnp.sqrt(entries)
    return (scaled / HALF_WIDTH).reshape(1, -1)


def chebyshev(first, apply):
    previous = first
    present = apply(first)
    for step in range(DEGREE - 1):
        previous, present = (present, 2.0 * apply(present) - previous)
    return present


def orthonormal(mine, total_rows):
    both = lax.all_gather(mine.astype(jnp.bfloat16), "vec", axis=0, tiled=True).astype(mine.dtype)
    part_gram = jnp.dot(both, both.T, precision=lax.Precision.HIGHEST)
    gram = lax.psum(part_gram, "row") / total_rows
    lower = jnp.linalg.cholesky(gram)
    solved = jax.scipy.linalg.solve_triangular(lower, both, lower=True)
    width = mine.shape[0]
    return lax.dynamic_slice_in_dim(solved, lax.axis_index("vec") * width, width, 0)


def orthonormal_value(y):
    n, total = y.shape
    hi = lax.Precision.HIGHEST
    a = lax.dot_general(y, y, (((1,), (1,)), ((), ())), precision=hi, preferred_element_type=jnp.float32)
    a = a / total
    rows = lax.broadcasted_iota(jnp.int32, (n, n), 0)
    cols = lax.broadcasted_iota(jnp.int32, (n, n), 1)
    inverse = (rows == cols).astype(jnp.float32)
    diagonal = jnp.zeros((n, 1), jnp.float32)
    for k in range(n):
        top = (k // 8) * 8
        pivot = a[k : k + 1, k : k + 1]
        down = jnp.where(rows[top:, k : k + 1] > k, a[top:, k : k + 1] * (1.0 / pivot), 0.0)
        across = jnp.where(cols[k : k + 1, :] > k, a[k : k + 1, :], 0.0)
        lower_a = a[top:] - down * across
        lower_inverse = inverse[top:] - down * inverse[k : k + 1, :]
        if top:
            a = jnp.concatenate([a[:top], lower_a], axis=0)
            inverse = jnp.concatenate([inverse[:top], lower_inverse], axis=0)
        else:
            a, inverse = lower_a, lower_inverse
        diagonal = jnp.where(rows[:, :1] == k, pivot, diagonal)
    inverse = inverse / jnp.sqrt(diagonal)
    return lax.dot_general(
        inverse, y, (((1,), (0,)), ((), ())), precision=hi, preferred_element_type=jnp.float32
    )


def filter_kernel(index_ref, w_ref, x_ref, whole_ref, *, n_row, n_col, vec_cols):
    total = w_ref.shape[0]
    block = w_ref.shape[1] - total
    nb_dev = total // (block * n_row)
    share = 2 * vec_cols
    halves = []
    for half in range(2):
        parts = []
        for place in range(total // block):
            local, row = divmod(place, n_row)
            base = half * n_row * n_col * share + (row * n_col + local) * share
            high = w_ref[base : base + vec_cols, total:].astype(jnp.float32)
            low = w_ref[base + vec_cols : base + share, total:].astype(jnp.float32)
            parts.append(high + low)
        halves.append(jnp.concatenate(parts, axis=1))
    current = jnp.concatenate(halves, axis=0)

    def apply(values):
        return lax.dot_general(
            values.astype(jnp.bfloat16),
            w_ref[:, :total],
            (((1,), (1,)), ((), ())),
            preferred_element_type=jnp.float32,
        )

    for outer in range(ITERS):
        current = orthonormal_value(chebyshev(current, apply))
    whole_ref[...] = current
    row = index_ref[0]
    first = pl.multiple_of(index_ref[1] * vec_cols, 8)
    for local in range(nb_dev):
        place = pl.multiple_of((local * n_row + row) * block, 128)
        x_ref[:, local * block : (local + 1) * block] = whole_ref[pl.ds(first, vec_cols), pl.ds(place, block)]


def filter_local(packed, index, n_row, n_col, vec_cols):
    total = packed.shape[0]
    block = packed.shape[1] - total
    nb_dev = total // (block * n_row)
    return pl.pallas_call(
        functools.partial(filter_kernel, n_row=n_row, n_col=n_col, vec_cols=vec_cols),
        out_shape=jax.ShapeDtypeStruct((vec_cols, nb_dev * block), jnp.float32),
        in_specs=[pl.BlockSpec(memory_space=pltpu.SMEM), pl.BlockSpec(memory_space=pltpu.VMEM)],
        out_specs=pl.BlockSpec(memory_space=pltpu.VMEM),
        scratch_shapes=[pltpu.VMEM((2 * vec_cols, total), jnp.float32)],
    )(index, packed)

def distributed(start, tiles, pattern, counts):
    nb_dev = tiles.shape[0]
    block = tiles.shape[2]
    total_rows = nb_dev * block * lax.axis_size("row")
    vec_cols = start.shape[0]
    col_index = lax.axis_index("col")
    kb_dev = tiles.shape[1]
    slot_ids = col_index * kb_dev + jnp.arange(kb_dev, dtype=jnp.int32)
    live = (slot_ids[None, :] < counts[:, None]).astype(jnp.bfloat16)
    masked = tiles * live[:, :, None, None]
    local_pattern = lax.dynamic_slice_in_dim(pattern, col_index * kb_dev, kb_dev, 1)
    partial_squares = jnp.einsum(
        "bkmn,bkmn->bm", masked, masked, preferred_element_type=jnp.float32
    )
    square_sums = lax.psum(partial_squares, "col")
    scaling = row_scaling(square_sums, counts, block)

    def apply_slots(current):
        whole = lax.all_gather(current.astype(jnp.bfloat16), "row", axis=1, tiled=True)
        blocks = whole.reshape(vec_cols, -1, block)
        picked = jnp.take(blocks, local_pattern, axis=1)
        product = jnp.einsum("cbkn,bkmn->cbm", picked, masked, preferred_element_type=jnp.float32)
        total = lax.psum(product.astype(jnp.bfloat16), "col").astype(jnp.float32)
        return total.reshape(vec_cols, -1) * scaling

    current = start
    for outer in range(ITERS):
        filtered = chebyshev(current, apply_slots)
        current = orthonormal(filtered, total_rows)
    return current


def split_bf16(values):
    rounded = lax.reduce_precision(values, exponent_bits=8, mantissa_bits=7)
    return rounded.astype(jnp.bfloat16), (values - rounded).astype(jnp.bfloat16)


def replicated(start, tiles, pattern, counts):
    nb_dev, kb_dev, block = tiles.shape[0], tiles.shape[1], tiles.shape[2]
    n_row, n_col = lax.axis_size("row"), lax.axis_size("col")
    nblk = nb_dev * n_row
    total_rows = nblk * block
    share = block // n_col
    vec_cols = start.shape[0]
    cols = 2 * vec_cols
    row_index = lax.axis_index("row")
    col_index = lax.axis_index("col")
    vec_index = lax.axis_index("vec")

    own_tiles = lax.dynamic_index_in_dim(tiles, vec_index, 0, keepdims=False)
    own_pattern = lax.dynamic_slice_in_dim(
        lax.dynamic_index_in_dim(pattern, vec_index, 0, keepdims=False), col_index * kb_dev, kb_dev, 0
    )
    own_count = lax.dynamic_index_in_dim(counts, vec_index, 0, keepdims=False)
    slot_ids = col_index * kb_dev + jnp.arange(kb_dev, dtype=jnp.int32)
    live = slot_ids < own_count
    position = (own_pattern % nb_dev) * n_row + own_pattern // nb_dev
    onehot = (position[:, None] == jnp.arange(nblk, dtype=jnp.int32)) & live[:, None]
    dense = jnp.einsum(
        "kj,kmn->mjn", onehot.astype(jnp.bfloat16), own_tiles, preferred_element_type=jnp.float32
    ).reshape(block, total_rows)
    masked = own_tiles * live.astype(jnp.bfloat16)[:, None, None]
    squares = jnp.einsum("kmn,kmn->m", masked, masked, preferred_element_type=jnp.float32)
    squares = jnp.broadcast_to(squares[:, None], (block, 128))
    partial = jnp.concatenate([dense, squares], axis=1)
    chunks = partial.reshape(n_col, share, total_rows + 128)
    summed = lax.dynamic_index_in_dim(chunks, col_index, 0, keepdims=False)
    for shift in range(1, n_col):
        sent = lax.dynamic_index_in_dim(chunks, (col_index + shift) % n_col, 0, keepdims=False)
        summed = summed + lax.ppermute(sent, "col", [(i, (i + shift) % n_col) for i in range(n_col)])

    entries = (own_count * block).astype(jnp.float32)
    scale = lax.rsqrt(summed[:, total_rows] / entries + EPSILON) / jnp.sqrt(entries) / HALF_WIDTH

    piece = lax.dynamic_slice_in_dim(start, col_index * block, block, 1)
    start_hi, start_lo = split_bf16(piece)
    extra = jnp.concatenate([start_hi, start_lo], axis=0)
    rows_bf16 = (summed[:, :total_rows] * scale[:, None]).astype(jnp.bfloat16)

    packed = jnp.concatenate([rows_bf16, extra], axis=1)
    copies = jnp.broadcast_to(packed[None], (n_row * n_col,) + packed.shape)
    half = lax.all_to_all(copies, ("row", "col"), 0, 0, tiled=True)
    copies = jnp.broadcast_to(half[None], (2,) + half.shape)
    whole = lax.all_to_all(copies, "vec", 0, 0, tiled=True).reshape(total_rows, total_rows + block)
    index = jnp.stack([row_index, vec_index]).astype(jnp.int32)
    current = filter_local(whole, index, n_row, n_col, vec_cols)
    return current


def per_device(start, tiles, pattern, counts):
    total_rows = tiles.shape[0] * tiles.shape[2] * lax.axis_size("row")
    n_col, n_vec = lax.axis_size("col"), lax.axis_size("vec")
    block = tiles.shape[2]
    fits = (
        total_rows * total_rows * 2 <= DENSE_BUDGET
        and n_vec == 2
        and tiles.shape[0] == n_vec
        and block % n_col == 0
        and block // n_col == 2 * start.shape[0]
        and tiles.shape[0] == n_col
    )
    if fits:
        return replicated(start, tiles, pattern, counts)
    return distributed(start, tiles, pattern, counts)


def solution(mesh):
    in_specs = (
        P("vec", ("grp", "row")),
        P(("grp", "row"), "col", None, None),
        P(("grp", "row"), None),
        P(("grp", "row")),
    )
    out_specs = P("vec", ("grp", "row"))
    return jax.shard_map(
        per_device, mesh=mesh, in_specs=in_specs, out_specs=out_specs, check_vma=False
    )
```

```python
import functools

import jax
import jax.numpy as jnp
from jax import lax
from jax.experimental import pallas as pl
from jax.experimental.pallas import tpu as pltpu
from jax.sharding import PartitionSpec as P

DEGREE = 8
ITERS = 2


HALF_WIDTH = 2.0
EPSILON = 1e-06
DENSE_BUDGET = 16 * 1024 * 1024


def row_scaling(square_sums, live_counts, block):
    entries = (live_counts * block).astype(jnp.float32)[:, None]
    scaled = lax.rsqrt(square_sums / entries + EPSILON) / jnp.sqrt(entries)
    return (scaled / HALF_WIDTH).reshape(1, -1)


def chebyshev(first, apply):
    previous = first
    present = apply(first)
    for step in range(DEGREE - 1):
        previous, present = (present, 2.0 * apply(present) - previous)
    return present


def orthonormal(mine, total_rows):
    both = lax.all_gather(mine.astype(jnp.bfloat16), "vec", axis=0, tiled=True).astype(mine.dtype)
    part_gram = jnp.dot(both, both.T, precision=lax.Precision.HIGHEST)
    gram = lax.psum(part_gram, "row") / total_rows
    lower = jnp.linalg.cholesky(gram)
    solved = jax.scipy.linalg.solve_triangular(lower, both, lower=True)
    width = mine.shape[0]
    return lax.dynamic_slice_in_dim(solved, lax.axis_index("vec") * width, width, 0)


def orthonormal_value(y):
    n, total = y.shape
    hi = lax.Precision.HIGHEST
    a = lax.dot_general(y, y, (((1,), (1,)), ((), ())), precision=hi, preferred_element_type=jnp.float32)
    a = a / total
    rows = lax.broadcasted_iota(jnp.int32, (n, n), 0)
    cols = lax.broadcasted_iota(jnp.int32, (n, n), 1)
    inverse = (rows == cols).astype(jnp.float32)
    diagonal = jnp.zeros((n, 1), jnp.float32)
    for k in range(n):
        top = (k // 8) * 8
        pivot = a[k : k + 1, k : k + 1]
        down = jnp.where(rows[top:, k : k + 1] > k, a[top:, k : k + 1] * (1.0 / pivot), 0.0)
        across = jnp.where(cols[k : k + 1, :] > k, a[k : k + 1, :], 0.0)
        lower_a = a[top:] - down * across
        lower_inverse = inverse[top:] - down * inverse[k : k + 1, :]
        if top:
            a = jnp.concatenate([a[:top], lower_a], axis=0)
            inverse = jnp.concatenate([inverse[:top], lower_inverse], axis=0)
        else:
            a, inverse = lower_a, lower_inverse
        diagonal = jnp.where(rows[:, :1] == k, pivot, diagonal)
    inverse = inverse / jnp.sqrt(diagonal)
    return lax.dot_general(
        inverse, y, (((1,), (0,)), ((), ())), precision=hi, preferred_element_type=jnp.float32
    )


def filter_kernel(index_ref, w_ref, x_ref, whole_ref, *, n_row, n_col, vec_cols):
    total = w_ref.shape[0]
    block = w_ref.shape[1] - total
    nb_dev = total // (block * n_row)
    share = 2 * vec_cols
    halves = []
    for half in range(2):
        parts = []
        for place in range(total // block):
            local, row = divmod(place, n_row)
            base = half * n_row * n_col * share + (row * n_col + local) * share
            high = w_ref[base : base + vec_cols, total:].astype(jnp.float32)
            low = w_ref[base + vec_cols : base + share, total:].astype(jnp.float32)
            parts.append(high + low)
        halves.append(jnp.concatenate(parts, axis=1))
    current = jnp.concatenate(halves, axis=0)

    def apply(values):
        return lax.dot_general(
            values.astype(jnp.bfloat16),
            w_ref[:, :total],
            (((1,), (1,)), ((), ())),
            preferred_element_type=jnp.float32,
        )

    for outer in range(ITERS):
        current = orthonormal_value(chebyshev(current, apply))
    whole_ref[...] = current
    row = index_ref[0]
    first = pl.multiple_of(index_ref[1] * vec_cols, 8)
    for local in range(nb_dev):
        place = pl.multiple_of((local * n_row + row) * block, 128)
        x_ref[:, local * block : (local + 1) * block] = whole_ref[pl.ds(first, vec_cols), pl.ds(place, block)]


def filter_local(packed, index, n_row, n_col, vec_cols):
    total = packed.shape[0]
    block = packed.shape[1] - total
    nb_dev = total // (block * n_row)
    return pl.pallas_call(
        functools.partial(filter_kernel, n_row=n_row, n_col=n_col, vec_cols=vec_cols),
        out_shape=jax.ShapeDtypeStruct((vec_cols, nb_dev * block), jnp.float32),
        in_specs=[pl.BlockSpec(memory_space=pltpu.SMEM), pl.BlockSpec(memory_space=pltpu.VMEM)],
        out_specs=pl.BlockSpec(memory_space=pltpu.VMEM),
        scratch_shapes=[pltpu.VMEM((2 * vec_cols, total), jnp.float32)],
    )(index, packed)

def partial_kernel(meta_ref, tiles_ref, out_ref, squares_ref):
    slots, block = tiles_ref.shape[1], tiles_ref.shape[2]
    total = out_ref.shape[1] - 128
    own = meta_ref[0]
    out_ref[...] = jnp.zeros(out_ref.shape, jnp.float32)
    squares_ref[...] = jnp.zeros(squares_ref.shape, jnp.float32)
    for slot in range(slots):
        place = pl.multiple_of(meta_ref[1 + slot] * block, block)
        live = meta_ref[1 + slots + slot].astype(jnp.float32)
        tile = tiles_ref[own, slot].astype(jnp.float32) * live
        out_ref[:, pl.ds(place, block)] += tile
        squares_ref[...] += tile * tile
    sums = jnp.sum(squares_ref[...], axis=1, keepdims=True)
    out_ref[:, total:] = jnp.broadcast_to(sums, (block, 128))


def partial_rows(tiles, meta, total_rows):
    block = tiles.shape[2]
    return pl.pallas_call(
        partial_kernel,
        out_shape=jax.ShapeDtypeStruct((block, total_rows + 128), jnp.float32),
        in_specs=[pl.BlockSpec(memory_space=pltpu.SMEM), pl.BlockSpec(memory_space=pltpu.VMEM)],
        out_specs=pl.BlockSpec(memory_space=pltpu.VMEM),
        scratch_shapes=[pltpu.VMEM((block, block), jnp.float32)],
    )(meta, tiles)


def distributed(start, tiles, pattern, counts):
    nb_dev = tiles.shape[0]
    block = tiles.shape[2]
    total_rows = nb_dev * block * lax.axis_size("row")
    vec_cols = start.shape[0]
    col_index = lax.axis_index("col")
    kb_dev = tiles.shape[1]
    slot_ids = col_index * kb_dev + jnp.arange(kb_dev, dtype=jnp.int32)
    live = (slot_ids[None, :] < counts[:, None]).astype(jnp.bfloat16)
    masked = tiles * live[:, :, None, None]
    local_pattern = lax.dynamic_slice_in_dim(pattern, col_index * kb_dev, kb_dev, 1)
    partial_squares = jnp.einsum(
        "bkmn,bkmn->bm", masked, masked, preferred_element_type=jnp.float32
    )
    square_sums = lax.psum(partial_squares, "col")
    scaling = row_scaling(square_sums, counts, block)

    def apply_slots(current):
        whole = lax.all_gather(current.astype(jnp.bfloat16), "row", axis=1, tiled=True)
        blocks = whole.reshape(vec_cols, -1, block)
        picked = jnp.take(blocks, local_pattern, axis=1)
        product = jnp.einsum("cbkn,bkmn->cbm", picked, masked, preferred_element_type=jnp.float32)
        total = lax.psum(product.astype(jnp.bfloat16), "col").astype(jnp.float32)
        return total.reshape(vec_cols, -1) * scaling

    current = start
    for outer in range(ITERS):
        filtered = chebyshev(current, apply_slots)
        current = orthonormal(filtered, total_rows)
    return current


def split_bf16(values):
    rounded = lax.reduce_precision(values, exponent_bits=8, mantissa_bits=7)
    return rounded.astype(jnp.bfloat16), (values - rounded).astype(jnp.bfloat16)


def replicated(start, tiles, pattern, counts):
    nb_dev, kb_dev, block = tiles.shape[0], tiles.shape[1], tiles.shape[2]
    n_row, n_col = lax.axis_size("row"), lax.axis_size("col")
    nblk = nb_dev * n_row
    total_rows = nblk * block
    share = block // n_col
    vec_cols = start.shape[0]
    cols = 2 * vec_cols
    row_index = lax.axis_index("row")
    col_index = lax.axis_index("col")
    vec_index = lax.axis_index("vec")

    own_pattern = lax.dynamic_slice_in_dim(
        lax.dynamic_index_in_dim(pattern, vec_index, 0, keepdims=False), col_index * kb_dev, kb_dev, 0
    )
    own_count = lax.dynamic_index_in_dim(counts, vec_index, 0, keepdims=False)
    slot_ids = col_index * kb_dev + jnp.arange(kb_dev, dtype=jnp.int32)
    live = (slot_ids < own_count).astype(jnp.int32)
    position = jnp.clip((own_pattern % nb_dev) * n_row + own_pattern // nb_dev, 0, nblk - 1)
    meta = jnp.concatenate([vec_index.astype(jnp.int32)[None], position, live])
    partial = partial_rows(tiles, meta, total_rows)
    chunks = partial.reshape(n_col, share, total_rows + 128)
    summed = lax.dynamic_index_in_dim(chunks, col_index, 0, keepdims=False)
    for shift in range(1, n_col):
        sent = lax.dynamic_index_in_dim(chunks, (col_index + shift) % n_col, 0, keepdims=False)
        summed = summed + lax.ppermute(sent, "col", [(i, (i + shift) % n_col) for i in range(n_col)])

    entries = (own_count * block).astype(jnp.float32)
    scale = lax.rsqrt(summed[:, total_rows] / entries + EPSILON) / jnp.sqrt(entries) / HALF_WIDTH

    piece = lax.dynamic_slice_in_dim(start, col_index * block, block, 1)
    start_hi, start_lo = split_bf16(piece)
    extra = jnp.concatenate([start_hi, start_lo], axis=0)
    rows_bf16 = (summed[:, :total_rows] * scale[:, None]).astype(jnp.bfloat16)

    packed = jnp.concatenate([rows_bf16, extra], axis=1)
    copies = jnp.broadcast_to(packed[None], (n_row * n_col,) + packed.shape)
    half = lax.all_to_all(copies, ("row", "col"), 0, 0, tiled=True)
    copies = jnp.broadcast_to(half[None], (2,) + half.shape)
    whole = lax.all_to_all(copies, "vec", 0, 0, tiled=True).reshape(total_rows, total_rows + block)
    index = jnp.stack([row_index, vec_index]).astype(jnp.int32)
    current = filter_local(whole, index, n_row, n_col, vec_cols)
    return current


def per_device(start, tiles, pattern, counts):
    total_rows = tiles.shape[0] * tiles.shape[2] * lax.axis_size("row")
    n_col, n_vec = lax.axis_size("col"), lax.axis_size("vec")
    block = tiles.shape[2]
    fits = (
        total_rows * total_rows * 2 <= DENSE_BUDGET
        and n_vec == 2
        and tiles.shape[0] == n_vec
        and block % n_col == 0
        and block // n_col == 2 * start.shape[0]
        and tiles.shape[0] == n_col
    )
    if fits:
        return replicated(start, tiles, pattern, counts)
    return distributed(start, tiles, pattern, counts)


def solution(mesh):
    in_specs = (
        P("vec", ("grp", "row")),
        P(("grp", "row"), "col", None, None),
        P(("grp", "row"), None),
        P(("grp", "row")),
    )
    out_specs = P("vec", ("grp", "row"))
    return jax.shard_map(
        per_device, mesh=mesh, in_specs=in_specs, out_specs=out_specs, check_vma=False
    )
```

```python
import functools

import jax
import jax.numpy as jnp
from jax import lax
from jax.experimental import pallas as pl
from jax.experimental.pallas import tpu as pltpu
from jax.sharding import PartitionSpec as P

DEGREE = 8
ITERS = 2


HALF_WIDTH = 2.0
EPSILON = 1e-06
DENSE_BUDGET = 16 * 1024 * 1024


def row_scaling(square_sums, live_counts, block):
    entries = (live_counts * block).astype(jnp.float32)[:, None]
    scaled = lax.rsqrt(square_sums / entries + EPSILON) / jnp.sqrt(entries)
    return (scaled / HALF_WIDTH).reshape(1, -1)


def chebyshev(first, apply):
    previous = first
    present = apply(first)
    for step in range(DEGREE - 1):
        previous, present = (present, 2.0 * apply(present) - previous)
    return present


def orthonormal(mine, total_rows):
    both = lax.all_gather(mine.astype(jnp.bfloat16), "vec", axis=0, tiled=True).astype(mine.dtype)
    part_gram = jnp.dot(both, both.T, precision=lax.Precision.HIGHEST)
    gram = lax.psum(part_gram, "row") / total_rows
    lower = jnp.linalg.cholesky(gram)
    solved = jax.scipy.linalg.solve_triangular(lower, both, lower=True)
    width = mine.shape[0]
    return lax.dynamic_slice_in_dim(solved, lax.axis_index("vec") * width, width, 0)


def orthonormal_value(y):
    n, total = y.shape
    hi = lax.Precision.HIGHEST
    a = lax.dot_general(y, y, (((1,), (1,)), ((), ())), precision=hi, preferred_element_type=jnp.float32)
    a = a / total
    rows = lax.broadcasted_iota(jnp.int32, (n, n), 0)
    cols = lax.broadcasted_iota(jnp.int32, (n, n), 1)
    inverse = (rows == cols).astype(jnp.float32)
    diagonal = jnp.zeros((n, 1), jnp.float32)
    for k in range(n):
        top = (k // 8) * 8
        pivot = a[k : k + 1, k : k + 1]
        down = jnp.where(rows[top:, k : k + 1] > k, a[top:, k : k + 1] * (1.0 / pivot), 0.0)
        across = jnp.where(cols[k : k + 1, :] > k, a[k : k + 1, :], 0.0)
        lower_a = a[top:] - down * across
        lower_inverse = inverse[top:] - down * inverse[k : k + 1, :]
        if top:
            a = jnp.concatenate([a[:top], lower_a], axis=0)
            inverse = jnp.concatenate([inverse[:top], lower_inverse], axis=0)
        else:
            a, inverse = lower_a, lower_inverse
        diagonal = jnp.where(rows[:, :1] == k, pivot, diagonal)
    inverse = inverse / jnp.sqrt(diagonal)
    return lax.dot_general(
        inverse, y, (((1,), (0,)), ((), ())), precision=hi, preferred_element_type=jnp.float32
    )


def filter_kernel(index_ref, own_ref, other_ref, x_ref, whole_ref, *, n_row, n_col, vec_cols):
    half_rows = own_ref.shape[0]
    total = 2 * half_rows
    block = own_ref.shape[1] - total
    nb_dev = total // (block * n_row)
    share = 2 * vec_cols
    row = index_ref[0]
    core = index_ref[1]
    own_first = pl.multiple_of(core * vec_cols, 8)
    other_first = pl.multiple_of((1 - core) * vec_cols, 8)
    own_place = pl.multiple_of(core * half_rows, 128)
    other_place = pl.multiple_of((1 - core) * half_rows, 128)

    def decode(ref):
        parts = []
        for place in range(total // block):
            local, src_row = divmod(place, n_row)
            base = (src_row * n_col + local) * share
            high = ref[base : base + vec_cols, total:].astype(jnp.float32)
            low = ref[base + vec_cols : base + share, total:].astype(jnp.float32)
            parts.append(high + low)
        return jnp.concatenate(parts, axis=1)

    whole_ref[pl.ds(own_first, vec_cols), :] = decode(own_ref)
    whole_ref[pl.ds(other_first, vec_cols), :] = decode(other_ref)
    current = whole_ref[...]

    def apply(values):
        rounded = values.astype(jnp.bfloat16)
        dims = (((1,), (1,)), ((), ()))
        whole_ref[:, pl.ds(own_place, half_rows)] = lax.dot_general(
            rounded, own_ref[:, :total], dims, preferred_element_type=jnp.float32
        )
        whole_ref[:, pl.ds(other_place, half_rows)] = lax.dot_general(
            rounded, other_ref[:, :total], dims, preferred_element_type=jnp.float32
        )
        return whole_ref[...]

    for outer in range(ITERS):
        current = orthonormal_value(chebyshev(current, apply))
    whole_ref[...] = current
    for local in range(nb_dev):
        place = pl.multiple_of((local * n_row + row) * block, 128)
        x_ref[:, local * block : (local + 1) * block] = whole_ref[pl.ds(own_first, vec_cols), pl.ds(place, block)]


def filter_local(own, other, index, n_row, n_col, vec_cols):
    total = 2 * own.shape[0]
    block = own.shape[1] - total
    nb_dev = total // (block * n_row)
    return pl.pallas_call(
        functools.partial(filter_kernel, n_row=n_row, n_col=n_col, vec_cols=vec_cols),
        out_shape=jax.ShapeDtypeStruct((vec_cols, nb_dev * block), jnp.float32),
        in_specs=[pl.BlockSpec(memory_space=pltpu.SMEM)] + [pl.BlockSpec(memory_space=pltpu.VMEM)] * 2,
        out_specs=pl.BlockSpec(memory_space=pltpu.VMEM),
        scratch_shapes=[pltpu.VMEM((2 * vec_cols, total), jnp.float32)],
    )(index, own, other)

def distributed(start, tiles, pattern, counts):
    nb_dev = tiles.shape[0]
    block = tiles.shape[2]
    total_rows = nb_dev * block * lax.axis_size("row")
    vec_cols = start.shape[0]
    col_index = lax.axis_index("col")
    kb_dev = tiles.shape[1]
    slot_ids = col_index * kb_dev + jnp.arange(kb_dev, dtype=jnp.int32)
    live = (slot_ids[None, :] < counts[:, None]).astype(jnp.bfloat16)
    masked = tiles * live[:, :, None, None]
    local_pattern = lax.dynamic_slice_in_dim(pattern, col_index * kb_dev, kb_dev, 1)
    partial_squares = jnp.einsum(
        "bkmn,bkmn->bm", masked, masked, preferred_element_type=jnp.float32
    )
    square_sums = lax.psum(partial_squares, "col")
    scaling = row_scaling(square_sums, counts, block)

    def apply_slots(current):
        whole = lax.all_gather(current.astype(jnp.bfloat16), "row", axis=1, tiled=True)
        blocks = whole.reshape(vec_cols, -1, block)
        picked = jnp.take(blocks, local_pattern, axis=1)
        product = jnp.einsum("cbkn,bkmn->cbm", picked, masked, preferred_element_type=jnp.float32)
        total = lax.psum(product.astype(jnp.bfloat16), "col").astype(jnp.float32)
        return total.reshape(vec_cols, -1) * scaling

    current = start
    for outer in range(ITERS):
        filtered = chebyshev(current, apply_slots)
        current = orthonormal(filtered, total_rows)
    return current


def split_bf16(values):
    rounded = lax.reduce_precision(values, exponent_bits=8, mantissa_bits=7)
    return rounded.astype(jnp.bfloat16), (values - rounded).astype(jnp.bfloat16)


def replicated(start, tiles, pattern, counts):
    nb_dev, kb_dev, block = tiles.shape[0], tiles.shape[1], tiles.shape[2]
    n_row, n_col = lax.axis_size("row"), lax.axis_size("col")
    nblk = nb_dev * n_row
    total_rows = nblk * block
    share = block // n_col
    vec_cols = start.shape[0]
    cols = 2 * vec_cols
    row_index = lax.axis_index("row")
    col_index = lax.axis_index("col")
    vec_index = lax.axis_index("vec")

    own_tiles = lax.dynamic_index_in_dim(tiles, vec_index, 0, keepdims=False)
    own_pattern = lax.dynamic_slice_in_dim(
        lax.dynamic_index_in_dim(pattern, vec_index, 0, keepdims=False), col_index * kb_dev, kb_dev, 0
    )
    own_count = lax.dynamic_index_in_dim(counts, vec_index, 0, keepdims=False)
    slot_ids = col_index * kb_dev + jnp.arange(kb_dev, dtype=jnp.int32)
    live = slot_ids < own_count
    position = (own_pattern % nb_dev) * n_row + own_pattern // nb_dev
    onehot = (position[:, None] == jnp.arange(nblk, dtype=jnp.int32)) & live[:, None]
    dense = jnp.einsum(
        "kj,kmn->mjn", onehot.astype(jnp.bfloat16), own_tiles, preferred_element_type=jnp.float32
    ).reshape(block, total_rows)
    masked = own_tiles * live.astype(jnp.bfloat16)[:, None, None]
    squares = jnp.einsum("kmn,kmn->m", masked, masked, preferred_element_type=jnp.float32)
    squares = jnp.broadcast_to(squares[:, None], (block, 128))
    partial = jnp.concatenate([dense, squares], axis=1)
    chunks = partial.reshape(n_col, share, total_rows + 128)
    summed = lax.dynamic_index_in_dim(chunks, col_index, 0, keepdims=False)
    for shift in range(1, n_col):
        sent = lax.dynamic_index_in_dim(chunks, (col_index + shift) % n_col, 0, keepdims=False)
        summed = summed + lax.ppermute(sent, "col", [(i, (i + shift) % n_col) for i in range(n_col)])

    entries = (own_count * block).astype(jnp.float32)
    scale = lax.rsqrt(summed[:, total_rows] / entries + EPSILON) / jnp.sqrt(entries) / HALF_WIDTH

    piece = lax.dynamic_slice_in_dim(start, col_index * block, block, 1)
    start_hi, start_lo = split_bf16(piece)
    extra = jnp.concatenate([start_hi, start_lo], axis=0)
    rows_bf16 = (summed[:, :total_rows] * scale[:, None]).astype(jnp.bfloat16)

    packed = jnp.concatenate([rows_bf16, extra], axis=1)
    copies = jnp.broadcast_to(packed[None], (n_row * n_col,) + packed.shape)
    half = lax.all_to_all(copies, ("row", "col"), 0, 0, tiled=True)
    half = half.reshape(n_row * n_col * share, total_rows + block)
    other = lax.ppermute(half, "vec", [(0, 1), (1, 0)])
    index = jnp.stack([row_index, vec_index]).astype(jnp.int32)
    current = filter_local(half, other, index, n_row, n_col, vec_cols)
    return current


def per_device(start, tiles, pattern, counts):
    total_rows = tiles.shape[0] * tiles.shape[2] * lax.axis_size("row")
    n_col, n_vec = lax.axis_size("col"), lax.axis_size("vec")
    block = tiles.shape[2]
    fits = (
        total_rows * total_rows * 2 <= DENSE_BUDGET
        and n_vec == 2
        and tiles.shape[0] == n_vec
        and block % n_col == 0
        and block // n_col == 2 * start.shape[0]
        and tiles.shape[0] == n_col
    )
    if fits:
        return replicated(start, tiles, pattern, counts)
    return distributed(start, tiles, pattern, counts)


def solution(mesh):
    in_specs = (
        P("vec", ("grp", "row")),
        P(("grp", "row"), "col", None, None),
        P(("grp", "row"), None),
        P(("grp", "row")),
    )
    out_specs = P("vec", ("grp", "row"))
    return jax.shard_map(
        per_device, mesh=mesh, in_specs=in_specs, out_specs=out_specs, check_vma=False
    )
```

```python
import functools

import jax
import jax.numpy as jnp
from jax import lax
from jax.experimental import pallas as pl
from jax.experimental.pallas import tpu as pltpu
from jax.sharding import PartitionSpec as P

DEGREE = 8
ITERS = 2


HALF_WIDTH = 2.0
EPSILON = 1e-06
DENSE_BUDGET = 16 * 1024 * 1024


def row_scaling(square_sums, live_counts, block):
    entries = (live_counts * block).astype(jnp.float32)[:, None]
    scaled = lax.rsqrt(square_sums / entries + EPSILON) / jnp.sqrt(entries)
    return (scaled / HALF_WIDTH).reshape(1, -1)


def chebyshev(first, apply):
    previous = first
    present = apply(first)
    for step in range(DEGREE - 1):
        previous, present = (present, 2.0 * apply(present) - previous)
    return present


def orthonormal(mine, total_rows):
    both = lax.all_gather(mine.astype(jnp.bfloat16), "vec", axis=0, tiled=True).astype(mine.dtype)
    part_gram = jnp.dot(both, both.T, precision=lax.Precision.HIGHEST)
    gram = lax.psum(part_gram, "row") / total_rows
    lower = jnp.linalg.cholesky(gram)
    solved = jax.scipy.linalg.solve_triangular(lower, both, lower=True)
    width = mine.shape[0]
    return lax.dynamic_slice_in_dim(solved, lax.axis_index("vec") * width, width, 0)


def orthonormal_value(y):
    n, total = y.shape
    hi = lax.Precision.HIGHEST
    a = lax.dot_general(y, y, (((1,), (1,)), ((), ())), precision=hi, preferred_element_type=jnp.float32)
    a = a / total
    rows = lax.broadcasted_iota(jnp.int32, (n, n), 0)
    cols = lax.broadcasted_iota(jnp.int32, (n, n), 1)
    inverse = (rows == cols).astype(jnp.float32)
    diagonal = jnp.zeros((n, 1), jnp.float32)
    for k in range(n):
        top = (k // 8) * 8
        pivot = a[k : k + 1, k : k + 1]
        down = jnp.where(rows[top:, k : k + 1] > k, a[top:, k : k + 1] * (1.0 / pivot), 0.0)
        across = jnp.where(cols[k : k + 1, :] > k, a[k : k + 1, :], 0.0)
        lower_a = a[top:] - down * across
        lower_inverse = inverse[top:] - down * inverse[k : k + 1, :]
        if top:
            a = jnp.concatenate([a[:top], lower_a], axis=0)
            inverse = jnp.concatenate([inverse[:top], lower_inverse], axis=0)
        else:
            a, inverse = lower_a, lower_inverse
        diagonal = jnp.where(rows[:, :1] == k, pivot, diagonal)
    inverse = inverse / jnp.sqrt(diagonal)
    return lax.dot_general(
        inverse, y, (((1,), (0,)), ((), ())), precision=hi, preferred_element_type=jnp.float32
    )


def filter_kernel(index_ref, own_ref, other_ref, x_ref, whole_ref, w_ref, *, n_row, n_col, vec_cols):
    half_rows = own_ref.shape[0]
    total = 2 * half_rows
    block = own_ref.shape[1] - total
    nb_dev = total // (block * n_row)
    share = 2 * vec_cols
    row = index_ref[0]
    core = index_ref[1]
    own_first = pl.multiple_of(core * vec_cols, 8)
    other_first = pl.multiple_of((1 - core) * vec_cols, 8)
    own_place = pl.multiple_of(core * half_rows, 128)
    other_place = pl.multiple_of((1 - core) * half_rows, 128)

    def decode(ref):
        parts = []
        for place in range(total // block):
            local, src_row = divmod(place, n_row)
            base = (src_row * n_col + local) * share
            high = ref[base : base + vec_cols, total:].astype(jnp.float32)
            low = ref[base + vec_cols : base + share, total:].astype(jnp.float32)
            parts.append(high + low)
        return jnp.concatenate(parts, axis=1)

    whole_ref[pl.ds(own_first, vec_cols), :] = decode(own_ref)
    whole_ref[pl.ds(other_first, vec_cols), :] = decode(other_ref)
    w_ref[:half_rows, :half_rows] = own_ref[:, pl.ds(own_place, half_rows)]
    w_ref[:half_rows, half_rows:] = own_ref[:, pl.ds(other_place, half_rows)]
    w_ref[half_rows:, :half_rows] = other_ref[:, pl.ds(own_place, half_rows)]
    w_ref[half_rows:, half_rows:] = other_ref[:, pl.ds(other_place, half_rows)]
    current = jnp.concatenate(
        [whole_ref[:, pl.ds(own_place, half_rows)], whole_ref[:, pl.ds(other_place, half_rows)]], axis=1
    )

    def apply(values):
        return lax.dot_general(
            values.astype(jnp.bfloat16),
            w_ref[...],
            (((1,), (1,)), ((), ())),
            preferred_element_type=jnp.float32,
        )

    for outer in range(ITERS):
        current = orthonormal_value(chebyshev(current, apply))
    whole_ref[...] = current
    for local in range(nb_dev):
        place = pl.multiple_of((((local + core) % 2) * n_row + row) * block, 128)
        x_ref[:, local * block : (local + 1) * block] = whole_ref[pl.ds(own_first, vec_cols), pl.ds(place, block)]

def filter_local(own, other, index, n_row, n_col, vec_cols):
    total = 2 * own.shape[0]
    block = own.shape[1] - total
    nb_dev = total // (block * n_row)
    return pl.pallas_call(
        functools.partial(filter_kernel, n_row=n_row, n_col=n_col, vec_cols=vec_cols),
        out_shape=jax.ShapeDtypeStruct((vec_cols, nb_dev * block), jnp.float32),
        in_specs=[pl.BlockSpec(memory_space=pltpu.SMEM)] + [pl.BlockSpec(memory_space=pltpu.VMEM)] * 2,
        out_specs=pl.BlockSpec(memory_space=pltpu.VMEM),
        scratch_shapes=[
            pltpu.VMEM((2 * vec_cols, total), jnp.float32),
            pltpu.VMEM((total, total), jnp.bfloat16),
        ],
    )(index, own, other)

def distributed(start, tiles, pattern, counts):
    nb_dev = tiles.shape[0]
    block = tiles.shape[2]
    total_rows = nb_dev * block * lax.axis_size("row")
    vec_cols = start.shape[0]
    col_index = lax.axis_index("col")
    kb_dev = tiles.shape[1]
    slot_ids = col_index * kb_dev + jnp.arange(kb_dev, dtype=jnp.int32)
    live = (slot_ids[None, :] < counts[:, None]).astype(jnp.bfloat16)
    masked = tiles * live[:, :, None, None]
    local_pattern = lax.dynamic_slice_in_dim(pattern, col_index * kb_dev, kb_dev, 1)
    partial_squares = jnp.einsum(
        "bkmn,bkmn->bm", masked, masked, preferred_element_type=jnp.float32
    )
    square_sums = lax.psum(partial_squares, "col")
    scaling = row_scaling(square_sums, counts, block)

    def apply_slots(current):
        whole = lax.all_gather(current.astype(jnp.bfloat16), "row", axis=1, tiled=True)
        blocks = whole.reshape(vec_cols, -1, block)
        picked = jnp.take(blocks, local_pattern, axis=1)
        product = jnp.einsum("cbkn,bkmn->cbm", picked, masked, preferred_element_type=jnp.float32)
        total = lax.psum(product.astype(jnp.bfloat16), "col").astype(jnp.float32)
        return total.reshape(vec_cols, -1) * scaling

    current = start
    for outer in range(ITERS):
        filtered = chebyshev(current, apply_slots)
        current = orthonormal(filtered, total_rows)
    return current


def split_bf16(values):
    rounded = lax.reduce_precision(values, exponent_bits=8, mantissa_bits=7)
    return rounded.astype(jnp.bfloat16), (values - rounded).astype(jnp.bfloat16)


def replicated(start, tiles, pattern, counts):
    nb_dev, kb_dev, block = tiles.shape[0], tiles.shape[1], tiles.shape[2]
    n_row, n_col = lax.axis_size("row"), lax.axis_size("col")
    nblk = nb_dev * n_row
    total_rows = nblk * block
    share = block // n_col
    vec_cols = start.shape[0]
    cols = 2 * vec_cols
    row_index = lax.axis_index("row")
    col_index = lax.axis_index("col")
    vec_index = lax.axis_index("vec")

    own_tiles = lax.dynamic_index_in_dim(tiles, vec_index, 0, keepdims=False)
    own_pattern = lax.dynamic_slice_in_dim(
        lax.dynamic_index_in_dim(pattern, vec_index, 0, keepdims=False), col_index * kb_dev, kb_dev, 0
    )
    own_count = lax.dynamic_index_in_dim(counts, vec_index, 0, keepdims=False)
    slot_ids = col_index * kb_dev + jnp.arange(kb_dev, dtype=jnp.int32)
    live = slot_ids < own_count
    position = (own_pattern % nb_dev) * n_row + own_pattern // nb_dev
    onehot = (position[:, None] == jnp.arange(nblk, dtype=jnp.int32)) & live[:, None]
    dense = jnp.einsum(
        "kj,kmn->mjn", onehot.astype(jnp.bfloat16), own_tiles, preferred_element_type=jnp.float32
    ).reshape(block, total_rows)
    masked = own_tiles * live.astype(jnp.bfloat16)[:, None, None]
    squares = jnp.einsum("kmn,kmn->m", masked, masked, preferred_element_type=jnp.float32)
    squares = jnp.broadcast_to(squares[:, None], (block, 128))
    partial = jnp.concatenate([dense, squares], axis=1)
    chunks = partial.reshape(n_col, share, total_rows + 128)
    summed = lax.dynamic_index_in_dim(chunks, col_index, 0, keepdims=False)
    for shift in range(1, n_col):
        sent = lax.dynamic_index_in_dim(chunks, (col_index + shift) % n_col, 0, keepdims=False)
        summed = summed + lax.ppermute(sent, "col", [(i, (i + shift) % n_col) for i in range(n_col)])

    entries = (own_count * block).astype(jnp.float32)
    scale = lax.rsqrt(summed[:, total_rows] / entries + EPSILON) / jnp.sqrt(entries) / HALF_WIDTH

    piece = lax.dynamic_slice_in_dim(start, col_index * block, block, 1)
    start_hi, start_lo = split_bf16(piece)
    extra = jnp.concatenate([start_hi, start_lo], axis=0)
    rows_bf16 = (summed[:, :total_rows] * scale[:, None]).astype(jnp.bfloat16)

    packed = jnp.concatenate([rows_bf16, extra], axis=1)
    copies = jnp.broadcast_to(packed[None], (n_row * n_col,) + packed.shape)
    half = lax.all_to_all(copies, ("row", "col"), 0, 0, tiled=True)
    half = half.reshape(n_row * n_col * share, total_rows + block)
    other = lax.ppermute(half, "vec", [(0, 1), (1, 0)])
    index = jnp.stack([row_index, vec_index]).astype(jnp.int32)
    current = filter_local(half, other, index, n_row, n_col, vec_cols)
    return current


def per_device(start, tiles, pattern, counts):
    total_rows = tiles.shape[0] * tiles.shape[2] * lax.axis_size("row")
    n_col, n_vec = lax.axis_size("col"), lax.axis_size("vec")
    block = tiles.shape[2]
    fits = (
        total_rows * total_rows * 2 <= DENSE_BUDGET
        and n_vec == 2
        and tiles.shape[0] == n_vec
        and block % n_col == 0
        and block // n_col == 2 * start.shape[0]
        and tiles.shape[0] == n_col
    )
    if fits:
        return replicated(start, tiles, pattern, counts)
    return distributed(start, tiles, pattern, counts)


def solution(mesh):
    in_specs = (
        P("vec", ("grp", "row")),
        P(("grp", "row"), "col", None, None),
        P(("grp", "row"), None),
        P(("grp", "row")),
    )
    out_specs = P("vec", ("grp", "row"))
    return jax.shard_map(
        per_device, mesh=mesh, in_specs=in_specs, out_specs=out_specs, check_vma=False
    )
```

```python
import functools

import jax
import jax.numpy as jnp
from jax import lax
from jax.experimental import pallas as pl
from jax.experimental.pallas import tpu as pltpu
from jax.sharding import PartitionSpec as P

DEGREE = 8
ITERS = 2


HALF_WIDTH = 2.0
EPSILON = 1e-06
DENSE_BUDGET = 16 * 1024 * 1024


def row_scaling(square_sums, live_counts, block):
    entries = (live_counts * block).astype(jnp.float32)[:, None]
    scaled = lax.rsqrt(square_sums / entries + EPSILON) / jnp.sqrt(entries)
    return (scaled / HALF_WIDTH).reshape(1, -1)


def chebyshev(first, apply):
    previous = first
    present = apply(first)
    for step in range(DEGREE - 1):
        previous, present = (present, 2.0 * apply(present) - previous)
    return present


def orthonormal(mine, total_rows):
    both = lax.all_gather(mine.astype(jnp.bfloat16), "vec", axis=0, tiled=True).astype(mine.dtype)
    part_gram = jnp.dot(both, both.T, precision=lax.Precision.HIGHEST)
    gram = lax.psum(part_gram, "row") / total_rows
    lower = jnp.linalg.cholesky(gram)
    solved = jax.scipy.linalg.solve_triangular(lower, both, lower=True)
    width = mine.shape[0]
    return lax.dynamic_slice_in_dim(solved, lax.axis_index("vec") * width, width, 0)


def orthonormal_value(y):
    n, total = y.shape
    hi = lax.Precision.HIGHEST
    a = lax.dot_general(y, y, (((1,), (1,)), ((), ())), precision=hi, preferred_element_type=jnp.float32)
    a = a / total
    rows = lax.broadcasted_iota(jnp.int32, (n, n), 0)
    cols = lax.broadcasted_iota(jnp.int32, (n, n), 1)
    inverse = (rows == cols).astype(jnp.float32)
    diagonal = jnp.zeros((n, 1), jnp.float32)
    for k in range(n):
        top = (k // 8) * 8
        pivot = a[k : k + 1, k : k + 1]
        down = jnp.where(rows[top:, k : k + 1] > k, a[top:, k : k + 1] * (1.0 / pivot), 0.0)
        across = jnp.where(cols[k : k + 1, :] > k, a[k : k + 1, :], 0.0)
        lower_a = a[top:] - down * across
        lower_inverse = inverse[top:] - down * inverse[k : k + 1, :]
        if top:
            a = jnp.concatenate([a[:top], lower_a], axis=0)
            inverse = jnp.concatenate([inverse[:top], lower_inverse], axis=0)
        else:
            a, inverse = lower_a, lower_inverse
        diagonal = jnp.where(rows[:, :1] == k, pivot, diagonal)
    inverse = inverse / jnp.sqrt(diagonal)
    return lax.dot_general(
        inverse, y, (((1,), (0,)), ((), ())), precision=hi, preferred_element_type=jnp.float32
    )


def filter_kernel(own_ref, other_ref, x_ref, whole_ref, w_ref, *, n_row, n_col, vec_cols):
    half_rows = own_ref.shape[0]
    total = 2 * half_rows
    block = own_ref.shape[1] - total
    nb_dev = total // (block * n_row)
    share = 2 * vec_cols
    row = lax.axis_index("row")
    core = lax.axis_index("vec")
    own_first = pl.multiple_of(core * vec_cols, 8)
    other_first = pl.multiple_of((1 - core) * vec_cols, 8)
    own_place = pl.multiple_of(core * half_rows, 128)
    other_place = pl.multiple_of((1 - core) * half_rows, 128)

    def decode(ref):
        parts = []
        for place in range(total // block):
            local, src_row = divmod(place, n_row)
            base = (src_row * n_col + local) * share
            high = ref[base : base + vec_cols, total:].astype(jnp.float32)
            low = ref[base + vec_cols : base + share, total:].astype(jnp.float32)
            parts.append(high + low)
        return jnp.concatenate(parts, axis=1)

    whole_ref[pl.ds(own_first, vec_cols), :] = decode(own_ref)
    whole_ref[pl.ds(other_first, vec_cols), :] = decode(other_ref)
    w_ref[:half_rows, :half_rows] = own_ref[:, pl.ds(own_place, half_rows)]
    w_ref[:half_rows, half_rows:] = own_ref[:, pl.ds(other_place, half_rows)]
    w_ref[half_rows:, :half_rows] = other_ref[:, pl.ds(own_place, half_rows)]
    w_ref[half_rows:, half_rows:] = other_ref[:, pl.ds(other_place, half_rows)]
    current = jnp.concatenate(
        [whole_ref[:, pl.ds(own_place, half_rows)], whole_ref[:, pl.ds(other_place, half_rows)]], axis=1
    )

    def apply(values):
        return lax.dot_general(
            values.astype(jnp.bfloat16),
            w_ref[...],
            (((1,), (1,)), ((), ())),
            preferred_element_type=jnp.float32,
        )

    for outer in range(ITERS):
        current = orthonormal_value(chebyshev(current, apply))
    whole_ref[...] = current
    for local in range(nb_dev):
        place = pl.multiple_of((((local + core) % 2) * n_row + row) * block, 128)
        x_ref[:, local * block : (local + 1) * block] = whole_ref[pl.ds(own_first, vec_cols), pl.ds(place, block)]

def filter_local(own, other, n_row, n_col, vec_cols):
    total = 2 * own.shape[0]
    block = own.shape[1] - total
    nb_dev = total // (block * n_row)
    return pl.pallas_call(
        functools.partial(filter_kernel, n_row=n_row, n_col=n_col, vec_cols=vec_cols),
        out_shape=jax.ShapeDtypeStruct((vec_cols, nb_dev * block), jnp.float32),
        in_specs=[pl.BlockSpec(memory_space=pltpu.VMEM)] * 2,
        out_specs=pl.BlockSpec(memory_space=pltpu.VMEM),
        scratch_shapes=[
            pltpu.VMEM((2 * vec_cols, total), jnp.float32),
            pltpu.VMEM((total, total), jnp.bfloat16),
        ],
    )(own, other)

def distributed(start, tiles, pattern, counts):
    nb_dev = tiles.shape[0]
    block = tiles.shape[2]
    total_rows = nb_dev * block * lax.axis_size("row")
    vec_cols = start.shape[0]
    col_index = lax.axis_index("col")
    kb_dev = tiles.shape[1]
    slot_ids = col_index * kb_dev + jnp.arange(kb_dev, dtype=jnp.int32)
    live = (slot_ids[None, :] < counts[:, None]).astype(jnp.bfloat16)
    masked = tiles * live[:, :, None, None]
    local_pattern = lax.dynamic_slice_in_dim(pattern, col_index * kb_dev, kb_dev, 1)
    partial_squares = jnp.einsum(
        "bkmn,bkmn->bm", masked, masked, preferred_element_type=jnp.float32
    )
    square_sums = lax.psum(partial_squares, "col")
    scaling = row_scaling(square_sums, counts, block)

    def apply_slots(current):
        whole = lax.all_gather(current.astype(jnp.bfloat16), "row", axis=1, tiled=True)
        blocks = whole.reshape(vec_cols, -1, block)
        picked = jnp.take(blocks, local_pattern, axis=1)
        product = jnp.einsum("cbkn,bkmn->cbm", picked, masked, preferred_element_type=jnp.float32)
        total = lax.psum(product.astype(jnp.bfloat16), "col").astype(jnp.float32)
        return total.reshape(vec_cols, -1) * scaling

    current = start
    for outer in range(ITERS):
        filtered = chebyshev(current, apply_slots)
        current = orthonormal(filtered, total_rows)
    return current


def split_bf16(values):
    rounded = lax.reduce_precision(values, exponent_bits=8, mantissa_bits=7)
    return rounded.astype(jnp.bfloat16), (values - rounded).astype(jnp.bfloat16)


def replicated(start, tiles, pattern, counts):
    nb_dev, kb_dev, block = tiles.shape[0], tiles.shape[1], tiles.shape[2]
    n_row, n_col = lax.axis_size("row"), lax.axis_size("col")
    nblk = nb_dev * n_row
    total_rows = nblk * block
    share = block // n_col
    vec_cols = start.shape[0]
    cols = 2 * vec_cols
    row_index = lax.axis_index("row")
    col_index = lax.axis_index("col")
    vec_index = lax.axis_index("vec")

    own_tiles = lax.dynamic_index_in_dim(tiles, vec_index, 0, keepdims=False)
    own_pattern = lax.dynamic_slice_in_dim(
        lax.dynamic_index_in_dim(pattern, vec_index, 0, keepdims=False), col_index * kb_dev, kb_dev, 0
    )
    own_count = lax.dynamic_index_in_dim(counts, vec_index, 0, keepdims=False)
    slot_ids = col_index * kb_dev + jnp.arange(kb_dev, dtype=jnp.int32)
    live = slot_ids < own_count
    position = (own_pattern % nb_dev) * n_row + own_pattern // nb_dev
    onehot = (position[:, None] == jnp.arange(nblk, dtype=jnp.int32)) & live[:, None]
    dense = jnp.einsum(
        "kj,kmn->mjn", onehot.astype(jnp.bfloat16), own_tiles, preferred_element_type=jnp.float32
    ).reshape(block, total_rows)
    masked = own_tiles * live.astype(jnp.bfloat16)[:, None, None]
    squares = jnp.einsum("kmn,kmn->m", masked, masked, preferred_element_type=jnp.float32)
    squares = jnp.broadcast_to(squares[:, None], (block, 128))
    partial = jnp.concatenate([dense, squares], axis=1)
    chunks = partial.reshape(n_col, share, total_rows + 128)
    summed = lax.dynamic_index_in_dim(chunks, col_index, 0, keepdims=False)
    for shift in range(1, n_col):
        sent = lax.dynamic_index_in_dim(chunks, (col_index + shift) % n_col, 0, keepdims=False)
        summed = summed + lax.ppermute(sent, "col", [(i, (i + shift) % n_col) for i in range(n_col)])

    entries = (own_count * block).astype(jnp.float32)
    scale = lax.rsqrt(summed[:, total_rows] / entries + EPSILON) / jnp.sqrt(entries) / HALF_WIDTH

    piece = lax.dynamic_slice_in_dim(start, col_index * block, block, 1)
    start_hi, start_lo = split_bf16(piece)
    extra = jnp.concatenate([start_hi, start_lo], axis=0)
    rows_bf16 = (summed[:, :total_rows] * scale[:, None]).astype(jnp.bfloat16)

    packed = jnp.concatenate([rows_bf16, extra], axis=1)
    copies = jnp.broadcast_to(packed[None], (n_row * n_col,) + packed.shape)
    half = lax.all_to_all(copies, ("row", "col"), 0, 0, tiled=True)
    half = half.reshape(n_row * n_col * share, total_rows + block)
    other = lax.ppermute(half, "vec", [(0, 1), (1, 0)])
    current = filter_local(half, other, n_row, n_col, vec_cols)
    return current


def per_device(start, tiles, pattern, counts):
    total_rows = tiles.shape[0] * tiles.shape[2] * lax.axis_size("row")
    n_col, n_vec = lax.axis_size("col"), lax.axis_size("vec")
    block = tiles.shape[2]
    fits = (
        total_rows * total_rows * 2 <= DENSE_BUDGET
        and n_vec == 2
        and tiles.shape[0] == n_vec
        and block % n_col == 0
        and block // n_col == 2 * start.shape[0]
        and tiles.shape[0] == n_col
    )
    if fits:
        return replicated(start, tiles, pattern, counts)
    return distributed(start, tiles, pattern, counts)


def solution(mesh):
    in_specs = (
        P("vec", ("grp", "row")),
        P(("grp", "row"), "col", None, None),
        P(("grp", "row"), None),
        P(("grp", "row")),
    )
    out_specs = P("vec", ("grp", "row"))
    return jax.shard_map(
        per_device, mesh=mesh, in_specs=in_specs, out_specs=out_specs, check_vma=False
    )
```

```python
import functools

import jax
import jax.numpy as jnp
from jax import lax
from jax.experimental import pallas as pl
from jax.experimental.pallas import tpu as pltpu
from jax.sharding import PartitionSpec as P

DEGREE = 8
ITERS = 2


HALF_WIDTH = 2.0
EPSILON = 1e-06
DENSE_BUDGET = 16 * 1024 * 1024


def row_scaling(square_sums, live_counts, block):
    entries = (live_counts * block).astype(jnp.float32)[:, None]
    scaled = lax.rsqrt(square_sums / entries + EPSILON) / jnp.sqrt(entries)
    return (scaled / HALF_WIDTH).reshape(1, -1)


def chebyshev(first, apply):
    previous = first
    present = apply(first)
    for step in range(DEGREE - 1):
        previous, present = (present, 2.0 * apply(present) - previous)
    return present


def orthonormal(mine, total_rows):
    both = lax.all_gather(mine.astype(jnp.bfloat16), "vec", axis=0, tiled=True).astype(mine.dtype)
    part_gram = jnp.dot(both, both.T, precision=lax.Precision.HIGHEST)
    gram = lax.psum(part_gram, "row") / total_rows
    lower = jnp.linalg.cholesky(gram)
    solved = jax.scipy.linalg.solve_triangular(lower, both, lower=True)
    width = mine.shape[0]
    return lax.dynamic_slice_in_dim(solved, lax.axis_index("vec") * width, width, 0)


def orthonormal_value(y):
    n, total = y.shape
    hi = lax.Precision.HIGHEST
    a = lax.dot_general(y, y, (((1,), (1,)), ((), ())), precision=hi, preferred_element_type=jnp.float32)
    a = a / total
    rows = lax.broadcasted_iota(jnp.int32, (n, n), 0)
    cols = lax.broadcasted_iota(jnp.int32, (n, n), 1)
    inverse = (rows == cols).astype(jnp.float32)
    diagonal = jnp.zeros((n, 1), jnp.float32)
    for k in range(n):
        top = (k // 8) * 8
        pivot = a[k : k + 1, k : k + 1]
        down = jnp.where(rows[top:, k : k + 1] > k, a[top:, k : k + 1] * (1.0 / pivot), 0.0)
        across = jnp.where(cols[k : k + 1, :] > k, a[k : k + 1, :], 0.0)
        lower_a = a[top:] - down * across
        lower_inverse = inverse[top:] - down * inverse[k : k + 1, :]
        if top:
            a = jnp.concatenate([a[:top], lower_a], axis=0)
            inverse = jnp.concatenate([inverse[:top], lower_inverse], axis=0)
        else:
            a, inverse = lower_a, lower_inverse
        diagonal = jnp.where(rows[:, :1] == k, pivot, diagonal)
    inverse = inverse / jnp.sqrt(diagonal)
    return lax.dot_general(
        inverse, y, (((1,), (0,)), ((), ())), precision=hi, preferred_element_type=jnp.float32
    )


def filter_kernel(own_ref, other_ref, x_ref, whole_ref, w_ref, *, n_row, n_col, vec_cols):
    half_rows = own_ref.shape[0]
    total = 2 * half_rows
    block = own_ref.shape[1] - total
    nb_dev = total // (block * n_row)
    share = 2 * vec_cols
    row = lax.axis_index("row")
    core = lax.axis_index("vec")
    own_first = pl.multiple_of(core * vec_cols, 8)
    other_first = pl.multiple_of((1 - core) * vec_cols, 8)
    own_place = pl.multiple_of(core * half_rows, 128)
    other_place = pl.multiple_of((1 - core) * half_rows, 128)

    def decode(ref):
        parts = []
        for place in range(total // block):
            local, src_row = divmod(place, n_row)
            base = (src_row * n_col + local) * share
            high = ref[base : base + vec_cols, total:].astype(jnp.float32)
            low = ref[base + vec_cols : base + share, total:].astype(jnp.float32)
            parts.append(high + low)
        return jnp.concatenate(parts, axis=1)

    whole_ref[pl.ds(own_first, vec_cols), :] = decode(own_ref)
    whole_ref[pl.ds(other_first, vec_cols), :] = decode(other_ref)
    w_ref[:half_rows, :half_rows] = own_ref[:, pl.ds(own_place, half_rows)].T
    w_ref[half_rows:, :half_rows] = own_ref[:, pl.ds(other_place, half_rows)].T
    w_ref[:half_rows, half_rows:] = other_ref[:, pl.ds(own_place, half_rows)].T
    w_ref[half_rows:, half_rows:] = other_ref[:, pl.ds(other_place, half_rows)].T
    current = jnp.concatenate(
        [whole_ref[:, pl.ds(own_place, half_rows)], whole_ref[:, pl.ds(other_place, half_rows)]], axis=1
    )

    def apply(values):
        return lax.dot_general(
            values.astype(jnp.bfloat16),
            w_ref[...],
            (((1,), (0,)), ((), ())),
            preferred_element_type=jnp.float32,
        )

    for outer in range(ITERS):
        current = orthonormal_value(chebyshev(current, apply))
    whole_ref[...] = current
    for local in range(nb_dev):
        place = pl.multiple_of((((local + core) % 2) * n_row + row) * block, 128)
        x_ref[:, local * block : (local + 1) * block] = whole_ref[pl.ds(own_first, vec_cols), pl.ds(place, block)]

def filter_local(own, other, n_row, n_col, vec_cols):
    total = 2 * own.shape[0]
    block = own.shape[1] - total
    nb_dev = total // (block * n_row)
    return pl.pallas_call(
        functools.partial(filter_kernel, n_row=n_row, n_col=n_col, vec_cols=vec_cols),
        out_shape=jax.ShapeDtypeStruct((vec_cols, nb_dev * block), jnp.float32),
        in_specs=[pl.BlockSpec(memory_space=pltpu.VMEM)] * 2,
        out_specs=pl.BlockSpec(memory_space=pltpu.VMEM),
        scratch_shapes=[
            pltpu.VMEM((2 * vec_cols, total), jnp.float32),
            pltpu.VMEM((total, total), jnp.bfloat16),
        ],
    )(own, other)

def distributed(start, tiles, pattern, counts):
    nb_dev = tiles.shape[0]
    block = tiles.shape[2]
    total_rows = nb_dev * block * lax.axis_size("row")
    vec_cols = start.shape[0]
    col_index = lax.axis_index("col")
    kb_dev = tiles.shape[1]
    slot_ids = col_index * kb_dev + jnp.arange(kb_dev, dtype=jnp.int32)
    live = (slot_ids[None, :] < counts[:, None]).astype(jnp.bfloat16)
    masked = tiles * live[:, :, None, None]
    local_pattern = lax.dynamic_slice_in_dim(pattern, col_index * kb_dev, kb_dev, 1)
    partial_squares = jnp.einsum(
        "bkmn,bkmn->bm", masked, masked, preferred_element_type=jnp.float32
    )
    square_sums = lax.psum(partial_squares, "col")
    scaling = row_scaling(square_sums, counts, block)

    def apply_slots(current):
        whole = lax.all_gather(current.astype(jnp.bfloat16), "row", axis=1, tiled=True)
        blocks = whole.reshape(vec_cols, -1, block)
        picked = jnp.take(blocks, local_pattern, axis=1)
        product = jnp.einsum("cbkn,bkmn->cbm", picked, masked, preferred_element_type=jnp.float32)
        total = lax.psum(product.astype(jnp.bfloat16), "col").astype(jnp.float32)
        return total.reshape(vec_cols, -1) * scaling

    current = start
    for outer in range(ITERS):
        filtered = chebyshev(current, apply_slots)
        current = orthonormal(filtered, total_rows)
    return current


def split_bf16(values):
    rounded = lax.reduce_precision(values, exponent_bits=8, mantissa_bits=7)
    return rounded.astype(jnp.bfloat16), (values - rounded).astype(jnp.bfloat16)


def replicated(start, tiles, pattern, counts):
    nb_dev, kb_dev, block = tiles.shape[0], tiles.shape[1], tiles.shape[2]
    n_row, n_col = lax.axis_size("row"), lax.axis_size("col")
    nblk = nb_dev * n_row
    total_rows = nblk * block
    share = block // n_col
    vec_cols = start.shape[0]
    cols = 2 * vec_cols
    row_index = lax.axis_index("row")
    col_index = lax.axis_index("col")
    vec_index = lax.axis_index("vec")

    own_tiles = lax.dynamic_index_in_dim(tiles, vec_index, 0, keepdims=False)
    own_pattern = lax.dynamic_slice_in_dim(
        lax.dynamic_index_in_dim(pattern, vec_index, 0, keepdims=False), col_index * kb_dev, kb_dev, 0
    )
    own_count = lax.dynamic_index_in_dim(counts, vec_index, 0, keepdims=False)
    slot_ids = col_index * kb_dev + jnp.arange(kb_dev, dtype=jnp.int32)
    live = slot_ids < own_count
    position = (own_pattern % nb_dev) * n_row + own_pattern // nb_dev
    onehot = (position[:, None] == jnp.arange(nblk, dtype=jnp.int32)) & live[:, None]
    dense = jnp.einsum(
        "kj,kmn->mjn", onehot.astype(jnp.bfloat16), own_tiles, preferred_element_type=jnp.float32
    ).reshape(block, total_rows)
    masked = own_tiles * live.astype(jnp.bfloat16)[:, None, None]
    squares = jnp.einsum("kmn,kmn->m", masked, masked, preferred_element_type=jnp.float32)
    squares = jnp.broadcast_to(squares[:, None], (block, 128))
    partial = jnp.concatenate([dense, squares], axis=1)
    chunks = partial.reshape(n_col, share, total_rows + 128)
    summed = lax.dynamic_index_in_dim(chunks, col_index, 0, keepdims=False)
    for shift in range(1, n_col):
        sent = lax.dynamic_index_in_dim(chunks, (col_index + shift) % n_col, 0, keepdims=False)
        summed = summed + lax.ppermute(sent, "col", [(i, (i + shift) % n_col) for i in range(n_col)])

    entries = (own_count * block).astype(jnp.float32)
    scale = lax.rsqrt(summed[:, total_rows] / entries + EPSILON) / jnp.sqrt(entries) / HALF_WIDTH

    piece = lax.dynamic_slice_in_dim(start, col_index * block, block, 1)
    start_hi, start_lo = split_bf16(piece)
    extra = jnp.concatenate([start_hi, start_lo], axis=0)
    rows_bf16 = (summed[:, :total_rows] * scale[:, None]).astype(jnp.bfloat16)

    packed = jnp.concatenate([rows_bf16, extra], axis=1)
    copies = jnp.broadcast_to(packed[None], (n_row * n_col,) + packed.shape)
    half = lax.all_to_all(copies, ("row", "col"), 0, 0, tiled=True)
    half = half.reshape(n_row * n_col * share, total_rows + block)
    other = lax.ppermute(half, "vec", [(0, 1), (1, 0)])
    current = filter_local(half, other, n_row, n_col, vec_cols)
    return current


def per_device(start, tiles, pattern, counts):
    total_rows = tiles.shape[0] * tiles.shape[2] * lax.axis_size("row")
    n_col, n_vec = lax.axis_size("col"), lax.axis_size("vec")
    block = tiles.shape[2]
    fits = (
        total_rows * total_rows * 2 <= DENSE_BUDGET
        and n_vec == 2
        and tiles.shape[0] == n_vec
        and block % n_col == 0
        and block // n_col == 2 * start.shape[0]
        and tiles.shape[0] == n_col
    )
    if fits:
        return replicated(start, tiles, pattern, counts)
    return distributed(start, tiles, pattern, counts)


def solution(mesh):
    in_specs = (
        P("vec", ("grp", "row")),
        P(("grp", "row"), "col", None, None),
        P(("grp", "row"), None),
        P(("grp", "row")),
    )
    out_specs = P("vec", ("grp", "row"))
    return jax.shard_map(
        per_device, mesh=mesh, in_specs=in_specs, out_specs=out_specs, check_vma=False
    )
```

```python
import functools

import jax
import jax.numpy as jnp
from jax import lax
from jax.experimental import pallas as pl
from jax.experimental.pallas import tpu as pltpu
from jax.sharding import PartitionSpec as P

DEGREE = 8
ITERS = 2


HALF_WIDTH = 2.0
EPSILON = 1e-06
DENSE_BUDGET = 16 * 1024 * 1024


def row_scaling(square_sums, live_counts, block):
    entries = (live_counts * block).astype(jnp.float32)[:, None]
    scaled = lax.rsqrt(square_sums / entries + EPSILON) / jnp.sqrt(entries)
    return (scaled / HALF_WIDTH).reshape(1, -1)


def chebyshev(first, apply):
    previous = first
    present = apply(first)
    for step in range(DEGREE - 1):
        previous, present = (present, 2.0 * apply(present) - previous)
    return present


def orthonormal(mine, total_rows):
    both = lax.all_gather(mine.astype(jnp.bfloat16), "vec", axis=0, tiled=True).astype(mine.dtype)
    part_gram = jnp.dot(both, both.T, precision=lax.Precision.HIGHEST)
    gram = lax.psum(part_gram, "row") / total_rows
    lower = jnp.linalg.cholesky(gram)
    solved = jax.scipy.linalg.solve_triangular(lower, both, lower=True)
    width = mine.shape[0]
    return lax.dynamic_slice_in_dim(solved, lax.axis_index("vec") * width, width, 0)


def orthonormal_value(y):
    n, total = y.shape
    hi = lax.Precision.HIGHEST
    a = lax.dot_general(y, y, (((1,), (1,)), ((), ())), precision=hi, preferred_element_type=jnp.float32)
    a = a / total
    rows = lax.broadcasted_iota(jnp.int32, (n, n), 0)
    cols = lax.broadcasted_iota(jnp.int32, (n, n), 1)
    inverse = (rows == cols).astype(jnp.float32)
    for k in range(n):
        top = (k // 8) * 8
        pivot = a[k : k + 1, k : k + 1]
        down = jnp.where(rows[top:, k : k + 1] > k, a[top:, k : k + 1] * (1.0 / pivot), 0.0)
        across = jnp.where(cols[k : k + 1, :] > k, a[k : k + 1, :], 0.0)
        lower_a = a[top:] - down * across
        lower_inverse = inverse[top:] - down * inverse[k : k + 1, :]
        if top:
            a = jnp.concatenate([a[:top], lower_a], axis=0)
            inverse = jnp.concatenate([inverse[:top], lower_inverse], axis=0)
        else:
            a, inverse = lower_a, lower_inverse
    diagonal = jnp.sum(jnp.where(rows == cols, a, 0.0), axis=1, keepdims=True)
    inverse = inverse / jnp.sqrt(diagonal)
    return lax.dot_general(
        inverse, y, (((1,), (0,)), ((), ())), precision=hi, preferred_element_type=jnp.float32
    )


def filter_kernel(own_ref, other_ref, x_ref, whole_ref, w_ref, *, n_row, n_col, vec_cols):
    half_rows = own_ref.shape[0]
    total = 2 * half_rows
    block = own_ref.shape[1] - total
    nb_dev = total // (block * n_row)
    share = 2 * vec_cols
    row = lax.axis_index("row")
    core = lax.axis_index("vec")
    own_first = pl.multiple_of(core * vec_cols, 8)
    other_first = pl.multiple_of((1 - core) * vec_cols, 8)
    own_place = pl.multiple_of(core * half_rows, 128)
    other_place = pl.multiple_of((1 - core) * half_rows, 128)

    def decode(ref):
        parts = []
        for place in range(total // block):
            local, src_row = divmod(place, n_row)
            base = (src_row * n_col + local) * share
            high = ref[base : base + vec_cols, total:].astype(jnp.float32)
            low = ref[base + vec_cols : base + share, total:].astype(jnp.float32)
            parts.append(high + low)
        return jnp.concatenate(parts, axis=1)

    whole_ref[pl.ds(own_first, vec_cols), :] = decode(own_ref)
    whole_ref[pl.ds(other_first, vec_cols), :] = decode(other_ref)
    w_ref[:half_rows, :half_rows] = own_ref[:, pl.ds(own_place, half_rows)].T
    w_ref[half_rows:, :half_rows] = own_ref[:, pl.ds(other_place, half_rows)].T
    w_ref[:half_rows, half_rows:] = other_ref[:, pl.ds(own_place, half_rows)].T
    w_ref[half_rows:, half_rows:] = other_ref[:, pl.ds(other_place, half_rows)].T
    current = jnp.concatenate(
        [whole_ref[:, pl.ds(own_place, half_rows)], whole_ref[:, pl.ds(other_place, half_rows)]], axis=1
    )

    def apply(values):
        return lax.dot_general(
            values.astype(jnp.bfloat16),
            w_ref[...],
            (((1,), (0,)), ((), ())),
            preferred_element_type=jnp.float32,
        )

    for outer in range(ITERS):
        current = orthonormal_value(chebyshev(current, apply))
    whole_ref[...] = current
    for local in range(nb_dev):
        place = pl.multiple_of((((local + core) % 2) * n_row + row) * block, 128)
        x_ref[:, local * block : (local + 1) * block] = whole_ref[pl.ds(own_first, vec_cols), pl.ds(place, block)]

def filter_local(own, other, n_row, n_col, vec_cols):
    total = 2 * own.shape[0]
    block = own.shape[1] - total
    nb_dev = total // (block * n_row)
    return pl.pallas_call(
        functools.partial(filter_kernel, n_row=n_row, n_col=n_col, vec_cols=vec_cols),
        out_shape=jax.ShapeDtypeStruct((vec_cols, nb_dev * block), jnp.float32),
        in_specs=[pl.BlockSpec(memory_space=pltpu.VMEM)] * 2,
        out_specs=pl.BlockSpec(memory_space=pltpu.VMEM),
        scratch_shapes=[
            pltpu.VMEM((2 * vec_cols, total), jnp.float32),
            pltpu.VMEM((total, total), jnp.bfloat16),
        ],
    )(own, other)

def distributed(start, tiles, pattern, counts):
    nb_dev = tiles.shape[0]
    block = tiles.shape[2]
    total_rows = nb_dev * block * lax.axis_size("row")
    vec_cols = start.shape[0]
    col_index = lax.axis_index("col")
    kb_dev = tiles.shape[1]
    slot_ids = col_index * kb_dev + jnp.arange(kb_dev, dtype=jnp.int32)
    live = (slot_ids[None, :] < counts[:, None]).astype(jnp.bfloat16)
    masked = tiles * live[:, :, None, None]
    local_pattern = lax.dynamic_slice_in_dim(pattern, col_index * kb_dev, kb_dev, 1)
    partial_squares = jnp.einsum(
        "bkmn,bkmn->bm", masked, masked, preferred_element_type=jnp.float32
    )
    square_sums = lax.psum(partial_squares, "col")
    scaling = row_scaling(square_sums, counts, block)

    def apply_slots(current):
        whole = lax.all_gather(current.astype(jnp.bfloat16), "row", axis=1, tiled=True)
        blocks = whole.reshape(vec_cols, -1, block)
        picked = jnp.take(blocks, local_pattern, axis=1)
        product = jnp.einsum("cbkn,bkmn->cbm", picked, masked, preferred_element_type=jnp.float32)
        total = lax.psum(product.astype(jnp.bfloat16), "col").astype(jnp.float32)
        return total.reshape(vec_cols, -1) * scaling

    current = start
    for outer in range(ITERS):
        filtered = chebyshev(current, apply_slots)
        current = orthonormal(filtered, total_rows)
    return current


def split_bf16(values):
    rounded = lax.reduce_precision(values, exponent_bits=8, mantissa_bits=7)
    return rounded.astype(jnp.bfloat16), (values - rounded).astype(jnp.bfloat16)


def replicated(start, tiles, pattern, counts):
    nb_dev, kb_dev, block = tiles.shape[0], tiles.shape[1], tiles.shape[2]
    n_row, n_col = lax.axis_size("row"), lax.axis_size("col")
    nblk = nb_dev * n_row
    total_rows = nblk * block
    share = block // n_col
    vec_cols = start.shape[0]
    cols = 2 * vec_cols
    row_index = lax.axis_index("row")
    col_index = lax.axis_index("col")
    vec_index = lax.axis_index("vec")

    own_tiles = lax.dynamic_index_in_dim(tiles, vec_index, 0, keepdims=False)
    own_pattern = lax.dynamic_slice_in_dim(
        lax.dynamic_index_in_dim(pattern, vec_index, 0, keepdims=False), col_index * kb_dev, kb_dev, 0
    )
    own_count = lax.dynamic_index_in_dim(counts, vec_index, 0, keepdims=False)
    slot_ids = col_index * kb_dev + jnp.arange(kb_dev, dtype=jnp.int32)
    live = slot_ids < own_count
    position = (own_pattern % nb_dev) * n_row + own_pattern // nb_dev
    onehot = (position[:, None] == jnp.arange(nblk, dtype=jnp.int32)) & live[:, None]
    dense = jnp.einsum(
        "kj,kmn->mjn", onehot.astype(jnp.bfloat16), own_tiles, preferred_element_type=jnp.float32
    ).reshape(block, total_rows)
    masked = own_tiles * live.astype(jnp.bfloat16)[:, None, None]
    squares = jnp.einsum("kmn,kmn->m", masked, masked, preferred_element_type=jnp.float32)
    squares = jnp.broadcast_to(squares[:, None], (block, 128))
    partial = jnp.concatenate([dense, squares], axis=1)
    chunks = partial.reshape(n_col, share, total_rows + 128)
    summed = lax.dynamic_index_in_dim(chunks, col_index, 0, keepdims=False)
    for shift in range(1, n_col):
        sent = lax.dynamic_index_in_dim(chunks, (col_index + shift) % n_col, 0, keepdims=False)
        summed = summed + lax.ppermute(sent, "col", [(i, (i + shift) % n_col) for i in range(n_col)])

    entries = (own_count * block).astype(jnp.float32)
    scale = lax.rsqrt(summed[:, total_rows] / entries + EPSILON) / jnp.sqrt(entries) / HALF_WIDTH

    piece = lax.dynamic_slice_in_dim(start, col_index * block, block, 1)
    start_hi, start_lo = split_bf16(piece)
    extra = jnp.concatenate([start_hi, start_lo], axis=0)
    rows_bf16 = (summed[:, :total_rows] * scale[:, None]).astype(jnp.bfloat16)

    packed = jnp.concatenate([rows_bf16, extra], axis=1)
    copies = jnp.broadcast_to(packed[None], (n_row * n_col,) + packed.shape)
    half = lax.all_to_all(copies, ("row", "col"), 0, 0, tiled=True)
    half = half.reshape(n_row * n_col * share, total_rows + block)
    other = lax.ppermute(half, "vec", [(0, 1), (1, 0)])
    current = filter_local(half, other, n_row, n_col, vec_cols)
    return current


def per_device(start, tiles, pattern, counts):
    total_rows = tiles.shape[0] * tiles.shape[2] * lax.axis_size("row")
    n_col, n_vec = lax.axis_size("col"), lax.axis_size("vec")
    block = tiles.shape[2]
    fits = (
        total_rows * total_rows * 2 <= DENSE_BUDGET
        and n_vec == 2
        and tiles.shape[0] == n_vec
        and block % n_col == 0
        and block // n_col == 2 * start.shape[0]
        and tiles.shape[0] == n_col
    )
    if fits:
        return replicated(start, tiles, pattern, counts)
    return distributed(start, tiles, pattern, counts)


def solution(mesh):
    in_specs = (
        P("vec", ("grp", "row")),
        P(("grp", "row"), "col", None, None),
        P(("grp", "row"), None),
        P(("grp", "row")),
    )
    out_specs = P("vec", ("grp", "row"))
    return jax.shard_map(
        per_device, mesh=mesh, in_specs=in_specs, out_specs=out_specs, check_vma=False
    )
```

```python
import functools

import jax
import jax.numpy as jnp
from jax import lax
from jax.experimental import pallas as pl
from jax.experimental.pallas import tpu as pltpu
from jax.sharding import PartitionSpec as P

DEGREE = 8
ITERS = 2


HALF_WIDTH = 2.0
EPSILON = 1e-06
DENSE_BUDGET = 16 * 1024 * 1024


def row_scaling(square_sums, live_counts, block):
    entries = (live_counts * block).astype(jnp.float32)[:, None]
    scaled = lax.rsqrt(square_sums / entries + EPSILON) / jnp.sqrt(entries)
    return (scaled / HALF_WIDTH).reshape(1, -1)


def chebyshev(first, apply):
    previous = first
    present = apply(first)
    for step in range(DEGREE - 1):
        previous, present = (present, 2.0 * apply(present) - previous)
    return present


def orthonormal(mine, total_rows):
    both = lax.all_gather(mine.astype(jnp.bfloat16), "vec", axis=0, tiled=True).astype(mine.dtype)
    part_gram = jnp.dot(both, both.T, precision=lax.Precision.HIGHEST)
    gram = lax.psum(part_gram, "row") / total_rows
    lower = jnp.linalg.cholesky(gram)
    solved = jax.scipy.linalg.solve_triangular(lower, both, lower=True)
    width = mine.shape[0]
    return lax.dynamic_slice_in_dim(solved, lax.axis_index("vec") * width, width, 0)


def orthonormal_value(y):
    n, total = y.shape
    hi = lax.Precision.HIGHEST
    a = lax.dot_general(y, y, (((1,), (1,)), ((), ())), precision=hi, preferred_element_type=jnp.float32)
    a = a / total
    rows = lax.broadcasted_iota(jnp.int32, (n, n), 0)
    cols = lax.broadcasted_iota(jnp.int32, (n, n), 1)
    inverse = (rows == cols).astype(jnp.float32)
    for k in range(n):
        top = (k // 8) * 8
        pivot = a[k : k + 1, k : k + 1]
        down = jnp.where(rows[top:, k : k + 1] > k, a[top:, k : k + 1] * (1.0 / pivot), 0.0)
        across = jnp.where(cols[k : k + 1, :] > k, a[k : k + 1, :], 0.0)
        lower_a = a[top:] - down * across
        lower_inverse = inverse[top:] - down * inverse[k : k + 1, :]
        if top:
            a = jnp.concatenate([a[:top], lower_a], axis=0)
            inverse = jnp.concatenate([inverse[:top], lower_inverse], axis=0)
        else:
            a, inverse = lower_a, lower_inverse
    diagonal = jnp.sum(jnp.where(rows == cols, a, 0.0), axis=1, keepdims=True)
    inverse = inverse / jnp.sqrt(diagonal)
    return lax.dot_general(
        inverse, y, (((1,), (0,)), ((), ())), precision=hi, preferred_element_type=jnp.float32
    )


def filter_kernel(own_ref, other_ref, x_ref, whole_ref, w_ref, *, n_row, n_col, vec_cols):
    half_rows = own_ref.shape[0]
    total = 2 * half_rows
    block = own_ref.shape[1] - total
    nb_dev = total // (block * n_row)
    share = 2 * vec_cols
    row = lax.axis_index("row")
    core = lax.axis_index("vec")
    own_first = pl.multiple_of(core * vec_cols, 8)
    other_first = pl.multiple_of((1 - core) * vec_cols, 8)
    own_place = pl.multiple_of(core * half_rows, 128)
    other_place = pl.multiple_of((1 - core) * half_rows, 128)

    def decode(ref):
        parts = []
        for place in range(total // block):
            local, src_row = divmod(place, n_row)
            base = (src_row * n_col + local) * share
            high = ref[base : base + vec_cols, total:].astype(jnp.float32)
            low = ref[base + vec_cols : base + share, total:].astype(jnp.float32)
            parts.append(high + low)
        return jnp.concatenate(parts, axis=1)

    whole_ref[pl.ds(own_first, vec_cols), :] = decode(own_ref)
    whole_ref[pl.ds(other_first, vec_cols), :] = decode(other_ref)
    w_ref[:half_rows, :half_rows] = own_ref[:, pl.ds(own_place, half_rows)].T
    w_ref[half_rows:, :half_rows] = own_ref[:, pl.ds(other_place, half_rows)].T
    w_ref[:half_rows, half_rows:] = other_ref[:, pl.ds(own_place, half_rows)].T
    w_ref[half_rows:, half_rows:] = other_ref[:, pl.ds(other_place, half_rows)].T
    current = jnp.concatenate(
        [whole_ref[:, pl.ds(own_place, half_rows)], whole_ref[:, pl.ds(other_place, half_rows)]], axis=1
    )

    def apply(values):
        return lax.dot_general(
            values.astype(jnp.bfloat16),
            w_ref[...],
            (((1,), (0,)), ((), ())),
            preferred_element_type=jnp.float32,
        )

    for outer in range(ITERS):
        current = orthonormal_value(chebyshev(current, apply))
    whole_ref[...] = current
    for local in range(nb_dev):
        place = pl.multiple_of((((local + core) % 2) * n_row + row) * block, 128)
        x_ref[:, local * block : (local + 1) * block] = whole_ref[pl.ds(own_first, vec_cols), pl.ds(place, block)]

def filter_local(own, other, n_row, n_col, vec_cols):
    total = 2 * own.shape[0]
    block = own.shape[1] - total
    nb_dev = total // (block * n_row)
    return pl.pallas_call(
        functools.partial(filter_kernel, n_row=n_row, n_col=n_col, vec_cols=vec_cols),
        out_shape=jax.ShapeDtypeStruct((vec_cols, nb_dev * block), jnp.float32),
        in_specs=[pl.BlockSpec(memory_space=pltpu.VMEM)] * 2,
        out_specs=pl.BlockSpec(memory_space=pltpu.VMEM),
        scratch_shapes=[
            pltpu.VMEM((2 * vec_cols, total), jnp.float32),
            pltpu.VMEM((total, total), jnp.bfloat16),
        ],
    )(own, other)

def distributed(start, tiles, pattern, counts):
    nb_dev = tiles.shape[0]
    block = tiles.shape[2]
    total_rows = nb_dev * block * lax.axis_size("row")
    vec_cols = start.shape[0]
    col_index = lax.axis_index("col")
    kb_dev = tiles.shape[1]
    slot_ids = col_index * kb_dev + jnp.arange(kb_dev, dtype=jnp.int32)
    live = (slot_ids[None, :] < counts[:, None]).astype(jnp.bfloat16)
    masked = tiles * live[:, :, None, None]
    local_pattern = lax.dynamic_slice_in_dim(pattern, col_index * kb_dev, kb_dev, 1)
    partial_squares = jnp.einsum(
        "bkmn,bkmn->bm", masked, masked, preferred_element_type=jnp.float32
    )
    square_sums = lax.psum(partial_squares, "col")
    scaling = row_scaling(square_sums, counts, block)

    def apply_slots(current):
        whole = lax.all_gather(current.astype(jnp.bfloat16), "row", axis=1, tiled=True)
        blocks = whole.reshape(vec_cols, -1, block)
        picked = jnp.take(blocks, local_pattern, axis=1)
        product = jnp.einsum("cbkn,bkmn->cbm", picked, masked, preferred_element_type=jnp.float32)
        total = lax.psum(product.astype(jnp.bfloat16), "col").astype(jnp.float32)
        return total.reshape(vec_cols, -1) * scaling

    current = start
    for outer in range(ITERS):
        filtered = chebyshev(current, apply_slots)
        current = orthonormal(filtered, total_rows)
    return current


def split_bf16(values):
    rounded = lax.reduce_precision(values, exponent_bits=8, mantissa_bits=7)
    return rounded.astype(jnp.bfloat16), (values - rounded).astype(jnp.bfloat16)


def replicated(start, tiles, pattern, counts):
    nb_dev, kb_dev, block = tiles.shape[0], tiles.shape[1], tiles.shape[2]
    n_row, n_col = lax.axis_size("row"), lax.axis_size("col")
    nblk = nb_dev * n_row
    total_rows = nblk * block
    share = block // n_col
    vec_cols = start.shape[0]
    cols = 2 * vec_cols
    row_index = lax.axis_index("row")
    col_index = lax.axis_index("col")
    vec_index = lax.axis_index("vec")

    own_pattern = lax.dynamic_slice_in_dim(
        lax.dynamic_index_in_dim(pattern, vec_index, 0, keepdims=False), col_index * kb_dev, kb_dev, 0
    )
    own_count = lax.dynamic_index_in_dim(counts, vec_index, 0, keepdims=False)
    slot_ids = col_index * kb_dev + jnp.arange(kb_dev, dtype=jnp.int32)
    live = slot_ids < own_count
    position = (own_pattern % nb_dev) * n_row + own_pattern // nb_dev
    onehot = (position[:, None] == jnp.arange(nblk, dtype=jnp.int32)) & live[:, None]
    own_block = (jnp.arange(nb_dev, dtype=jnp.int32) == vec_index)[:, None]
    weights = (own_block[:, :, None] & onehot[None]).astype(jnp.bfloat16)
    dense = jnp.einsum(
        "bkj,bkmn->mjn", weights, tiles, preferred_element_type=jnp.float32
    ).reshape(block, total_rows)
    masked = tiles * (own_block & live[None]).astype(jnp.bfloat16)[:, :, None, None]
    squares = jnp.einsum("bkmn,bkmn->m", masked, masked, preferred_element_type=jnp.float32)
    squares = jnp.broadcast_to(squares[:, None], (block, 128))
    partial = jnp.concatenate([dense, squares], axis=1)
    chunks = partial.reshape(n_col, share, total_rows + 128)
    summed = lax.dynamic_index_in_dim(chunks, col_index, 0, keepdims=False)
    for shift in range(1, n_col):
        sent = lax.dynamic_index_in_dim(chunks, (col_index + shift) % n_col, 0, keepdims=False)
        summed = summed + lax.ppermute(sent, "col", [(i, (i + shift) % n_col) for i in range(n_col)])

    entries = (own_count * block).astype(jnp.float32)
    scale = lax.rsqrt(summed[:, total_rows] / entries + EPSILON) / jnp.sqrt(entries) / HALF_WIDTH

    piece = lax.dynamic_slice_in_dim(start, col_index * block, block, 1)
    start_hi, start_lo = split_bf16(piece)
    extra = jnp.concatenate([start_hi, start_lo], axis=0)
    rows_bf16 = (summed[:, :total_rows] * scale[:, None]).astype(jnp.bfloat16)

    packed = jnp.concatenate([rows_bf16, extra], axis=1)
    copies = jnp.broadcast_to(packed[None], (n_row * n_col,) + packed.shape)
    half = lax.all_to_all(copies, ("row", "col"), 0, 0, tiled=True)
    half = half.reshape(n_row * n_col * share, total_rows + block)
    other = lax.ppermute(half, "vec", [(0, 1), (1, 0)])
    current = filter_local(half, other, n_row, n_col, vec_cols)
    return current


def per_device(start, tiles, pattern, counts):
    total_rows = tiles.shape[0] * tiles.shape[2] * lax.axis_size("row")
    n_col, n_vec = lax.axis_size("col"), lax.axis_size("vec")
    block = tiles.shape[2]
    fits = (
        total_rows * total_rows * 2 <= DENSE_BUDGET
        and n_vec == 2
        and tiles.shape[0] == n_vec
        and block % n_col == 0
        and block // n_col == 2 * start.shape[0]
        and tiles.shape[0] == n_col
    )
    if fits:
        return replicated(start, tiles, pattern, counts)
    return distributed(start, tiles, pattern, counts)


def solution(mesh):
    in_specs = (
        P("vec", ("grp", "row")),
        P(("grp", "row"), "col", None, None),
        P(("grp", "row"), None),
        P(("grp", "row")),
    )
    out_specs = P("vec", ("grp", "row"))
    return jax.shard_map(
        per_device, mesh=mesh, in_specs=in_specs, out_specs=out_specs, check_vma=False
    )
```

```python
import functools

import jax
import jax.numpy as jnp
from jax import lax
from jax.experimental import pallas as pl
from jax.experimental.pallas import tpu as pltpu
from jax.sharding import PartitionSpec as P

DEGREE = 8
ITERS = 2


HALF_WIDTH = 2.0
EPSILON = 1e-06
DENSE_BUDGET = 16 * 1024 * 1024


def row_scaling(square_sums, live_counts, block):
    entries = (live_counts * block).astype(jnp.float32)[:, None]
    scaled = lax.rsqrt(square_sums / entries + EPSILON) / jnp.sqrt(entries)
    return (scaled / HALF_WIDTH).reshape(1, -1)


def chebyshev(first, apply):
    previous = first
    present = apply(first)
    for step in range(DEGREE - 1):
        previous, present = (present, 2.0 * apply(present) - previous)
    return present


def orthonormal(mine, total_rows):
    both = lax.all_gather(mine.astype(jnp.bfloat16), "vec", axis=0, tiled=True).astype(mine.dtype)
    part_gram = jnp.dot(both, both.T, precision=lax.Precision.HIGHEST)
    gram = lax.psum(part_gram, "row") / total_rows
    lower = jnp.linalg.cholesky(gram)
    solved = jax.scipy.linalg.solve_triangular(lower, both, lower=True)
    width = mine.shape[0]
    return lax.dynamic_slice_in_dim(solved, lax.axis_index("vec") * width, width, 0)


def orthonormal_factor(y):
    n, total = y.shape
    hi = lax.Precision.HIGHEST
    a = lax.dot_general(y, y, (((1,), (1,)), ((), ())), precision=hi, preferred_element_type=jnp.float32)
    a = a / total
    rows = lax.broadcasted_iota(jnp.int32, (n, n), 0)
    cols = lax.broadcasted_iota(jnp.int32, (n, n), 1)
    inverse = (rows == cols).astype(jnp.float32)
    for k in range(n):
        top = (k // 8) * 8
        pivot = a[k : k + 1, k : k + 1]
        down = jnp.where(rows[top:, k : k + 1] > k, a[top:, k : k + 1] * (1.0 / pivot), 0.0)
        across = jnp.where(cols[k : k + 1, :] > k, a[k : k + 1, :], 0.0)
        lower_a = a[top:] - down * across
        lower_inverse = inverse[top:] - down * inverse[k : k + 1, :]
        if top:
            a = jnp.concatenate([a[:top], lower_a], axis=0)
            inverse = jnp.concatenate([inverse[:top], lower_inverse], axis=0)
        else:
            a, inverse = lower_a, lower_inverse
    diagonal = jnp.sum(jnp.where(rows == cols, a, 0.0), axis=1, keepdims=True)
    return inverse / jnp.sqrt(diagonal)


def orthonormal_value(y):
    return lax.dot_general(
        orthonormal_factor(y), y, (((1,), (0,)), ((), ())),
        precision=lax.Precision.HIGHEST, preferred_element_type=jnp.float32,
    )


def filter_kernel(own_ref, other_ref, x_ref, whole_ref, w_ref, inverse_ref, *, n_row, n_col, vec_cols):
    half_rows = own_ref.shape[0]
    total = 2 * half_rows
    block = own_ref.shape[1] - total
    nb_dev = total // (block * n_row)
    share = 2 * vec_cols
    row = lax.axis_index("row")
    core = lax.axis_index("vec")
    own_first = pl.multiple_of(core * vec_cols, 8)
    other_first = pl.multiple_of((1 - core) * vec_cols, 8)
    own_place = pl.multiple_of(core * half_rows, 128)
    other_place = pl.multiple_of((1 - core) * half_rows, 128)

    def decode(ref):
        parts = []
        for place in range(total // block):
            local, src_row = divmod(place, n_row)
            base = (src_row * n_col + local) * share
            high = ref[base : base + vec_cols, total:].astype(jnp.float32)
            low = ref[base + vec_cols : base + share, total:].astype(jnp.float32)
            parts.append(high + low)
        return jnp.concatenate(parts, axis=1)

    whole_ref[pl.ds(own_first, vec_cols), :] = decode(own_ref)
    whole_ref[pl.ds(other_first, vec_cols), :] = decode(other_ref)
    w_ref[:half_rows, :half_rows] = own_ref[:, pl.ds(own_place, half_rows)].T
    w_ref[half_rows:, :half_rows] = own_ref[:, pl.ds(other_place, half_rows)].T
    w_ref[:half_rows, half_rows:] = other_ref[:, pl.ds(own_place, half_rows)].T
    w_ref[half_rows:, half_rows:] = other_ref[:, pl.ds(other_place, half_rows)].T
    current = jnp.concatenate(
        [whole_ref[:, pl.ds(own_place, half_rows)], whole_ref[:, pl.ds(other_place, half_rows)]], axis=1
    )

    def apply(values):
        return lax.dot_general(
            values.astype(jnp.bfloat16),
            w_ref[...],
            (((1,), (0,)), ((), ())),
            preferred_element_type=jnp.float32,
        )

    for outer in range(ITERS - 1):
        current = orthonormal_value(chebyshev(current, apply))
    filtered = chebyshev(current, apply)
    inverse_ref[...] = orthonormal_factor(filtered)
    whole_ref[...] = filtered
    mine = inverse_ref[pl.ds(own_first, vec_cols), :]
    for local in range(nb_dev):
        place = pl.multiple_of((((local + core) % 2) * n_row + row) * block, 128)
        x_ref[:, local * block : (local + 1) * block] = lax.dot_general(
            mine, whole_ref[:, pl.ds(place, block)], (((1,), (0,)), ((), ())),
            precision=lax.Precision.HIGHEST, preferred_element_type=jnp.float32,
        )

def filter_local(own, other, n_row, n_col, vec_cols):
    total = 2 * own.shape[0]
    block = own.shape[1] - total
    nb_dev = total // (block * n_row)
    return pl.pallas_call(
        functools.partial(filter_kernel, n_row=n_row, n_col=n_col, vec_cols=vec_cols),
        out_shape=jax.ShapeDtypeStruct((vec_cols, nb_dev * block), jnp.float32),
        in_specs=[pl.BlockSpec(memory_space=pltpu.VMEM)] * 2,
        out_specs=pl.BlockSpec(memory_space=pltpu.VMEM),
        scratch_shapes=[
            pltpu.VMEM((2 * vec_cols, total), jnp.float32),
            pltpu.VMEM((total, total), jnp.bfloat16),
            pltpu.VMEM((2 * vec_cols, 2 * vec_cols), jnp.float32),
        ],
    )(own, other)

def distributed(start, tiles, pattern, counts):
    nb_dev = tiles.shape[0]
    block = tiles.shape[2]
    total_rows = nb_dev * block * lax.axis_size("row")
    vec_cols = start.shape[0]
    col_index = lax.axis_index("col")
    kb_dev = tiles.shape[1]
    slot_ids = col_index * kb_dev + jnp.arange(kb_dev, dtype=jnp.int32)
    live = (slot_ids[None, :] < counts[:, None]).astype(jnp.bfloat16)
    masked = tiles * live[:, :, None, None]
    local_pattern = lax.dynamic_slice_in_dim(pattern, col_index * kb_dev, kb_dev, 1)
    partial_squares = jnp.einsum(
        "bkmn,bkmn->bm", masked, masked, preferred_element_type=jnp.float32
    )
    square_sums = lax.psum(partial_squares, "col")
    scaling = row_scaling(square_sums, counts, block)

    def apply_slots(current):
        whole = lax.all_gather(current.astype(jnp.bfloat16), "row", axis=1, tiled=True)
        blocks = whole.reshape(vec_cols, -1, block)
        picked = jnp.take(blocks, local_pattern, axis=1)
        product = jnp.einsum("cbkn,bkmn->cbm", picked, masked, preferred_element_type=jnp.float32)
        total = lax.psum(product.astype(jnp.bfloat16), "col").astype(jnp.float32)
        return total.reshape(vec_cols, -1) * scaling

    current = start
    for outer in range(ITERS):
        filtered = chebyshev(current, apply_slots)
        current = orthonormal(filtered, total_rows)
    return current


def split_bf16(values):
    rounded = lax.reduce_precision(values, exponent_bits=8, mantissa_bits=7)
    return rounded.astype(jnp.bfloat16), (values - rounded).astype(jnp.bfloat16)


def replicated(start, tiles, pattern, counts):
    nb_dev, kb_dev, block = tiles.shape[0], tiles.shape[1], tiles.shape[2]
    n_row, n_col = lax.axis_size("row"), lax.axis_size("col")
    nblk = nb_dev * n_row
    total_rows = nblk * block
    share = block // n_col
    vec_cols = start.shape[0]
    cols = 2 * vec_cols
    row_index = lax.axis_index("row")
    col_index = lax.axis_index("col")
    vec_index = lax.axis_index("vec")

    own_tiles = lax.dynamic_index_in_dim(tiles, vec_index, 0, keepdims=False)
    own_pattern = lax.dynamic_slice_in_dim(
        lax.dynamic_index_in_dim(pattern, vec_index, 0, keepdims=False), col_index * kb_dev, kb_dev, 0
    )
    own_count = lax.dynamic_index_in_dim(counts, vec_index, 0, keepdims=False)
    slot_ids = col_index * kb_dev + jnp.arange(kb_dev, dtype=jnp.int32)
    live = slot_ids < own_count
    position = (own_pattern % nb_dev) * n_row + own_pattern // nb_dev
    onehot = (position[:, None] == jnp.arange(nblk, dtype=jnp.int32)) & live[:, None]
    dense = jnp.einsum(
        "kj,kmn->mjn", onehot.astype(jnp.bfloat16), own_tiles, preferred_element_type=jnp.float32
    ).reshape(block, total_rows)
    masked = own_tiles * live.astype(jnp.bfloat16)[:, None, None]
    squares = jnp.einsum("kmn,kmn->m", masked, masked, preferred_element_type=jnp.float32)
    squares = jnp.broadcast_to(squares[:, None], (block, 128))
    partial = jnp.concatenate([dense, squares], axis=1)
    chunks = partial.reshape(n_col, share, total_rows + 128)
    summed = lax.dynamic_index_in_dim(chunks, col_index, 0, keepdims=False)
    for shift in range(1, n_col):
        sent = lax.dynamic_index_in_dim(chunks, (col_index + shift) % n_col, 0, keepdims=False)
        summed = summed + lax.ppermute(sent, "col", [(i, (i + shift) % n_col) for i in range(n_col)])

    entries = (own_count * block).astype(jnp.float32)
    scale = lax.rsqrt(summed[:, total_rows] / entries + EPSILON) / jnp.sqrt(entries) / HALF_WIDTH

    piece = lax.dynamic_slice_in_dim(start, col_index * block, block, 1)
    start_hi, start_lo = split_bf16(piece)
    extra = jnp.concatenate([start_hi, start_lo], axis=0)
    rows_bf16 = (summed[:, :total_rows] * scale[:, None]).astype(jnp.bfloat16)

    packed = jnp.concatenate([rows_bf16, extra], axis=1)
    copies = jnp.broadcast_to(packed[None], (n_row * n_col,) + packed.shape)
    half = lax.all_to_all(copies, ("row", "col"), 0, 0, tiled=True)
    half = half.reshape(n_row * n_col * share, total_rows + block)
    other = lax.ppermute(half, "vec", [(0, 1), (1, 0)])
    current = filter_local(half, other, n_row, n_col, vec_cols)
    return current


def per_device(start, tiles, pattern, counts):
    total_rows = tiles.shape[0] * tiles.shape[2] * lax.axis_size("row")
    n_col, n_vec = lax.axis_size("col"), lax.axis_size("vec")
    block = tiles.shape[2]
    fits = (
        total_rows * total_rows * 2 <= DENSE_BUDGET
        and n_vec == 2
        and tiles.shape[0] == n_vec
        and block % n_col == 0
        and block // n_col == 2 * start.shape[0]
        and tiles.shape[0] == n_col
    )
    if fits:
        return replicated(start, tiles, pattern, counts)
    return distributed(start, tiles, pattern, counts)


def solution(mesh):
    in_specs = (
        P("vec", ("grp", "row")),
        P(("grp", "row"), "col", None, None),
        P(("grp", "row"), None),
        P(("grp", "row")),
    )
    out_specs = P("vec", ("grp", "row"))
    return jax.shard_map(
        per_device, mesh=mesh, in_specs=in_specs, out_specs=out_specs, check_vma=False
    )
```

```python
import functools

import jax
import jax.numpy as jnp
from jax import lax
from jax.experimental import pallas as pl
from jax.experimental.pallas import tpu as pltpu
from jax.sharding import PartitionSpec as P

DEGREE = 8
ITERS = 2


HALF_WIDTH = 2.0
EPSILON = 1e-06
DENSE_BUDGET = 16 * 1024 * 1024


def row_scaling(square_sums, live_counts, block):
    entries = (live_counts * block).astype(jnp.float32)[:, None]
    scaled = lax.rsqrt(square_sums / entries + EPSILON) / jnp.sqrt(entries)
    return (scaled / HALF_WIDTH).reshape(1, -1)


def chebyshev(first, apply):
    previous = first
    present = apply(first)
    for step in range(DEGREE - 1):
        previous, present = (present, 2.0 * apply(present) - previous)
    return present


def orthonormal(mine, total_rows):
    both = lax.all_gather(mine.astype(jnp.bfloat16), "vec", axis=0, tiled=True).astype(mine.dtype)
    part_gram = jnp.dot(both, both.T, precision=lax.Precision.HIGHEST)
    gram = lax.psum(part_gram, "row") / total_rows
    lower = jnp.linalg.cholesky(gram)
    solved = jax.scipy.linalg.solve_triangular(lower, both, lower=True)
    width = mine.shape[0]
    return lax.dynamic_slice_in_dim(solved, lax.axis_index("vec") * width, width, 0)


def orthonormal_factor(y):
    n, total = y.shape
    hi = lax.Precision.HIGHEST
    a = lax.dot_general(y, y, (((1,), (1,)), ((), ())), precision=hi, preferred_element_type=jnp.float32)
    a = a / total
    rows = lax.broadcasted_iota(jnp.int32, (n, n), 0)
    cols = lax.broadcasted_iota(jnp.int32, (n, n), 1)
    inverse = (rows == cols).astype(jnp.float32)
    for k in range(n):
        top = (k // 8) * 8
        pivot = a[k : k + 1, k : k + 1]
        down = jnp.where(rows[top:, k : k + 1] > k, a[top:, k : k + 1] * (1.0 / pivot), 0.0)
        across = jnp.where(cols[k : k + 1, :] > k, a[k : k + 1, :], 0.0)
        lower_a = a[top:] - down * across
        lower_inverse = inverse[top:] - down * inverse[k : k + 1, :]
        if top:
            a = jnp.concatenate([a[:top], lower_a], axis=0)
            inverse = jnp.concatenate([inverse[:top], lower_inverse], axis=0)
        else:
            a, inverse = lower_a, lower_inverse
    diagonal = jnp.sum(jnp.where(rows == cols, a, 0.0), axis=1, keepdims=True)
    return inverse / jnp.sqrt(diagonal)


def orthonormal_value(y):
    return lax.dot_general(
        orthonormal_factor(y), y, (((1,), (0,)), ((), ())),
        precision=lax.Precision.HIGHEST, preferred_element_type=jnp.float32,
    )


def filter_kernel(own_ref, other_ref, x_ref, whole_ref, w_ref, inverse_ref, *, n_row, n_col, vec_cols):
    half_rows = own_ref.shape[0]
    total = 2 * half_rows
    block = own_ref.shape[1] - total
    nb_dev = total // (block * n_row)
    share = 2 * vec_cols
    row = lax.axis_index("row")
    core = lax.axis_index("vec")
    own_first = pl.multiple_of(core * vec_cols, 8)
    other_first = pl.multiple_of((1 - core) * vec_cols, 8)
    own_place = pl.multiple_of(core * half_rows, 128)
    other_place = pl.multiple_of((1 - core) * half_rows, 128)

    def decode(ref):
        parts = []
        for place in range(total // block):
            local, src_row = divmod(place, n_row)
            base = (src_row * n_col + local) * share
            high = ref[base : base + vec_cols, total:].astype(jnp.float32)
            low = ref[base + vec_cols : base + share, total:].astype(jnp.float32)
            parts.append(high + low)
        return jnp.concatenate(parts, axis=1)

    whole_ref[pl.ds(own_first, vec_cols), :] = decode(own_ref)
    whole_ref[pl.ds(other_first, vec_cols), :] = decode(other_ref)
    w_ref[:half_rows, :half_rows] = own_ref[:, pl.ds(own_place, half_rows)].T
    w_ref[half_rows:, :half_rows] = own_ref[:, pl.ds(other_place, half_rows)].T
    w_ref[:half_rows, half_rows:] = other_ref[:, pl.ds(own_place, half_rows)].T
    w_ref[half_rows:, half_rows:] = other_ref[:, pl.ds(other_place, half_rows)].T
    current = jnp.concatenate(
        [whole_ref[:, pl.ds(own_place, half_rows)], whole_ref[:, pl.ds(other_place, half_rows)]], axis=1
    )

    def apply(values):
        return lax.dot_general(
            values.astype(jnp.bfloat16),
            w_ref[...],
            (((1,), (0,)), ((), ())),
            preferred_element_type=jnp.float32,
        )

    for outer in range(ITERS - 1):
        current = orthonormal_value(chebyshev(current, apply))
    filtered = chebyshev(current, apply)
    inverse_ref[...] = orthonormal_factor(filtered)
    whole_ref[...] = filtered
    mine = inverse_ref[pl.ds(own_first, vec_cols), :]
    for local in range(nb_dev):
        place = pl.multiple_of((((local + core) % 2) * n_row + row) * block, 128)
        x_ref[:, local * block : (local + 1) * block] = lax.dot_general(
            mine, whole_ref[:, pl.ds(place, block)], (((1,), (0,)), ((), ())),
            precision=lax.Precision.HIGHEST, preferred_element_type=jnp.float32,
        )

def filter_local(own, other, n_row, n_col, vec_cols):
    total = 2 * own.shape[0]
    block = own.shape[1] - total
    nb_dev = total // (block * n_row)
    return pl.pallas_call(
        functools.partial(filter_kernel, n_row=n_row, n_col=n_col, vec_cols=vec_cols),
        out_shape=jax.ShapeDtypeStruct((vec_cols, nb_dev * block), jnp.float32),
        in_specs=[pl.BlockSpec(memory_space=pltpu.VMEM)] * 2,
        out_specs=pl.BlockSpec(memory_space=pltpu.VMEM),
        scratch_shapes=[
            pltpu.VMEM((2 * vec_cols, total), jnp.float32),
            pltpu.VMEM((total, total), jnp.bfloat16),
            pltpu.VMEM((2 * vec_cols, 2 * vec_cols), jnp.float32),
        ],
    )(own, other)

def distributed(start, tiles, pattern, counts):
    nb_dev = tiles.shape[0]
    block = tiles.shape[2]
    total_rows = nb_dev * block * lax.axis_size("row")
    vec_cols = start.shape[0]
    col_index = lax.axis_index("col")
    kb_dev = tiles.shape[1]
    slot_ids = col_index * kb_dev + jnp.arange(kb_dev, dtype=jnp.int32)
    live = (slot_ids[None, :] < counts[:, None]).astype(jnp.bfloat16)
    masked = tiles * live[:, :, None, None]
    local_pattern = lax.dynamic_slice_in_dim(pattern, col_index * kb_dev, kb_dev, 1)
    partial_squares = jnp.einsum(
        "bkmn,bkmn->bm", masked, masked, preferred_element_type=jnp.float32
    )
    square_sums = lax.psum(partial_squares, "col")
    scaling = row_scaling(square_sums, counts, block)

    def apply_slots(current):
        whole = lax.all_gather(current.astype(jnp.bfloat16), "row", axis=1, tiled=True)
        blocks = whole.reshape(vec_cols, -1, block)
        picked = jnp.take(blocks, local_pattern, axis=1)
        product = jnp.einsum("cbkn,bkmn->cbm", picked, masked, preferred_element_type=jnp.float32)
        total = lax.psum(product.astype(jnp.bfloat16), "col").astype(jnp.float32)
        return total.reshape(vec_cols, -1) * scaling

    current = start
    for outer in range(ITERS):
        filtered = chebyshev(current, apply_slots)
        current = orthonormal(filtered, total_rows)
    return current


def split_bf16(values):
    rounded = lax.reduce_precision(values, exponent_bits=8, mantissa_bits=7)
    return rounded.astype(jnp.bfloat16), (values - rounded).astype(jnp.bfloat16)


def replicated(start, tiles, pattern, counts):
    nb_dev, kb_dev, block = tiles.shape[0], tiles.shape[1], tiles.shape[2]
    n_row, n_col = lax.axis_size("row"), lax.axis_size("col")
    nblk = nb_dev * n_row
    total_rows = nblk * block
    share = block // n_col
    vec_cols = start.shape[0]
    cols = 2 * vec_cols
    row_index = lax.axis_index("row")
    col_index = lax.axis_index("col")
    vec_index = lax.axis_index("vec")

    own_tiles = lax.dynamic_index_in_dim(tiles, vec_index, 0, keepdims=False)
    own_pattern = lax.dynamic_slice_in_dim(
        lax.dynamic_index_in_dim(pattern, vec_index, 0, keepdims=False), col_index * kb_dev, kb_dev, 0
    )
    own_count = lax.dynamic_index_in_dim(counts, vec_index, 0, keepdims=False)
    slot_ids = col_index * kb_dev + jnp.arange(kb_dev, dtype=jnp.int32)
    live = slot_ids < own_count
    position = (own_pattern % nb_dev) * n_row + own_pattern // nb_dev
    onehot = (position[:, None] == jnp.arange(nblk, dtype=jnp.int32)) & live[:, None]
    weights = onehot.astype(jnp.bfloat16)
    live_bf16 = live.astype(jnp.bfloat16)[:, None, None]

    def chunk(index):
        part = lax.dynamic_slice_in_dim(own_tiles, index * share, share, 1)
        dense = jnp.einsum(
            "kj,kmn->mjn", weights, part, preferred_element_type=jnp.float32
        ).reshape(share, total_rows)
        masked = part * live_bf16
        squares = jnp.einsum("kmn,kmn->m", masked, masked, preferred_element_type=jnp.float32)
        return jnp.concatenate([dense, jnp.broadcast_to(squares[:, None], (share, 128))], axis=1)

    received = []
    for shift in range(1, n_col):
        sent = chunk((col_index + shift) % n_col)
        received.append(lax.ppermute(sent, "col", [(i, (i + shift) % n_col) for i in range(n_col)]))
    summed = chunk(col_index)
    for part in received:
        summed = summed + part

    entries = (own_count * block).astype(jnp.float32)
    scale = lax.rsqrt(summed[:, total_rows] / entries + EPSILON) / jnp.sqrt(entries) / HALF_WIDTH

    piece = lax.dynamic_slice_in_dim(start, col_index * block, block, 1)
    start_hi, start_lo = split_bf16(piece)
    extra = jnp.concatenate([start_hi, start_lo], axis=0)
    rows_bf16 = (summed[:, :total_rows] * scale[:, None]).astype(jnp.bfloat16)

    packed = jnp.concatenate([rows_bf16, extra], axis=1)
    copies = jnp.broadcast_to(packed[None], (n_row * n_col,) + packed.shape)
    half = lax.all_to_all(copies, ("row", "col"), 0, 0, tiled=True)
    half = half.reshape(n_row * n_col * share, total_rows + block)
    other = lax.ppermute(half, "vec", [(0, 1), (1, 0)])
    current = filter_local(half, other, n_row, n_col, vec_cols)
    return current


def per_device(start, tiles, pattern, counts):
    total_rows = tiles.shape[0] * tiles.shape[2] * lax.axis_size("row")
    n_col, n_vec = lax.axis_size("col"), lax.axis_size("vec")
    block = tiles.shape[2]
    fits = (
        total_rows * total_rows * 2 <= DENSE_BUDGET
        and n_vec == 2
        and tiles.shape[0] == n_vec
        and block % n_col == 0
        and block // n_col == 2 * start.shape[0]
        and tiles.shape[0] == n_col
    )
    if fits:
        return replicated(start, tiles, pattern, counts)
    return distributed(start, tiles, pattern, counts)


def solution(mesh):
    in_specs = (
        P("vec", ("grp", "row")),
        P(("grp", "row"), "col", None, None),
        P(("grp", "row"), None),
        P(("grp", "row")),
    )
    out_specs = P("vec", ("grp", "row"))
    return jax.shard_map(
        per_device, mesh=mesh, in_specs=in_specs, out_specs=out_specs, check_vma=False
    )
```
